32 devices in a mesh: gx: 4 (over z), gy: 8 (over y, x, core).
Axes of the slice: x: 2, y: 2, z: 4, core: 2. Of those that a mesh axis runs over, the one named last changes fastest.
Arguments:
- forcing: float32 [2, 16, 64, 1024], P(None, None, 'gx', 'gy'), may hold values from -6 to 6
- viscosity: float32 [16, 64, 1024], P(None, 'gx', 'gy'), may hold values from 0.05 to 0.5
- observed: float32 [2, 64, 1024], P(None, 'gx', 'gy'), may hold values from -6 to 6
- beta_tiles: float32 [4, 128], P('gx', 'gy'), may hold values from 1 to 30
- ice_mask: int32 [64, 1024], P('gx', 'gy'), may hold values 0 or 1
- tile_owner: int32 [64, 1024], P('gx', 'gy'), may hold values from 0 to 127
Outputs:
- velocity: float32 [2, 16, 64, 1024], P(None, None, 'gx', 'gy')
- adjoint: float32 [2, 16, 64, 1024], P(None, None, 'gx', 'gy')
- grad_tiles: float32 [4, 128], P('gx', 'gy')
The draws below stay inside these ranges and needn't reach their ends.
All inputs are finite; a program needn't handle non-finite values. No bound on the sum of `ice_mask` on one device may be relied on, other than what follows from the above.
Results may differ from the reference program's by a relative error of at most 0.000025.
Values sent between devices are 32-bit elements; how exact they have to be, the bound alone decides.
No kernel may reach another device: no remote copies, remote signals or barrier semaphores. Data moves between devices by JAX's collectives and lax.ppermute only.
A program may use at most 64 MiB of HBM per device.

```python
import math
import jax
import jax.numpy as jnp

L = 16
PASSES = 4
CX = 16
NX = 64
NY = 1024
STRIPS = 4
TILES = 128


def place_ends(drawn, stream_key, smallest, largest):
    place = [jax.random.randint(jax.random.fold_in(stream_key, axis), (), 0, length) for axis, length in enumerate(drawn.shape)]
    longest = drawn.shape.index(max(drawn.shape))
    next_to = place[:longest] + [(place[longest] + 1) % drawn.shape[longest]] + place[longest + 1:]
    return drawn.at[tuple(place)].set(smallest).at[tuple(next_to)].set(largest)


def block_levels(key, dims, cuts, low, top_value):
    loudness = 1.0
    for position, blocks in cuts:
        heights = jax.random.uniform(jax.random.fold_in(jax.random.fold_in(key, 6), position), (blocks,), jnp.float32, low / len(cuts), top_value / len(cuts))
        loudness = loudness * jnp.repeat(jnp.exp(heights), dims[position] // blocks).reshape((-1,) + (1,) * (len(dims) - 1 - position))
    return loudness


def scatter_about(rng, extent, width, reach, shards=(), dtype=jnp.bfloat16):
    values = width * jax.random.normal(rng, extent, jnp.float32)
    if shards:
        values = values * block_levels(rng, extent, shards, -0.22, 0.18)
    return jnp.clip(values, -reach, reach).astype(dtype)


def setup_inputs(seed: int = 0) -> dict:
    keys = jax.random.split(jax.random.key(seed), 7)
    return {
        "forcing": scatter_about(keys[0], (2, L, NX, NY), 1.0, 6.0, ((2, 4), (3, 8)), jnp.float32),
        "viscosity": jnp.clip(jnp.exp(math.log(0.5) - 2.3025851 * jax.random.uniform(keys[1], (L, NX, NY), jnp.float32) ** block_levels(keys[1], (L, NX, NY), ((1, 4), (2, 8)), -0.2, 0.2)), 0.05, 0.5),
        "observed": scatter_about(keys[2], (2, NX, NY), 1.0, 6.0, ((1, 4), (2, 8)), jnp.float32),
        "beta_tiles": jnp.clip(jnp.exp(math.log(30.0) - 3.4011974 * jax.random.uniform(keys[3], (STRIPS, TILES), jnp.float32) ** block_levels(keys[3], (STRIPS, TILES), ((0, 4), (1, 8)), -0.2, 0.2)), 1.0, 30.0),
        "ice_mask": place_ends((jax.random.randint(keys[4], (NX, NY), 0, 8) < 7).astype(jnp.int32), jax.random.fold_in(keys[4], 1), 0, 1),
        "tile_owner": place_ends(jax.random.randint(keys[5], (NX, NY), 0, TILES), jax.random.fold_in(keys[5], 1), 0, TILES - 1).astype(jnp.int32),
    }


OMEGA = 0.8
VERTICAL = 16.0


def lateral_terms(visc_pad):
    centre_visc = visc_pad[:, 1:-1, 1:-1]
    west_face = 0.5 * (centre_visc + visc_pad[:, :-2, 1:-1])
    east_face = 0.5 * (centre_visc + visc_pad[:, 2:, 1:-1])
    south_face = 0.5 * (centre_visc + visc_pad[:, 1:-1, :-2])
    north_face = 0.5 * (centre_visc + visc_pad[:, 1:-1, 2:])
    return west_face, east_face, south_face, north_face


def weights_xy():
    along_x = jnp.array([4.0, 1.0], jnp.float32).reshape(2, 1, 1, 1)
    along_y = jnp.array([1.0, 4.0], jnp.float32).reshape(2, 1, 1, 1)
    return along_x, along_y


def prepare(visc_pad, beta_col, ice_cover):
    faces = lateral_terms(visc_pad)
    west_face, east_face, south_face, north_face = faces
    along_x, along_y = weights_xy()
    centre_visc = visc_pad[:, 1:-1, 1:-1]
    vertical = VERTICAL * 0.5 * (centre_visc[:-1] + centre_visc[1:])
    zero_row = jnp.zeros_like(centre_visc[:1])
    upper_link = jnp.concatenate([vertical, zero_row], 0)
    lower_link = jnp.concatenate([zero_row, vertical], 0)
    basal = jnp.concatenate([jnp.zeros_like(centre_visc[:-1]), beta_col[None]], 0)
    diagonal = along_x * (west_face + east_face) + along_y * (south_face + north_face)
    diagonal = diagonal + upper_link + lower_link + basal + (1.0 - ice_cover)
    layer_count = visc_pad.shape[0]
    ratio_list = []
    inverse_list = []
    for layer_idx in range(layer_count):
        pivot = diagonal[:, layer_idx]
        if layer_idx > 0:
            pivot = pivot + lower_link[layer_idx] * ratio_list[-1]
        inverse = 1.0 / pivot
        inverse_list.append(inverse)
        ratio_list.append(-upper_link[layer_idx] * inverse)
    return faces, lower_link, jnp.stack(ratio_list, 1), jnp.stack(inverse_list, 1)


def relax(vel_pad, rhs_field, faces, lower_link, ratios, inverses, ice_cover):
    west_face, east_face, south_face, north_face = faces
    along_x, along_y = weights_xy()
    lateral = along_x * (west_face * vel_pad[:, :, :-2, 1:-1] + east_face * vel_pad[:, :, 2:, 1:-1])
    lateral = lateral + along_y * (south_face * vel_pad[:, :, 1:-1, :-2] + north_face * vel_pad[:, :, 1:-1, 2:])
    right_side = rhs_field + lateral
    layer_count = right_side.shape[1]
    forward_list = []
    for layer_idx in range(layer_count):
        value = right_side[:, layer_idx]
        if layer_idx > 0:
            value = value + lower_link[layer_idx] * forward_list[-1]
        forward_list.append(value * inverses[:, layer_idx])
    solved = [None] * layer_count
    solved[layer_count - 1] = forward_list[layer_count - 1]
    for layer_idx in range(layer_count - 2, -1, -1):
        solved[layer_idx] = forward_list[layer_idx] - ratios[:, layer_idx] * solved[layer_idx + 1]
    line_value = jnp.stack(solved, 1)
    centre = vel_pad[:, :, 1:-1, 1:-1]
    return ice_cover * ((1.0 - OMEGA) * centre + OMEGA * line_value)


def pad_cells(field):
    return jnp.pad(field, [(0, 0)] * (field.ndim - 2) + [(1, 1), (1, 1)])


def reference(forcing, viscosity, observed, beta_tiles, ice_mask, tile_owner):
    ice_cover = ice_mask.astype(jnp.float32)
    strip_idx = (jnp.arange(NX) // CX).astype(jnp.int32)
    beta_col = beta_tiles[strip_idx[:, None], tile_owner]
    faces, lower_link, ratios, inverses = prepare(pad_cells(viscosity), beta_col, ice_cover)
    velocity = jnp.zeros_like(forcing)
    for sweep_idx in range(PASSES):
        velocity = relax(pad_cells(velocity), forcing, faces, lower_link, ratios, inverses, ice_cover)
    misfit = velocity[:, 0] - observed
    adjoint_rhs = jnp.zeros_like(forcing).at[:, 0].set(misfit)
    adjoint = jnp.zeros_like(forcing)
    for sweep_idx in range(PASSES):
        adjoint = relax(pad_cells(adjoint), adjoint_rhs, faces, lower_link, ratios, inverses, ice_cover)
    grad_col = -ice_cover * beta_col * jnp.sum(adjoint[:, -1] * velocity[:, -1], axis=0)
    segment_ids = (strip_idx[:, None] * TILES + tile_owner).astype(jnp.int32)
    grad_tiles = jax.ops.segment_sum(grad_col.reshape(-1), segment_ids.reshape(-1), num_segments=STRIPS * TILES)
    return velocity, adjoint, grad_tiles.reshape(STRIPS, TILES)
```

```python
import jax
import jax.numpy as jnp
from jax import lax
from jax.sharding import PartitionSpec as P

PASSES = 4


OMEGA = 0.8
VERTICAL = 16.0
HALO = 2 * PASSES - 1


def with_halo(cells, sides, width):
    for axis, dim in sides:
        count = lax.axis_size(axis)
        ends = count - 1
        head = lax.slice_in_dim(cells, 0, width, axis=dim)
        tail = lax.slice_in_dim(cells, cells.shape[dim] - width, cells.shape[dim], axis=dim)
        cells = jnp.concatenate(
            [
                lax.ppermute(tail, axis, [(i, (i + 1) % count) for i in range(ends)]),
                cells,
                lax.ppermute(head, axis, [((i + 1) % count, i) for i in range(ends)]),
            ],
            axis=dim,
        )
    return cells


def lateral_terms(visc_pad):
    centre_visc = visc_pad[:, 1:-1, 1:-1]
    west_face = 0.5 * (centre_visc + visc_pad[:, :-2, 1:-1])
    east_face = 0.5 * (centre_visc + visc_pad[:, 2:, 1:-1])
    south_face = 0.5 * (centre_visc + visc_pad[:, 1:-1, :-2])
    north_face = 0.5 * (centre_visc + visc_pad[:, 1:-1, 2:])
    return (west_face, east_face, south_face, north_face)


def weights_xy():
    along_x = jnp.array([4.0, 1.0], jnp.float32).reshape(2, 1, 1, 1)
    along_y = jnp.array([1.0, 4.0], jnp.float32).reshape(2, 1, 1, 1)
    return (along_x, along_y)


def prepare(visc_pad, beta_col, ice_cover):
    faces = lateral_terms(visc_pad)
    west_face, east_face, south_face, north_face = faces
    along_x, along_y = weights_xy()
    centre_visc = visc_pad[:, 1:-1, 1:-1]
    vertical = VERTICAL * 0.5 * (centre_visc[:-1] + centre_visc[1:])
    zero_row = jnp.zeros_like(centre_visc[:1])
    upper_link = jnp.concatenate([vertical, zero_row], 0)
    lower_link = jnp.concatenate([zero_row, vertical], 0)
    basal = jnp.concatenate([jnp.zeros_like(centre_visc[:-1]), beta_col[None]], 0)
    diagonal = along_x * (west_face + east_face) + along_y * (south_face + north_face)
    diagonal = diagonal + upper_link + lower_link + basal + (1.0 - ice_cover)
    layer_count = visc_pad.shape[0]
    ratio_list = []
    inverse_list = []
    for layer_idx in range(layer_count):
        pivot = diagonal[:, layer_idx]
        if layer_idx > 0:
            pivot = pivot + lower_link[layer_idx] * ratio_list[-1]
        inverse = 1.0 / pivot
        inverse_list.append(inverse)
        ratio_list.append(-upper_link[layer_idx] * inverse)
    return (faces, lower_link, jnp.stack(ratio_list, 1), jnp.stack(inverse_list, 1))


def relax(vel_pad, rhs_field, faces, lower_link, ratios, inverses, ice_cover):
    west_face, east_face, south_face, north_face = faces
    along_x, along_y = weights_xy()
    lateral = along_x * (west_face * vel_pad[:, :, :-2, 1:-1] + east_face * vel_pad[:, :, 2:, 1:-1])
    lateral = lateral + along_y * (
        south_face * vel_pad[:, :, 1:-1, :-2] + north_face * vel_pad[:, :, 1:-1, 2:]
    )
    right_side = rhs_field + lateral
    layer_count = right_side.shape[1]
    forward_list = []
    for layer_idx in range(layer_count):
        value = right_side[:, layer_idx]
        if layer_idx > 0:
            value = value + lower_link[layer_idx] * forward_list[-1]
        forward_list.append(value * inverses[:, layer_idx])
    solved = [None] * layer_count
    solved[layer_count - 1] = forward_list[layer_count - 1]
    for layer_idx in range(layer_count - 2, -1, -1):
        solved[layer_idx] = forward_list[layer_idx] - ratios[:, layer_idx] * solved[layer_idx + 1]
    line_value = jnp.stack(solved, 1)
    centre = vel_pad[:, :, 1:-1, 1:-1]
    return ice_cover * ((1.0 - OMEGA) * centre + OMEGA * line_value)


def pad_cells(field):
    return jnp.pad(field, [(0, 0)] * (field.ndim - 2) + [(1, 1), (1, 1)])


def local(forcing, viscosity, observed, beta_tiles, ice_mask, tile_owner):
    comps, layers, rows, cols = forcing.shape
    strip_count = lax.axis_size("gx")
    strips_near = jnp.concatenate(
        [
            lax.ppermute(beta_tiles, "gx", [(i, i + 1) for i in range(strip_count - 1)]),
            beta_tiles,
            lax.ppermute(beta_tiles, "gx", [(i + 1, i) for i in range(strip_count - 1)]),
        ],
        axis=0,
    )
    friction_rows = lax.all_gather(strips_near, "gy", axis=1, tiled=True)
    tile_count = friction_rows.shape[1]

    packed = jnp.concatenate(
        [
            forcing.reshape(comps * layers, rows, cols),
            viscosity,
            observed,
            ice_mask.astype(jnp.float32)[None],
            tile_owner.astype(jnp.float32)[None],
        ],
        axis=0,
    )
    packed = with_halo(packed, (("gx", 1), ("gy", 2)), HALO)
    ext_rows, ext_cols = packed.shape[1], packed.shape[2]
    at = 0
    forcing_ext = packed[at:at + comps * layers].reshape(comps, layers, ext_rows, ext_cols)
    at += comps * layers
    visc_ext = packed[at:at + layers]
    at += layers
    observed_ext = packed[at:at + comps]
    at += comps
    ice_cover = packed[at]
    owner_ext = packed[at + 1].astype(jnp.int32)

    tiles = lax.broadcasted_iota(jnp.int32, (1, 1, tile_count), 2)
    owner_match = owner_ext[:, :, None] == tiles
    row_strip = jnp.concatenate(
        [
            jnp.broadcast_to(friction_rows[0], (HALO, tile_count)),
            jnp.broadcast_to(friction_rows[1], (rows, tile_count)),
            jnp.broadcast_to(friction_rows[2], (HALO, tile_count)),
        ],
        axis=0,
    )
    beta_col = jnp.sum(jnp.where(owner_match, row_strip[:, None, :], 0.0), axis=-1)

    faces, lower_link, ratios, inverses = prepare(pad_cells(visc_ext), beta_col, ice_cover)

    def advance(field, rhs_field):
        return relax(pad_cells(field), rhs_field, faces, lower_link, ratios, inverses, ice_cover)

    velocity = jnp.zeros_like(forcing_ext)
    for sweep_idx in range(PASSES):
        velocity = advance(velocity, forcing_ext)
    misfit = velocity[:, 0] - observed_ext
    adjoint_rhs = jnp.zeros_like(forcing_ext).at[:, 0].set(misfit)
    adjoint = jnp.zeros_like(forcing_ext)
    for sweep_idx in range(PASSES):
        adjoint = advance(adjoint, adjoint_rhs)

    inner = (slice(HALO, HALO + rows), slice(HALO, HALO + cols))
    velocity = velocity[:, :, inner[0], inner[1]]
    adjoint = adjoint[:, :, inner[0], inner[1]]
    grad_col = -ice_cover[inner] * beta_col[inner] * jnp.sum(adjoint[:, -1] * velocity[:, -1], axis=0)
    block_match = owner_match[inner[0], inner[1]]
    partial_sum = jnp.sum(jnp.where(block_match, grad_col[:, :, None], 0.0), axis=(0, 1))[None]
    grad_tiles = lax.psum_scatter(partial_sum, "gy", scatter_dimension=1, tiled=True)
    return (velocity, adjoint, grad_tiles)


def solution(mesh):
    in_specs = (
        P(None, None, "gx", "gy"),
        P(None, "gx", "gy"),
        P(None, "gx", "gy"),
        P("gx", "gy"),
        P("gx", "gy"),
        P("gx", "gy"),
    )
    out_specs = (P(None, None, "gx", "gy"), P(None, None, "gx", "gy"), P("gx", "gy"))
    return jax.shard_map(local, mesh=mesh, in_specs=in_specs, out_specs=out_specs, check_vma=False)
```

```python
import jax
import jax.numpy as jnp
from jax import lax
from jax.sharding import PartitionSpec as P

PASSES = 4


OMEGA = 0.8
VERTICAL = 16.0
HALO = 2 * PASSES - 1


def with_halo(cells, sides, width):
    for axis, dim in sides:
        count = lax.axis_size(axis)
        ends = count - 1
        head = lax.slice_in_dim(cells, 0, width, axis=dim)
        tail = lax.slice_in_dim(cells, cells.shape[dim] - width, cells.shape[dim], axis=dim)
        cells = jnp.concatenate(
            [
                lax.ppermute(tail, axis, [(i, (i + 1) % count) for i in range(ends)]),
                cells,
                lax.ppermute(head, axis, [((i + 1) % count, i) for i in range(ends)]),
            ],
            axis=dim,
        )
    return cells


def lateral_terms(visc_pad):
    centre_visc = visc_pad[:, 1:-1, 1:-1]
    west_face = 0.5 * (centre_visc + visc_pad[:, :-2, 1:-1])
    east_face = 0.5 * (centre_visc + visc_pad[:, 2:, 1:-1])
    south_face = 0.5 * (centre_visc + visc_pad[:, 1:-1, :-2])
    north_face = 0.5 * (centre_visc + visc_pad[:, 1:-1, 2:])
    return (west_face, east_face, south_face, north_face)


def weights_xy():
    along_x = jnp.array([4.0, 1.0], jnp.float32).reshape(2, 1, 1, 1)
    along_y = jnp.array([1.0, 4.0], jnp.float32).reshape(2, 1, 1, 1)
    return (along_x, along_y)


def prepare(visc_pad, beta_col, ice_cover):
    faces = lateral_terms(visc_pad)
    west_face, east_face, south_face, north_face = faces
    along_x, along_y = weights_xy()
    centre_visc = visc_pad[:, 1:-1, 1:-1]
    vertical = VERTICAL * 0.5 * (centre_visc[:-1] + centre_visc[1:])
    zero_row = jnp.zeros_like(centre_visc[:1])
    upper_link = jnp.concatenate([vertical, zero_row], 0)
    lower_link = jnp.concatenate([zero_row, vertical], 0)
    basal = jnp.concatenate([jnp.zeros_like(centre_visc[:-1]), beta_col[None]], 0)
    diagonal = along_x * (west_face + east_face) + along_y * (south_face + north_face)
    diagonal = diagonal + upper_link + lower_link + basal + (1.0 - ice_cover)
    layer_count = visc_pad.shape[0]
    ratio_list = []
    inverse_list = []
    for layer_idx in range(layer_count):
        pivot = diagonal[:, layer_idx]
        if layer_idx > 0:
            pivot = pivot + lower_link[layer_idx] * ratio_list[-1]
        inverse = 1.0 / pivot
        inverse_list.append(inverse)
        ratio_list.append(-upper_link[layer_idx] * inverse)
    return (faces, lower_link, jnp.stack(ratio_list, 1), jnp.stack(inverse_list, 1))


def relax(vel_pad, rhs_field, faces, lower_link, ratios, inverses, ice_cover):
    west_face, east_face, south_face, north_face = faces
    along_x, along_y = weights_xy()
    lateral = along_x * (west_face * vel_pad[:, :, :-2, 1:-1] + east_face * vel_pad[:, :, 2:, 1:-1])
    lateral = lateral + along_y * (
        south_face * vel_pad[:, :, 1:-1, :-2] + north_face * vel_pad[:, :, 1:-1, 2:]
    )
    right_side = rhs_field + lateral
    layer_count = right_side.shape[1]
    forward_list = []
    for layer_idx in range(layer_count):
        value = right_side[:, layer_idx]
        if layer_idx > 0:
            value = value + lower_link[layer_idx] * forward_list[-1]
        forward_list.append(value * inverses[:, layer_idx])
    solved = [None] * layer_count
    solved[layer_count - 1] = forward_list[layer_count - 1]
    for layer_idx in range(layer_count - 2, -1, -1):
        solved[layer_idx] = forward_list[layer_idx] - ratios[:, layer_idx] * solved[layer_idx + 1]
    line_value = jnp.stack(solved, 1)
    centre = vel_pad[:, :, 1:-1, 1:-1]
    return ice_cover * ((1.0 - OMEGA) * centre + OMEGA * line_value)


def pad_cells(field):
    return jnp.pad(field, [(0, 0)] * (field.ndim - 2) + [(1, 1), (1, 1)])


def local(forcing, viscosity, observed, beta_tiles, ice_mask, tile_owner):
    comps, layers, rows, cols = forcing.shape
    strip_count = lax.axis_size("gx")
    strips_near = jnp.concatenate(
        [
            lax.ppermute(beta_tiles, "gx", [(i, i + 1) for i in range(strip_count - 1)]),
            beta_tiles,
            lax.ppermute(beta_tiles, "gx", [(i + 1, i) for i in range(strip_count - 1)]),
        ],
        axis=0,
    )
    friction_rows = lax.all_gather(strips_near, "gy", axis=1, tiled=True)
    tile_count = friction_rows.shape[1]

    packed = jnp.concatenate(
        [
            forcing.reshape(comps * layers, rows, cols),
            viscosity,
            observed,
            ice_mask.astype(jnp.float32)[None],
            tile_owner.astype(jnp.float32)[None],
        ],
        axis=0,
    )
    packed = with_halo(packed, (("gx", 1), ("gy", 2)), HALO)
    ext_rows, ext_cols = packed.shape[1], packed.shape[2]
    at = 0
    forcing_ext = packed[at:at + comps * layers].reshape(comps, layers, ext_rows, ext_cols)
    at += comps * layers
    visc_ext = packed[at:at + layers]
    at += layers
    observed_ext = packed[at:at + comps]
    at += comps
    ice_cover = packed[at]
    owner_ext = packed[at + 1].astype(jnp.int32)

    tiles = lax.broadcasted_iota(jnp.int32, (1, 1, tile_count), 2)
    owner_match = owner_ext[:, :, None] == tiles
    row_strip = jnp.concatenate(
        [
            jnp.broadcast_to(friction_rows[0], (HALO, tile_count)),
            jnp.broadcast_to(friction_rows[1], (rows, tile_count)),
            jnp.broadcast_to(friction_rows[2], (HALO, tile_count)),
        ],
        axis=0,
    )
    beta_col = jnp.sum(jnp.where(owner_match, row_strip[:, None, :], 0.0), axis=-1)

    faces, lower_link, ratios, inverses = prepare(pad_cells(visc_ext), beta_col, ice_cover)

    def advance(field, rhs_field):
        return relax(pad_cells(field), rhs_field, faces, lower_link, ratios, inverses, ice_cover)

    velocity = jnp.zeros_like(forcing_ext)
    for sweep_idx in range(PASSES):
        velocity = advance(velocity, forcing_ext)
    misfit = velocity[:, 0] - observed_ext
    adjoint_rhs = jnp.zeros_like(forcing_ext).at[:, 0].set(misfit)
    adjoint = jnp.zeros_like(forcing_ext)
    for sweep_idx in range(PASSES):
        adjoint = advance(adjoint, adjoint_rhs)

    inner = (slice(HALO, HALO + rows), slice(HALO, HALO + cols))
    velocity = velocity[:, :, inner[0], inner[1]]
    adjoint = adjoint[:, :, inner[0], inner[1]]
    grad_col = -ice_cover[inner] * beta_col[inner] * jnp.sum(adjoint[:, -1] * velocity[:, -1], axis=0)
    block_match = owner_match[inner[0], inner[1]]
    partial_sum = jnp.sum(jnp.where(block_match, grad_col[:, :, None], 0.0), axis=(0, 1))
    owners = lax.axis_size("gy")
    chunk = tile_count // owners
    gathered = lax.all_gather(partial_sum.reshape(owners, chunk), "gy")
    mine = lax.dynamic_index_in_dim(gathered, lax.axis_index("gy"), axis=1, keepdims=False)
    grad_tiles = jnp.sum(mine, axis=0)[None]
    return (velocity, adjoint, grad_tiles)


def solution(mesh):
    in_specs = (
        P(None, None, "gx", "gy"),
        P(None, "gx", "gy"),
        P(None, "gx", "gy"),
        P("gx", "gy"),
        P("gx", "gy"),
        P("gx", "gy"),
    )
    out_specs = (P(None, None, "gx", "gy"), P(None, None, "gx", "gy"), P("gx", "gy"))
    return jax.shard_map(local, mesh=mesh, in_specs=in_specs, out_specs=out_specs, check_vma=False)
```

```python
import jax
import jax.numpy as jnp
from jax import lax
from jax.sharding import PartitionSpec as P

PASSES = 4


OMEGA = 0.8
VERTICAL = 16.0
HALO = 2 * PASSES - 1


def with_halo(cells, sides, width):
    for axis, dim in sides:
        count = lax.axis_size(axis)
        ends = count - 1
        head = lax.slice_in_dim(cells, 0, width, axis=dim)
        tail = lax.slice_in_dim(cells, cells.shape[dim] - width, cells.shape[dim], axis=dim)
        cells = jnp.concatenate(
            [
                lax.ppermute(tail, axis, [(i, (i + 1) % count) for i in range(ends)]),
                cells,
                lax.ppermute(head, axis, [((i + 1) % count, i) for i in range(ends)]),
            ],
            axis=dim,
        )
    return cells


def lateral_terms(visc_pad):
    centre_visc = visc_pad[:, 1:-1, 1:-1]
    west_face = 0.5 * (centre_visc + visc_pad[:, :-2, 1:-1])
    east_face = 0.5 * (centre_visc + visc_pad[:, 2:, 1:-1])
    south_face = 0.5 * (centre_visc + visc_pad[:, 1:-1, :-2])
    north_face = 0.5 * (centre_visc + visc_pad[:, 1:-1, 2:])
    return (west_face, east_face, south_face, north_face)


def weights_xy():
    along_x = jnp.array([4.0, 1.0], jnp.float32).reshape(2, 1, 1, 1)
    along_y = jnp.array([1.0, 4.0], jnp.float32).reshape(2, 1, 1, 1)
    return (along_x, along_y)


def prepare(visc_pad, beta_col, ice_cover):
    faces = lateral_terms(visc_pad)
    west_face, east_face, south_face, north_face = faces
    along_x, along_y = weights_xy()
    centre_visc = visc_pad[:, 1:-1, 1:-1]
    vertical = VERTICAL * 0.5 * (centre_visc[:-1] + centre_visc[1:])
    zero_row = jnp.zeros_like(centre_visc[:1])
    upper_link = jnp.concatenate([vertical, zero_row], 0)
    lower_link = jnp.concatenate([zero_row, vertical], 0)
    basal = jnp.concatenate([jnp.zeros_like(centre_visc[:-1]), beta_col[None]], 0)
    diagonal = along_x * (west_face + east_face) + along_y * (south_face + north_face)
    diagonal = diagonal + upper_link + lower_link + basal + (1.0 - ice_cover)
    layer_count = visc_pad.shape[0]
    ratio_list = []
    inverse_list = []
    for layer_idx in range(layer_count):
        pivot = diagonal[:, layer_idx]
        if layer_idx > 0:
            pivot = pivot + lower_link[layer_idx] * ratio_list[-1]
        inverse = 1.0 / pivot
        inverse_list.append(inverse)
        ratio_list.append(-upper_link[layer_idx] * inverse)
    return (faces, lower_link, jnp.stack(ratio_list, 1), jnp.stack(inverse_list, 1))


def relax(vel_pad, rhs_field, faces, lower_link, ratios, inverses, ice_cover):
    west_face, east_face, south_face, north_face = faces
    along_x, along_y = weights_xy()
    lateral = along_x * (west_face * vel_pad[:, :, :-2, 1:-1] + east_face * vel_pad[:, :, 2:, 1:-1])
    lateral = lateral + along_y * (
        south_face * vel_pad[:, :, 1:-1, :-2] + north_face * vel_pad[:, :, 1:-1, 2:]
    )
    right_side = rhs_field + lateral
    layer_count = right_side.shape[1]
    forward_list = []
    for layer_idx in range(layer_count):
        value = right_side[:, layer_idx]
        if layer_idx > 0:
            value = value + lower_link[layer_idx] * forward_list[-1]
        forward_list.append(value * inverses[:, layer_idx])
    solved = [None] * layer_count
    solved[layer_count - 1] = forward_list[layer_count - 1]
    for layer_idx in range(layer_count - 2, -1, -1):
        solved[layer_idx] = forward_list[layer_idx] - ratios[:, layer_idx] * solved[layer_idx + 1]
    line_value = jnp.stack(solved, 1)
    centre = vel_pad[:, :, 1:-1, 1:-1]
    return ice_cover * ((1.0 - OMEGA) * centre + OMEGA * line_value)


def pad_cells(field):
    return jnp.pad(field, [(0, 0)] * (field.ndim - 2) + [(1, 1), (1, 1)])


def shifted(piece, axis, down):
    count = lax.axis_size(axis)
    if down:
        pairs = [(i, i + 1) for i in range(count - 1)]
    else:
        pairs = [(i + 1, i) for i in range(count - 1)]
    return lax.ppermute(piece, axis, pairs)


def local(forcing, viscosity, observed, beta_tiles, ice_mask, tile_owner):
    comps, layers, rows, cols = forcing.shape
    tiles_here = beta_tiles.shape[1]
    planes = [
        forcing.reshape(comps * layers, rows, cols),
        viscosity,
        observed,
        ice_mask.astype(jnp.float32)[None],
        tile_owner.astype(jnp.float32)[None],
    ]
    plane_count = sum(p.shape[0] for p in planes)

    beta_plane = jnp.pad(beta_tiles, ((0, HALO - 1), (0, cols - tiles_here)))[None]
    head = jnp.concatenate([p[:, :HALO] for p in planes] + [beta_plane], axis=0)
    tail = jnp.concatenate([p[:, rows - HALO:] for p in planes] + [beta_plane], axis=0)
    from_above = shifted(tail, "gx", True)
    from_below = shifted(head, "gx", False)

    def stack_rows(lo, hi):
        return jnp.concatenate(
            [from_above[:plane_count, :, lo:hi]]
            + [jnp.concatenate([p[:, :, lo:hi] for p in planes], axis=0)]
            + [from_below[:plane_count, :, lo:hi]],
            axis=1,
        )

    from_left = shifted(stack_rows(cols - HALO, cols), "gy", True)
    from_right = shifted(stack_rows(0, HALO), "gy", False)

    strips_near = jnp.stack(
        [from_above[plane_count, 0, :tiles_here], beta_tiles[0], from_below[plane_count, 0, :tiles_here]]
    )
    friction_rows = lax.all_gather(strips_near, "gy", axis=1, tiled=True)
    tile_count = friction_rows.shape[1]

    packed = jnp.concatenate([from_left, stack_rows(0, cols), from_right], axis=2)
    ext_rows, ext_cols = packed.shape[1], packed.shape[2]
    at = 0
    forcing_ext = packed[at:at + comps * layers].reshape(comps, layers, ext_rows, ext_cols)
    at += comps * layers
    visc_ext = packed[at:at + layers]
    at += layers
    observed_ext = packed[at:at + comps]
    at += comps
    ice_cover = packed[at]
    owner_ext = packed[at + 1].astype(jnp.int32)

    tiles = lax.broadcasted_iota(jnp.int32, (1, 1, tile_count), 2)
    owner_match = owner_ext[:, :, None] == tiles
    row_strip = jnp.concatenate(
        [
            jnp.broadcast_to(friction_rows[0], (HALO, tile_count)),
            jnp.broadcast_to(friction_rows[1], (rows, tile_count)),
            jnp.broadcast_to(friction_rows[2], (HALO, tile_count)),
        ],
        axis=0,
    )
    beta_col = jnp.sum(jnp.where(owner_match, row_strip[:, None, :], 0.0), axis=-1)

    faces, lower_link, ratios, inverses = prepare(pad_cells(visc_ext), beta_col, ice_cover)

    def advance(field, rhs_field):
        return relax(pad_cells(field), rhs_field, faces, lower_link, ratios, inverses, ice_cover)

    velocity = jnp.zeros_like(forcing_ext)
    for sweep_idx in range(PASSES):
        velocity = advance(velocity, forcing_ext)
    misfit = velocity[:, 0] - observed_ext
    adjoint_rhs = jnp.zeros_like(forcing_ext).at[:, 0].set(misfit)
    adjoint = jnp.zeros_like(forcing_ext)
    for sweep_idx in range(PASSES):
        adjoint = advance(adjoint, adjoint_rhs)

    inner = (slice(HALO, HALO + rows), slice(HALO, HALO + cols))
    velocity = velocity[:, :, inner[0], inner[1]]
    adjoint = adjoint[:, :, inner[0], inner[1]]
    grad_col = -ice_cover[inner] * beta_col[inner] * jnp.sum(adjoint[:, -1] * velocity[:, -1], axis=0)
    block_match = owner_match[inner[0], inner[1]]
    partial_sum = jnp.sum(jnp.where(block_match, grad_col[:, :, None], 0.0), axis=(0, 1))
    owners = lax.axis_size("gy")
    chunk = tile_count // owners
    gathered = lax.all_gather(partial_sum.reshape(owners, chunk), "gy")
    mine = lax.dynamic_index_in_dim(gathered, lax.axis_index("gy"), axis=1, keepdims=False)
    grad_tiles = jnp.sum(mine, axis=0)[None]
    return (velocity, adjoint, grad_tiles)


def solution(mesh):
    in_specs = (
        P(None, None, "gx", "gy"),
        P(None, "gx", "gy"),
        P(None, "gx", "gy"),
        P("gx", "gy"),
        P("gx", "gy"),
        P("gx", "gy"),
    )
    out_specs = (P(None, None, "gx", "gy"), P(None, None, "gx", "gy"), P("gx", "gy"))
    return jax.shard_map(local, mesh=mesh, in_specs=in_specs, out_specs=out_specs, check_vma=False)
```

```python
import jax
import jax.numpy as jnp
from jax import lax
from jax.experimental import pallas as pl
from jax.experimental.pallas import tpu as pltpu
from jax.sharding import PartitionSpec as P

PASSES = 4


OMEGA = 0.8
VERTICAL = 16.0
HALO = 2 * PASSES - 1


def with_halo(cells, sides, width):
    for axis, dim in sides:
        count = lax.axis_size(axis)
        ends = count - 1
        head = lax.slice_in_dim(cells, 0, width, axis=dim)
        tail = lax.slice_in_dim(cells, cells.shape[dim] - width, cells.shape[dim], axis=dim)
        cells = jnp.concatenate(
            [
                lax.ppermute(tail, axis, [(i, (i + 1) % count) for i in range(ends)]),
                cells,
                lax.ppermute(head, axis, [((i + 1) % count, i) for i in range(ends)]),
            ],
            axis=dim,
        )
    return cells


def lateral_terms(visc_pad):
    centre_visc = visc_pad[:, 1:-1, 1:-1]
    west_face = 0.5 * (centre_visc + visc_pad[:, :-2, 1:-1])
    east_face = 0.5 * (centre_visc + visc_pad[:, 2:, 1:-1])
    south_face = 0.5 * (centre_visc + visc_pad[:, 1:-1, :-2])
    north_face = 0.5 * (centre_visc + visc_pad[:, 1:-1, 2:])
    return (west_face, east_face, south_face, north_face)


def weights_xy():
    along_x = jnp.array([4.0, 1.0], jnp.float32).reshape(2, 1, 1, 1)
    along_y = jnp.array([1.0, 4.0], jnp.float32).reshape(2, 1, 1, 1)
    return (along_x, along_y)


def prepare(visc_pad, beta_col, ice_cover):
    faces = lateral_terms(visc_pad)
    west_face, east_face, south_face, north_face = faces
    along_x, along_y = weights_xy()
    centre_visc = visc_pad[:, 1:-1, 1:-1]
    vertical = VERTICAL * 0.5 * (centre_visc[:-1] + centre_visc[1:])
    zero_row = jnp.zeros_like(centre_visc[:1])
    upper_link = jnp.concatenate([vertical, zero_row], 0)
    lower_link = jnp.concatenate([zero_row, vertical], 0)
    basal = jnp.concatenate([jnp.zeros_like(centre_visc[:-1]), beta_col[None]], 0)
    diagonal = along_x * (west_face + east_face) + along_y * (south_face + north_face)
    diagonal = diagonal + upper_link + lower_link + basal + (1.0 - ice_cover)
    layer_count = visc_pad.shape[0]
    ratio_list = []
    inverse_list = []
    for layer_idx in range(layer_count):
        pivot = diagonal[:, layer_idx]
        if layer_idx > 0:
            pivot = pivot + lower_link[layer_idx] * ratio_list[-1]
        inverse = 1.0 / pivot
        inverse_list.append(inverse)
        ratio_list.append(-upper_link[layer_idx] * inverse)
    return (faces, lower_link, jnp.stack(ratio_list, 1), jnp.stack(inverse_list, 1))


def relax(vel_pad, rhs_field, faces, lower_link, ratios, inverses, ice_cover):
    west_face, east_face, south_face, north_face = faces
    along_x, along_y = weights_xy()
    lateral = along_x * (west_face * vel_pad[:, :, :-2, 1:-1] + east_face * vel_pad[:, :, 2:, 1:-1])
    lateral = lateral + along_y * (
        south_face * vel_pad[:, :, 1:-1, :-2] + north_face * vel_pad[:, :, 1:-1, 2:]
    )
    right_side = rhs_field + lateral
    layer_count = right_side.shape[1]
    forward_list = []
    for layer_idx in range(layer_count):
        value = right_side[:, layer_idx]
        if layer_idx > 0:
            value = value + lower_link[layer_idx] * forward_list[-1]
        forward_list.append(value * inverses[:, layer_idx])
    solved = [None] * layer_count
    solved[layer_count - 1] = forward_list[layer_count - 1]
    for layer_idx in range(layer_count - 2, -1, -1):
        solved[layer_idx] = forward_list[layer_idx] - ratios[:, layer_idx] * solved[layer_idx + 1]
    line_value = jnp.stack(solved, 1)
    centre = vel_pad[:, :, 1:-1, 1:-1]
    return ice_cover * ((1.0 - OMEGA) * centre + OMEGA * line_value)


def pad_cells(field):
    return jnp.pad(field, [(0, 0)] * (field.ndim - 2) + [(1, 1), (1, 1)])


WEIGHTS = ((4.0, 1.0), (1.0, 4.0))


def passes_kernel(forcing_ref, visc_ref, obs_ref, ice_ref, beta_ref, vel_ref, adj_ref,
                  face_ref, link_ref, ratio_ref, inv_ref, iter_ref, fwd_ref, misfit_ref):
    comps, layers, tall, wide = forcing_ref.shape
    rows, cols = vel_ref.shape[2], vel_ref.shape[3]
    ice = ice_ref[...]

    def along_rows(x, step):
        return pltpu.roll(x, step % tall, 0)

    def along_cols(x, step):
        return pltpu.roll(x, step % wide, 1)

    for k in range(layers):
        visc = visc_ref[k]
        face_ref[0, k] = 0.5 * (visc + along_rows(visc, 1))
        face_ref[1, k] = 0.5 * (visc + along_rows(visc, -1))
        face_ref[2, k] = 0.5 * (visc + along_cols(visc, 1))
        face_ref[3, k] = 0.5 * (visc + along_cols(visc, -1))
        if k == 0:
            link_ref[0] = jnp.zeros_like(visc)
        else:
            link_ref[k] = (VERTICAL * 0.5) * (visc_ref[k - 1] + visc)

    open_water = 1.0 - ice
    for c in range(comps):
        wx, wy = WEIGHTS[c]
        ratio_prev = None
        for k in range(layers):
            diag = wx * (face_ref[0, k] + face_ref[1, k]) + wy * (face_ref[2, k] + face_ref[3, k])
            lower = link_ref[k]
            upper = link_ref[k + 1] if k < layers - 1 else None
            if upper is not None:
                diag = diag + upper
            diag = diag + lower
            if k == layers - 1:
                diag = diag + beta_ref[...]
            diag = diag + open_water
            pivot = diag if k == 0 else diag + lower * ratio_prev
            inverse = 1.0 / pivot
            inv_ref[c, k] = inverse
            ratio_prev = -upper * inverse if upper is not None else jnp.zeros_like(inverse)
            ratio_ref[c, k] = ratio_prev

    def run_pass(src, dst, forced, first):
        for c in range(comps):
            wx, wy = WEIGHTS[c]

            def right_side(k, base):
                if first:
                    return base
                u = iter_ref[src, c, k]
                lateral = wx * (face_ref[0, k] * along_rows(u, 1) + face_ref[1, k] * along_rows(u, -1))
                lateral = lateral + wy * (face_ref[2, k] * along_cols(u, 1) + face_ref[3, k] * along_cols(u, -1))
                return lateral if base is None else base + lateral

            if forced:
                base0 = forcing_ref[c, 0]
            else:
                base0 = misfit_ref[c]
            f0 = right_side(0, base0) * inv_ref[c, 0]
            fwd_ref[0] = f0

            def down(k, f_prev):
                base = forcing_ref[c, k] if forced else None
                value = right_side(k, base)
                if value is None:
                    value = jnp.zeros_like(f_prev)
                value = value + link_ref[k] * f_prev
                f = value * inv_ref[c, k]
                fwd_ref[k] = f
                return f

            lax.fori_loop(1, layers, down, f0)

            def put(k, line):
                if first:
                    iter_ref[dst, c, k] = ice * (OMEGA * line)
                else:
                    iter_ref[dst, c, k] = ice * ((1.0 - OMEGA) * iter_ref[src, c, k] + OMEGA * line)

            last = fwd_ref[layers - 1]
            put(layers - 1, last)

            def up(j, s_next):
                k = layers - 2 - j
                line = fwd_ref[k] - ratio_ref[c, k] * s_next
                put(k, line)
                return line

            lax.fori_loop(0, layers - 1, up, last)

    def inner(x):
        x = along_cols(along_rows(x, -HALO), -HALO)
        return x[:rows, :cols]

    buf = 0
    for sweep_idx in range(PASSES):
        run_pass(1 - buf, buf, True, sweep_idx == 0)
        buf = 1 - buf
    velocity_buf = 1 - buf
    for c in range(comps):
        misfit_ref[c] = iter_ref[velocity_buf, c, 0] - obs_ref[c]
        for k in range(layers):
            vel_ref[c, k] = inner(iter_ref[velocity_buf, c, k])
    buf = 0
    for sweep_idx in range(PASSES):
        run_pass(1 - buf, buf, False, sweep_idx == 0)
        buf = 1 - buf
    adjoint_buf = 1 - buf
    for c in range(comps):
        for k in range(layers):
            adj_ref[c, k] = inner(iter_ref[adjoint_buf, c, k])


def shifted(piece, axis, down):
    count = lax.axis_size(axis)
    if down:
        pairs = [(i, i + 1) for i in range(count - 1)]
    else:
        pairs = [(i + 1, i) for i in range(count - 1)]
    return lax.ppermute(piece, axis, pairs)


def local(forcing, viscosity, observed, beta_tiles, ice_mask, tile_owner):
    comps, layers, rows, cols = forcing.shape
    tiles_here = beta_tiles.shape[1]
    planes = [
        forcing.reshape(comps * layers, rows, cols),
        viscosity,
        observed,
        ice_mask.astype(jnp.float32)[None],
        tile_owner.astype(jnp.float32)[None],
    ]
    plane_count = sum(p.shape[0] for p in planes)

    beta_plane = jnp.pad(beta_tiles, ((0, HALO - 1), (0, cols - tiles_here)))[None]
    head = jnp.concatenate([p[:, :HALO] for p in planes] + [beta_plane], axis=0)
    tail = jnp.concatenate([p[:, rows - HALO:] for p in planes] + [beta_plane], axis=0)
    from_above = shifted(tail, "gx", True)
    from_below = shifted(head, "gx", False)

    def stack_rows(lo, hi):
        return jnp.concatenate(
            [from_above[:plane_count, :, lo:hi]]
            + [jnp.concatenate([p[:, :, lo:hi] for p in planes], axis=0)]
            + [from_below[:plane_count, :, lo:hi]],
            axis=1,
        )

    from_left = shifted(stack_rows(cols - HALO, cols), "gy", True)
    from_right = shifted(stack_rows(0, HALO), "gy", False)

    strips_near = jnp.stack(
        [from_above[plane_count, 0, :tiles_here], beta_tiles[0], from_below[plane_count, 0, :tiles_here]]
    )
    friction_rows = lax.all_gather(strips_near, "gy", axis=1, tiled=True)
    tile_count = friction_rows.shape[1]

    packed = jnp.concatenate([from_left, stack_rows(0, cols), from_right], axis=2)
    ext_rows, ext_cols = packed.shape[1], packed.shape[2]
    at = 0
    forcing_ext = packed[at:at + comps * layers].reshape(comps, layers, ext_rows, ext_cols)
    at += comps * layers
    visc_ext = packed[at:at + layers]
    at += layers
    observed_ext = packed[at:at + comps]
    at += comps
    ice_cover = packed[at]
    owner_ext = packed[at + 1].astype(jnp.int32)

    tiles = lax.broadcasted_iota(jnp.int32, (1, 1, tile_count), 2)
    owner_match = owner_ext[:, :, None] == tiles
    row_strip = jnp.concatenate(
        [
            jnp.broadcast_to(friction_rows[0], (HALO, tile_count)),
            jnp.broadcast_to(friction_rows[1], (rows, tile_count)),
            jnp.broadcast_to(friction_rows[2], (HALO, tile_count)),
        ],
        axis=0,
    )
    beta_col = jnp.sum(jnp.where(owner_match, row_strip[:, None, :], 0.0), axis=-1)

    tall = -(-ext_rows // 8) * 8
    wide = -(-ext_cols // 128) * 128

    def fit(x):
        return jnp.pad(x, [(0, 0)] * (x.ndim - 2) + [(0, tall - ext_rows), (0, wide - ext_cols)])

    grid_shape = (comps, layers, tall, wide)
    scratch = [
        pltpu.VMEM((4, layers, tall, wide), jnp.float32),
        pltpu.VMEM((layers, tall, wide), jnp.float32),
        pltpu.VMEM(grid_shape, jnp.float32),
        pltpu.VMEM(grid_shape, jnp.float32),
        pltpu.VMEM((2,) + grid_shape, jnp.float32),
        pltpu.VMEM((layers, tall, wide), jnp.float32),
        pltpu.VMEM((comps, tall, wide), jnp.float32),
    ]
    out_shape = jax.ShapeDtypeStruct(forcing.shape, jnp.float32)
    velocity, adjoint = pl.pallas_call(
        passes_kernel,
        out_shape=(out_shape, out_shape),
        scratch_shapes=scratch,
    )(fit(forcing_ext), fit(visc_ext), fit(observed_ext), fit(ice_cover), fit(beta_col))

    inner = (slice(HALO, HALO + rows), slice(HALO, HALO + cols))
    grad_col = -ice_cover[inner] * beta_col[inner] * jnp.sum(adjoint[:, -1] * velocity[:, -1], axis=0)
    block_match = owner_match[inner[0], inner[1]]
    partial_sum = jnp.sum(jnp.where(block_match, grad_col[:, :, None], 0.0), axis=(0, 1))
    owners = lax.axis_size("gy")
    chunk = tile_count // owners
    gathered = lax.all_gather(partial_sum.reshape(owners, chunk), "gy")
    mine = lax.dynamic_index_in_dim(gathered, lax.axis_index("gy"), axis=1, keepdims=False)
    grad_tiles = jnp.sum(mine, axis=0)[None]
    return (velocity, adjoint, grad_tiles)


def solution(mesh):
    in_specs = (
        P(None, None, "gx", "gy"),
        P(None, "gx", "gy"),
        P(None, "gx", "gy"),
        P("gx", "gy"),
        P("gx", "gy"),
        P("gx", "gy"),
    )
    out_specs = (P(None, None, "gx", "gy"), P(None, None, "gx", "gy"), P("gx", "gy"))
    return jax.shard_map(local, mesh=mesh, in_specs=in_specs, out_specs=out_specs, check_vma=False)
```

```python
import jax
import jax.numpy as jnp
from jax import lax
from jax.sharding import PartitionSpec as P

PASSES = 4


OMEGA = 0.8
VERTICAL = 16.0
HALO = 2 * PASSES - 1


def with_halo(cells, sides, width):
    for axis, dim in sides:
        count = lax.axis_size(axis)
        ends = count - 1
        head = lax.slice_in_dim(cells, 0, width, axis=dim)
        tail = lax.slice_in_dim(cells, cells.shape[dim] - width, cells.shape[dim], axis=dim)
        cells = jnp.concatenate(
            [
                lax.ppermute(tail, axis, [(i, (i + 1) % count) for i in range(ends)]),
                cells,
                lax.ppermute(head, axis, [((i + 1) % count, i) for i in range(ends)]),
            ],
            axis=dim,
        )
    return cells


def lateral_terms(visc_pad):
    centre_visc = visc_pad[:, 1:-1, 1:-1]
    west_face = 0.5 * (centre_visc + visc_pad[:, :-2, 1:-1])
    east_face = 0.5 * (centre_visc + visc_pad[:, 2:, 1:-1])
    south_face = 0.5 * (centre_visc + visc_pad[:, 1:-1, :-2])
    north_face = 0.5 * (centre_visc + visc_pad[:, 1:-1, 2:])
    return (west_face, east_face, south_face, north_face)


def weights_xy():
    along_x = jnp.array([4.0, 1.0], jnp.float32).reshape(2, 1, 1, 1)
    along_y = jnp.array([1.0, 4.0], jnp.float32).reshape(2, 1, 1, 1)
    return (along_x, along_y)


def prepare(visc_pad, beta_col, ice_cover):
    faces = lateral_terms(visc_pad)
    west_face, east_face, south_face, north_face = faces
    along_x, along_y = weights_xy()
    centre_visc = visc_pad[:, 1:-1, 1:-1]
    vertical = VERTICAL * 0.5 * (centre_visc[:-1] + centre_visc[1:])
    zero_row = jnp.zeros_like(centre_visc[:1])
    upper_link = jnp.concatenate([vertical, zero_row], 0)
    lower_link = jnp.concatenate([zero_row, vertical], 0)
    basal = jnp.concatenate([jnp.zeros_like(centre_visc[:-1]), beta_col[None]], 0)
    diagonal = along_x * (west_face + east_face) + along_y * (south_face + north_face)
    diagonal = diagonal + upper_link + lower_link + basal + (1.0 - ice_cover)
    layer_count = visc_pad.shape[0]
    ratio_list = []
    inverse_list = []
    for layer_idx in range(layer_count):
        pivot = diagonal[:, layer_idx]
        if layer_idx > 0:
            pivot = pivot + lower_link[layer_idx] * ratio_list[-1]
        inverse = 1.0 / pivot
        inverse_list.append(inverse)
        ratio_list.append(-upper_link[layer_idx] * inverse)
    return (faces, lower_link, jnp.stack(ratio_list, 1), jnp.stack(inverse_list, 1))


def relax(vel_pad, rhs_field, faces, lower_link, ratios, inverses, ice_cover):
    west_face, east_face, south_face, north_face = faces
    along_x, along_y = weights_xy()
    lateral = along_x * (west_face * vel_pad[:, :, :-2, 1:-1] + east_face * vel_pad[:, :, 2:, 1:-1])
    lateral = lateral + along_y * (
        south_face * vel_pad[:, :, 1:-1, :-2] + north_face * vel_pad[:, :, 1:-1, 2:]
    )
    right_side = rhs_field + lateral
    layer_count = right_side.shape[1]
    forward_list = []
    for layer_idx in range(layer_count):
        value = right_side[:, layer_idx]
        if layer_idx > 0:
            value = value + lower_link[layer_idx] * forward_list[-1]
        forward_list.append(value * inverses[:, layer_idx])
    solved = [None] * layer_count
    solved[layer_count - 1] = forward_list[layer_count - 1]
    for layer_idx in range(layer_count - 2, -1, -1):
        solved[layer_idx] = forward_list[layer_idx] - ratios[:, layer_idx] * solved[layer_idx + 1]
    line_value = jnp.stack(solved, 1)
    centre = vel_pad[:, :, 1:-1, 1:-1]
    return ice_cover * ((1.0 - OMEGA) * centre + OMEGA * line_value)


def pad_cells(field):
    return jnp.pad(field, [(0, 0)] * (field.ndim - 2) + [(1, 1), (1, 1)])


def shifted(piece, axis, down):
    count = lax.axis_size(axis)
    if down:
        pairs = [(i, i + 1) for i in range(count - 1)]
    else:
        pairs = [(i + 1, i) for i in range(count - 1)]
    return lax.ppermute(piece, axis, pairs)


def local(forcing, viscosity, observed, beta_tiles, ice_mask, tile_owner):
    comps, layers, rows, cols = forcing.shape
    friction_row = lax.all_gather(beta_tiles[0], "gy").reshape(-1)
    tile_count = friction_row.shape[0]
    tiles = lax.broadcasted_iota(jnp.int32, (1, 1, tile_count), 2)
    owner_match = tile_owner[:, :, None] == tiles
    beta_here = jnp.sum(jnp.where(owner_match, friction_row[None, None, :], 0.0), axis=-1)

    planes = [
        forcing.reshape(comps * layers, rows, cols),
        viscosity,
        observed,
        ice_mask.astype(jnp.float32)[None],
        beta_here[None],
    ]
    head = jnp.concatenate([p[:, :HALO] for p in planes], axis=0)
    tail = jnp.concatenate([p[:, rows - HALO:] for p in planes], axis=0)
    from_above = shifted(tail, "gx", True)
    from_below = shifted(head, "gx", False)

    def stack_rows(lo, hi):
        return jnp.concatenate(
            [from_above[:, :, lo:hi]]
            + [jnp.concatenate([p[:, :, lo:hi] for p in planes], axis=0)]
            + [from_below[:, :, lo:hi]],
            axis=1,
        )

    from_left = shifted(stack_rows(cols - HALO, cols), "gy", True)
    from_right = shifted(stack_rows(0, HALO), "gy", False)

    packed = jnp.concatenate([from_left, stack_rows(0, cols), from_right], axis=2)
    ext_rows, ext_cols = packed.shape[1], packed.shape[2]
    at = 0
    forcing_ext = packed[at:at + comps * layers].reshape(comps, layers, ext_rows, ext_cols)
    at += comps * layers
    visc_ext = packed[at:at + layers]
    at += layers
    observed_ext = packed[at:at + comps]
    at += comps
    ice_cover = packed[at]
    beta_col = packed[at + 1]

    faces, lower_link, ratios, inverses = prepare(pad_cells(visc_ext), beta_col, ice_cover)

    def advance(field, rhs_field):
        return relax(pad_cells(field), rhs_field, faces, lower_link, ratios, inverses, ice_cover)

    velocity = jnp.zeros_like(forcing_ext)
    for sweep_idx in range(PASSES):
        velocity = advance(velocity, forcing_ext)
    misfit = velocity[:, 0] - observed_ext
    adjoint_rhs = jnp.zeros_like(forcing_ext).at[:, 0].set(misfit)
    adjoint = jnp.zeros_like(forcing_ext)
    for sweep_idx in range(PASSES):
        adjoint = advance(adjoint, adjoint_rhs)

    inner = (slice(HALO, HALO + rows), slice(HALO, HALO + cols))
    velocity = velocity[:, :, inner[0], inner[1]]
    adjoint = adjoint[:, :, inner[0], inner[1]]
    grad_col = -ice_cover[inner] * beta_col[inner] * jnp.sum(adjoint[:, -1] * velocity[:, -1], axis=0)
    partial_sum = jnp.sum(jnp.where(owner_match, grad_col[:, :, None], 0.0), axis=(0, 1))
    owners = lax.axis_size("gy")
    received = lax.all_to_all(partial_sum.reshape(owners, -1), "gy", 0, 0, tiled=True)
    grad_tiles = jnp.sum(received, axis=0)[None]
    return (velocity, adjoint, grad_tiles)


def solution(mesh):
    in_specs = (
        P(None, None, "gx", "gy"),
        P(None, "gx", "gy"),
        P(None, "gx", "gy"),
        P("gx", "gy"),
        P("gx", "gy"),
        P("gx", "gy"),
    )
    out_specs = (P(None, None, "gx", "gy"), P(None, None, "gx", "gy"), P("gx", "gy"))
    return jax.shard_map(local, mesh=mesh, in_specs=in_specs, out_specs=out_specs, check_vma=False)
```

```python
import jax
import jax.numpy as jnp
from jax import lax
from jax.sharding import PartitionSpec as P

PASSES = 4


OMEGA = 0.8
VERTICAL = 16.0
HALO = 2 * PASSES - 1


def with_halo(cells, sides, width):
    for axis, dim in sides:
        count = lax.axis_size(axis)
        ends = count - 1
        head = lax.slice_in_dim(cells, 0, width, axis=dim)
        tail = lax.slice_in_dim(cells, cells.shape[dim] - width, cells.shape[dim], axis=dim)
        cells = jnp.concatenate(
            [
                lax.ppermute(tail, axis, [(i, (i + 1) % count) for i in range(ends)]),
                cells,
                lax.ppermute(head, axis, [((i + 1) % count, i) for i in range(ends)]),
            ],
            axis=dim,
        )
    return cells


def lateral_terms(visc_pad):
    centre_visc = visc_pad[:, 1:-1, 1:-1]
    west_face = 0.5 * (centre_visc + visc_pad[:, :-2, 1:-1])
    east_face = 0.5 * (centre_visc + visc_pad[:, 2:, 1:-1])
    south_face = 0.5 * (centre_visc + visc_pad[:, 1:-1, :-2])
    north_face = 0.5 * (centre_visc + visc_pad[:, 1:-1, 2:])
    return (west_face, east_face, south_face, north_face)


def weights_xy():
    along_x = jnp.array([4.0, 1.0], jnp.float32).reshape(2, 1, 1, 1)
    along_y = jnp.array([1.0, 4.0], jnp.float32).reshape(2, 1, 1, 1)
    return (along_x, along_y)


def prepare(visc_pad, beta_col, ice_cover):
    faces = lateral_terms(visc_pad)
    west_face, east_face, south_face, north_face = faces
    along_x, along_y = weights_xy()
    centre_visc = visc_pad[:, 1:-1, 1:-1]
    vertical = VERTICAL * 0.5 * (centre_visc[:-1] + centre_visc[1:])
    zero_row = jnp.zeros_like(centre_visc[:1])
    upper_link = jnp.concatenate([vertical, zero_row], 0)
    lower_link = jnp.concatenate([zero_row, vertical], 0)
    basal = jnp.concatenate([jnp.zeros_like(centre_visc[:-1]), beta_col[None]], 0)
    diagonal = along_x * (west_face + east_face) + along_y * (south_face + north_face)
    diagonal = diagonal + upper_link + lower_link + basal + (1.0 - ice_cover)
    layer_count = visc_pad.shape[0]
    ratio_list = []
    inverse_list = []
    for layer_idx in range(layer_count):
        pivot = diagonal[:, layer_idx]
        if layer_idx > 0:
            pivot = pivot + lower_link[layer_idx] * ratio_list[-1]
        inverse = 1.0 / pivot
        inverse_list.append(inverse)
        ratio_list.append(-upper_link[layer_idx] * inverse)
    return (faces, lower_link, jnp.stack(ratio_list, 1), jnp.stack(inverse_list, 1))


def relax(vel_pad, rhs_field, faces, lower_link, ratios, inverses, ice_cover):
    west_face, east_face, south_face, north_face = faces
    along_x, along_y = weights_xy()
    lateral = along_x * (west_face * vel_pad[:, :, :-2, 1:-1] + east_face * vel_pad[:, :, 2:, 1:-1])
    lateral = lateral + along_y * (
        south_face * vel_pad[:, :, 1:-1, :-2] + north_face * vel_pad[:, :, 1:-1, 2:]
    )
    right_side = rhs_field + lateral
    layer_count = right_side.shape[1]
    forward_list = []
    for layer_idx in range(layer_count):
        value = right_side[:, layer_idx]
        if layer_idx > 0:
            value = value + lower_link[layer_idx] * forward_list[-1]
        forward_list.append(value * inverses[:, layer_idx])
    solved = [None] * layer_count
    solved[layer_count - 1] = forward_list[layer_count - 1]
    for layer_idx in range(layer_count - 2, -1, -1):
        solved[layer_idx] = forward_list[layer_idx] - ratios[:, layer_idx] * solved[layer_idx + 1]
    line_value = jnp.stack(solved, 1)
    centre = vel_pad[:, :, 1:-1, 1:-1]
    return ice_cover * ((1.0 - OMEGA) * centre + OMEGA * line_value)


def lane_weights(comps, width):
    along_x = jnp.concatenate([jnp.full((width,), (4.0, 1.0)[c], jnp.float32) for c in range(comps)])
    along_y = jnp.concatenate([jnp.full((width,), (1.0, 4.0)[c], jnp.float32) for c in range(comps)])
    return (along_x, along_y)


def prepare_lanes(visc_pad, beta_col, ice_cover, weights):
    faces = lateral_terms(visc_pad)
    west_face, east_face, south_face, north_face = faces
    along_x, along_y = weights
    centre_visc = visc_pad[:, 1:-1, 1:-1]
    vertical = VERTICAL * 0.5 * (centre_visc[:-1] + centre_visc[1:])
    zero_row = jnp.zeros_like(centre_visc[:1])
    upper_link = jnp.concatenate([vertical, zero_row], 0)
    lower_link = jnp.concatenate([zero_row, vertical], 0)
    basal = jnp.concatenate([jnp.zeros_like(centre_visc[:-1]), beta_col[None]], 0)
    diagonal = along_x * (west_face + east_face) + along_y * (south_face + north_face)
    diagonal = diagonal + upper_link + lower_link + basal + (1.0 - ice_cover)
    layer_count = visc_pad.shape[0]
    ratio_list = []
    inverse_list = []
    for layer_idx in range(layer_count):
        pivot = diagonal[layer_idx]
        if layer_idx > 0:
            pivot = pivot + lower_link[layer_idx] * ratio_list[-1]
        inverse = 1.0 / pivot
        inverse_list.append(inverse)
        ratio_list.append(-upper_link[layer_idx] * inverse)
    return (faces, lower_link, ratio_list, inverse_list)


def relax_lanes(vel_pad, rhs_field, faces, lower_link, ratios, inverses, ice_cover, weights):
    west_face, east_face, south_face, north_face = faces
    along_x, along_y = weights
    lateral = along_x * (west_face * vel_pad[:, :-2, 1:-1] + east_face * vel_pad[:, 2:, 1:-1])
    lateral = lateral + along_y * (
        south_face * vel_pad[:, 1:-1, :-2] + north_face * vel_pad[:, 1:-1, 2:]
    )
    right_side = rhs_field + lateral
    layer_count = right_side.shape[0]
    forward_list = []
    for layer_idx in range(layer_count):
        value = right_side[layer_idx]
        if layer_idx > 0:
            value = value + lower_link[layer_idx] * forward_list[-1]
        forward_list.append(value * inverses[layer_idx])
    solved = [None] * layer_count
    solved[layer_count - 1] = forward_list[layer_count - 1]
    for layer_idx in range(layer_count - 2, -1, -1):
        solved[layer_idx] = forward_list[layer_idx] - ratios[layer_idx] * solved[layer_idx + 1]
    line_value = jnp.stack(solved, 0)
    centre = vel_pad[:, 1:-1, 1:-1]
    return ice_cover * ((1.0 - OMEGA) * centre + OMEGA * line_value)


def pad_cells(field):
    return jnp.pad(field, [(0, 0)] * (field.ndim - 2) + [(1, 1), (1, 1)])


def shifted(piece, axis, down):
    count = lax.axis_size(axis)
    if down:
        pairs = [(i, i + 1) for i in range(count - 1)]
    else:
        pairs = [(i + 1, i) for i in range(count - 1)]
    return lax.ppermute(piece, axis, pairs)


def local(forcing, viscosity, observed, beta_tiles, ice_mask, tile_owner):
    comps, layers, rows, cols = forcing.shape
    tiles_here = beta_tiles.shape[1]
    planes = [
        forcing.reshape(comps * layers, rows, cols),
        viscosity,
        observed,
        ice_mask.astype(jnp.float32)[None],
        tile_owner.astype(jnp.float32)[None],
    ]
    plane_count = sum(p.shape[0] for p in planes)

    beta_plane = jnp.pad(beta_tiles, ((0, HALO - 1), (0, cols - tiles_here)))[None]
    head = jnp.concatenate([p[:, :HALO] for p in planes] + [beta_plane], axis=0)
    tail = jnp.concatenate([p[:, rows - HALO:] for p in planes] + [beta_plane], axis=0)
    from_above = shifted(tail, "gx", True)
    from_below = shifted(head, "gx", False)

    def stack_rows(lo, hi):
        return jnp.concatenate(
            [from_above[:plane_count, :, lo:hi]]
            + [jnp.concatenate([p[:, :, lo:hi] for p in planes], axis=0)]
            + [from_below[:plane_count, :, lo:hi]],
            axis=1,
        )

    from_left = shifted(stack_rows(cols - HALO, cols), "gy", True)
    from_right = shifted(stack_rows(0, HALO), "gy", False)

    strips_near = jnp.stack(
        [from_above[plane_count, 0, :tiles_here], beta_tiles[0], from_below[plane_count, 0, :tiles_here]]
    )
    friction_rows = lax.all_gather(strips_near, "gy", axis=1, tiled=True)
    tile_count = friction_rows.shape[1]

    packed = jnp.concatenate([from_left, stack_rows(0, cols), from_right], axis=2)
    ext_rows, ext_cols = packed.shape[1], packed.shape[2]
    at = 0
    forcing_ext = packed[at:at + comps * layers].reshape(comps, layers, ext_rows, ext_cols)
    at += comps * layers
    visc_ext = packed[at:at + layers]
    at += layers
    observed_ext = packed[at:at + comps]
    at += comps
    ice_cover = packed[at]
    owner_ext = packed[at + 1].astype(jnp.int32)

    tiles = lax.broadcasted_iota(jnp.int32, (1, 1, tile_count), 2)
    owner_match = owner_ext[:, :, None] == tiles
    row_strip = jnp.concatenate(
        [
            jnp.broadcast_to(friction_rows[0], (HALO, tile_count)),
            jnp.broadcast_to(friction_rows[1], (rows, tile_count)),
            jnp.broadcast_to(friction_rows[2], (HALO, tile_count)),
        ],
        axis=0,
    )
    beta_col = jnp.sum(jnp.where(owner_match, row_strip[:, None, :], 0.0), axis=-1)

    def side_by_side(per_comp):
        return jnp.concatenate([per_comp[c] for c in range(comps)], axis=-1)

    weights = lane_weights(comps, ext_cols)
    visc_lanes = side_by_side([visc_ext] * comps)
    ice_lanes = side_by_side([ice_cover] * comps)
    beta_lanes = side_by_side([beta_col] * comps)
    forcing_lanes = side_by_side([forcing_ext[c] for c in range(comps)])
    observed_lanes = side_by_side([observed_ext[c] for c in range(comps)])
    faces, lower_link, ratios, inverses = prepare_lanes(
        pad_cells(visc_lanes), beta_lanes, ice_lanes, weights
    )

    def advance(field, rhs_field):
        return relax_lanes(pad_cells(field), rhs_field, faces, lower_link, ratios, inverses, ice_lanes, weights)

    velocity = jnp.zeros_like(forcing_lanes)
    for sweep_idx in range(PASSES):
        velocity = advance(velocity, forcing_lanes)
    misfit = velocity[0] - observed_lanes
    adjoint_rhs = jnp.zeros_like(forcing_lanes).at[0].set(misfit)
    adjoint = jnp.zeros_like(forcing_lanes)
    for sweep_idx in range(PASSES):
        adjoint = advance(adjoint, adjoint_rhs)

    inner = (slice(HALO, HALO + rows), slice(HALO, HALO + cols))

    def split(field):
        return jnp.stack(
            [field[:, inner[0], c * ext_cols + HALO:c * ext_cols + HALO + cols] for c in range(comps)]
        )

    velocity = split(velocity)
    adjoint = split(adjoint)
    grad_col = -ice_cover[inner] * beta_col[inner] * jnp.sum(adjoint[:, -1] * velocity[:, -1], axis=0)
    block_match = owner_match[inner[0], inner[1]]
    partial_sum = jnp.sum(jnp.where(block_match, grad_col[:, :, None], 0.0), axis=(0, 1))
    owners = lax.axis_size("gy")
    chunk = tile_count // owners
    gathered = lax.all_gather(partial_sum.reshape(owners, chunk), "gy")
    mine = lax.dynamic_index_in_dim(gathered, lax.axis_index("gy"), axis=1, keepdims=False)
    grad_tiles = jnp.sum(mine, axis=0)[None]
    return (velocity, adjoint, grad_tiles)


def solution(mesh):
    in_specs = (
        P(None, None, "gx", "gy"),
        P(None, "gx", "gy"),
        P(None, "gx", "gy"),
        P("gx", "gy"),
        P("gx", "gy"),
        P("gx", "gy"),
    )
    out_specs = (P(None, None, "gx", "gy"), P(None, None, "gx", "gy"), P("gx", "gy"))
    return jax.shard_map(local, mesh=mesh, in_specs=in_specs, out_specs=out_specs, check_vma=False)
```

```python
import jax
import jax.numpy as jnp
from jax import lax
from jax.sharding import PartitionSpec as P

PASSES = 4


OMEGA = 0.8
VERTICAL = 16.0
HALO = 2 * PASSES - 1


def with_halo(cells, sides, width):
    for axis, dim in sides:
        count = lax.axis_size(axis)
        ends = count - 1
        head = lax.slice_in_dim(cells, 0, width, axis=dim)
        tail = lax.slice_in_dim(cells, cells.shape[dim] - width, cells.shape[dim], axis=dim)
        cells = jnp.concatenate(
            [
                lax.ppermute(tail, axis, [(i, (i + 1) % count) for i in range(ends)]),
                cells,
                lax.ppermute(head, axis, [((i + 1) % count, i) for i in range(ends)]),
            ],
            axis=dim,
        )
    return cells


def lateral_terms(visc_pad):
    centre_visc = visc_pad[:, 1:-1, 1:-1]
    west_face = 0.5 * (centre_visc + visc_pad[:, :-2, 1:-1])
    east_face = 0.5 * (centre_visc + visc_pad[:, 2:, 1:-1])
    south_face = 0.5 * (centre_visc + visc_pad[:, 1:-1, :-2])
    north_face = 0.5 * (centre_visc + visc_pad[:, 1:-1, 2:])
    return (west_face, east_face, south_face, north_face)


def weights_xy():
    along_x = jnp.array([4.0, 1.0], jnp.float32).reshape(2, 1, 1, 1)
    along_y = jnp.array([1.0, 4.0], jnp.float32).reshape(2, 1, 1, 1)
    return (along_x, along_y)


def prepare(visc_pad, beta_col, ice_cover):
    faces = lateral_terms(visc_pad)
    west_face, east_face, south_face, north_face = faces
    along_x, along_y = weights_xy()
    centre_visc = visc_pad[:, 1:-1, 1:-1]
    vertical = VERTICAL * 0.5 * (centre_visc[:-1] + centre_visc[1:])
    zero_row = jnp.zeros_like(centre_visc[:1])
    upper_link = jnp.concatenate([vertical, zero_row], 0)
    lower_link = jnp.concatenate([zero_row, vertical], 0)
    basal = jnp.concatenate([jnp.zeros_like(centre_visc[:-1]), beta_col[None]], 0)
    diagonal = along_x * (west_face + east_face) + along_y * (south_face + north_face)
    diagonal = diagonal + upper_link + lower_link + basal + (1.0 - ice_cover)
    layer_count = visc_pad.shape[0]
    ratio_list = []
    inverse_list = []
    for layer_idx in range(layer_count):
        pivot = diagonal[:, layer_idx]
        if layer_idx > 0:
            pivot = pivot + lower_link[layer_idx] * ratio_list[-1]
        inverse = 1.0 / pivot
        inverse_list.append(inverse)
        ratio_list.append(-upper_link[layer_idx] * inverse)
    return (faces, lower_link, jnp.stack(ratio_list, 1), jnp.stack(inverse_list, 1))


def relax(vel_pad, rhs_field, faces, lower_link, ratios, inverses, ice_cover):
    west_face, east_face, south_face, north_face = faces
    along_x, along_y = weights_xy()
    lateral = along_x * (west_face * vel_pad[:, :, :-2, 1:-1] + east_face * vel_pad[:, :, 2:, 1:-1])
    lateral = lateral + along_y * (
        south_face * vel_pad[:, :, 1:-1, :-2] + north_face * vel_pad[:, :, 1:-1, 2:]
    )
    right_side = rhs_field + lateral
    layer_count = right_side.shape[1]
    forward_list = []
    for layer_idx in range(layer_count):
        value = right_side[:, layer_idx]
        if layer_idx > 0:
            value = value + lower_link[layer_idx] * forward_list[-1]
        forward_list.append(value * inverses[:, layer_idx])
    solved = [None] * layer_count
    solved[layer_count - 1] = forward_list[layer_count - 1]
    for layer_idx in range(layer_count - 2, -1, -1):
        solved[layer_idx] = forward_list[layer_idx] - ratios[:, layer_idx] * solved[layer_idx + 1]
    line_value = jnp.stack(solved, 1)
    centre = vel_pad[:, :, 1:-1, 1:-1]
    return ice_cover * ((1.0 - OMEGA) * centre + OMEGA * line_value)


def lane_weights(comps, width):
    along_x = jnp.concatenate([jnp.full((width,), (4.0, 1.0)[c], jnp.float32) for c in range(comps)])
    along_y = jnp.concatenate([jnp.full((width,), (1.0, 4.0)[c], jnp.float32) for c in range(comps)])
    return (along_x, along_y)


def prepare_lanes(visc_pad, beta_col, ice_cover, weights):
    faces = lateral_terms(visc_pad)
    west_face, east_face, south_face, north_face = faces
    along_x, along_y = weights
    centre_visc = visc_pad[:, 1:-1, 1:-1]
    vertical = VERTICAL * 0.5 * (centre_visc[:-1] + centre_visc[1:])
    zero_row = jnp.zeros_like(centre_visc[:1])
    upper_link = jnp.concatenate([vertical, zero_row], 0)
    lower_link = jnp.concatenate([zero_row, vertical], 0)
    basal = jnp.concatenate([jnp.zeros_like(centre_visc[:-1]), beta_col[None]], 0)
    diagonal = along_x * (west_face + east_face) + along_y * (south_face + north_face)
    diagonal = diagonal + upper_link + lower_link + basal + (1.0 - ice_cover)
    layer_count = visc_pad.shape[0]
    ratio_list = []
    inverse_list = []
    for layer_idx in range(layer_count):
        pivot = diagonal[layer_idx]
        if layer_idx > 0:
            pivot = pivot + lower_link[layer_idx] * ratio_list[-1]
        inverse = 1.0 / pivot
        inverse_list.append(inverse)
        ratio_list.append(-upper_link[layer_idx] * inverse)
    return (faces, lower_link, ratio_list, inverse_list)


def relax_lanes(vel_pad, rhs_field, faces, lower_link, ratios, inverses, ice_cover, weights):
    west_face, east_face, south_face, north_face = faces
    along_x, along_y = weights
    lateral = along_x * (west_face * vel_pad[:, :-2, 1:-1] + east_face * vel_pad[:, 2:, 1:-1])
    lateral = lateral + along_y * (
        south_face * vel_pad[:, 1:-1, :-2] + north_face * vel_pad[:, 1:-1, 2:]
    )
    right_side = rhs_field + lateral
    layer_count = right_side.shape[0]
    forward_list = []
    for layer_idx in range(layer_count):
        value = right_side[layer_idx]
        if layer_idx > 0:
            value = value + lower_link[layer_idx] * forward_list[-1]
        forward_list.append(value * inverses[layer_idx])
    solved = [None] * layer_count
    solved[layer_count - 1] = forward_list[layer_count - 1]
    for layer_idx in range(layer_count - 2, -1, -1):
        solved[layer_idx] = forward_list[layer_idx] - ratios[layer_idx] * solved[layer_idx + 1]
    line_value = jnp.stack(solved, 0)
    centre = vel_pad[:, 1:-1, 1:-1]
    return ice_cover * ((1.0 - OMEGA) * centre + OMEGA * line_value)


def pad_cells(field):
    return jnp.pad(field, [(0, 0)] * (field.ndim - 2) + [(1, 1), (1, 1)])


def shifted(piece, axis, down):
    count = lax.axis_size(axis)
    if down:
        pairs = [(i, i + 1) for i in range(count - 1)]
    else:
        pairs = [(i + 1, i) for i in range(count - 1)]
    return lax.ppermute(piece, axis, pairs)


def local(forcing, viscosity, observed, beta_tiles, ice_mask, tile_owner):
    comps, layers, rows, cols = forcing.shape
    tiles_here = beta_tiles.shape[1]
    planes = [
        forcing.reshape(comps * layers, rows, cols),
        viscosity,
        observed,
        ice_mask.astype(jnp.float32)[None],
        tile_owner.astype(jnp.float32)[None],
    ]
    plane_count = sum(p.shape[0] for p in planes)

    beta_plane = jnp.pad(beta_tiles, ((0, HALO - 1), (0, cols - tiles_here)))[None]
    head = jnp.concatenate([p[:, :HALO] for p in planes] + [beta_plane], axis=0)
    tail = jnp.concatenate([p[:, rows - HALO:] for p in planes] + [beta_plane], axis=0)
    from_above = shifted(tail, "gx", True)
    from_below = shifted(head, "gx", False)

    def stack_rows(lo, hi):
        return jnp.concatenate(
            [from_above[:plane_count, :, lo:hi]]
            + [jnp.concatenate([p[:, :, lo:hi] for p in planes], axis=0)]
            + [from_below[:plane_count, :, lo:hi]],
            axis=1,
        )

    from_left = shifted(stack_rows(cols - HALO, cols), "gy", True)
    from_right = shifted(stack_rows(0, HALO), "gy", False)

    strips_near = jnp.stack(
        [from_above[plane_count, 0, :tiles_here], beta_tiles[0], from_below[plane_count, 0, :tiles_here]]
    )
    friction_rows = lax.all_gather(strips_near, "gy", axis=1, tiled=True)
    tile_count = friction_rows.shape[1]

    packed = jnp.concatenate([from_left, stack_rows(0, cols), from_right], axis=2)
    ext_rows, ext_cols = packed.shape[1], packed.shape[2]
    at = 0
    forcing_ext = packed[at:at + comps * layers].reshape(comps, layers, ext_rows, ext_cols)
    at += comps * layers
    visc_ext = packed[at:at + layers]
    at += layers
    observed_ext = packed[at:at + comps]
    at += comps
    ice_cover = packed[at]
    owner_ext = packed[at + 1].astype(jnp.int32)

    tiles = lax.broadcasted_iota(jnp.int32, (tile_count, 1, 1), 0)
    owner_match = owner_ext[None] == tiles
    row_strip = jnp.concatenate(
        [
            jnp.broadcast_to(friction_rows[0][:, None], (tile_count, HALO)),
            jnp.broadcast_to(friction_rows[1][:, None], (tile_count, rows)),
            jnp.broadcast_to(friction_rows[2][:, None], (tile_count, HALO)),
        ],
        axis=1,
    )
    beta_col = jnp.sum(jnp.where(owner_match, row_strip[:, :, None], 0.0), axis=0)

    def side_by_side(per_comp):
        return jnp.concatenate([per_comp[c] for c in range(comps)], axis=-1)

    weights = lane_weights(comps, ext_cols)
    visc_lanes = side_by_side([visc_ext] * comps)
    ice_lanes = side_by_side([ice_cover] * comps)
    beta_lanes = side_by_side([beta_col] * comps)
    forcing_lanes = side_by_side([forcing_ext[c] for c in range(comps)])
    observed_lanes = side_by_side([observed_ext[c] for c in range(comps)])
    faces, lower_link, ratios, inverses = prepare_lanes(
        pad_cells(visc_lanes), beta_lanes, ice_lanes, weights
    )

    def advance(field, rhs_field):
        return relax_lanes(pad_cells(field), rhs_field, faces, lower_link, ratios, inverses, ice_lanes, weights)

    velocity = jnp.zeros_like(forcing_lanes)
    for sweep_idx in range(PASSES):
        velocity = advance(velocity, forcing_lanes)
    misfit = velocity[0] - observed_lanes
    adjoint_rhs = jnp.zeros_like(forcing_lanes).at[0].set(misfit)
    adjoint = jnp.zeros_like(forcing_lanes)
    for sweep_idx in range(PASSES):
        adjoint = advance(adjoint, adjoint_rhs)

    inner = (slice(HALO, HALO + rows), slice(HALO, HALO + cols))

    def split(field):
        return jnp.stack(
            [field[:, inner[0], c * ext_cols + HALO:c * ext_cols + HALO + cols] for c in range(comps)]
        )

    velocity = split(velocity)
    adjoint = split(adjoint)
    grad_col = -ice_cover[inner] * beta_col[inner] * jnp.sum(adjoint[:, -1] * velocity[:, -1], axis=0)
    block_match = owner_match[:, inner[0], inner[1]]
    partial_sum = jnp.sum(jnp.where(block_match, grad_col[None], 0.0), axis=(1, 2))
    owners = lax.axis_size("gy")
    chunk = tile_count // owners
    gathered = lax.all_gather(partial_sum.reshape(owners, chunk), "gy")
    mine = lax.dynamic_index_in_dim(gathered, lax.axis_index("gy"), axis=1, keepdims=False)
    grad_tiles = jnp.sum(mine, axis=0)[None]
    return (velocity, adjoint, grad_tiles)


def solution(mesh):
    in_specs = (
        P(None, None, "gx", "gy"),
        P(None, "gx", "gy"),
        P(None, "gx", "gy"),
        P("gx", "gy"),
        P("gx", "gy"),
        P("gx", "gy"),
    )
    out_specs = (P(None, None, "gx", "gy"), P(None, None, "gx", "gy"), P("gx", "gy"))
    return jax.shard_map(local, mesh=mesh, in_specs=in_specs, out_specs=out_specs, check_vma=False)
```

```python
import jax
import jax.numpy as jnp
from jax import lax
from jax.sharding import PartitionSpec as P

PASSES = 4


OMEGA = 0.8
VERTICAL = 16.0
HALO = 2 * PASSES - 1


def with_halo(cells, sides, width):
    for axis, dim in sides:
        count = lax.axis_size(axis)
        ends = count - 1
        head = lax.slice_in_dim(cells, 0, width, axis=dim)
        tail = lax.slice_in_dim(cells, cells.shape[dim] - width, cells.shape[dim], axis=dim)
        cells = jnp.concatenate(
            [
                lax.ppermute(tail, axis, [(i, (i + 1) % count) for i in range(ends)]),
                cells,
                lax.ppermute(head, axis, [((i + 1) % count, i) for i in range(ends)]),
            ],
            axis=dim,
        )
    return cells


def lateral_terms(visc_pad):
    centre_visc = visc_pad[:, 1:-1, 1:-1]
    west_face = 0.5 * (centre_visc + visc_pad[:, :-2, 1:-1])
    east_face = 0.5 * (centre_visc + visc_pad[:, 2:, 1:-1])
    south_face = 0.5 * (centre_visc + visc_pad[:, 1:-1, :-2])
    north_face = 0.5 * (centre_visc + visc_pad[:, 1:-1, 2:])
    return (west_face, east_face, south_face, north_face)


def weights_xy():
    along_x = jnp.array([4.0, 1.0], jnp.float32).reshape(2, 1, 1, 1)
    along_y = jnp.array([1.0, 4.0], jnp.float32).reshape(2, 1, 1, 1)
    return (along_x, along_y)


def prepare(visc_pad, beta_col, ice_cover):
    faces = lateral_terms(visc_pad)
    west_face, east_face, south_face, north_face = faces
    along_x, along_y = weights_xy()
    centre_visc = visc_pad[:, 1:-1, 1:-1]
    vertical = VERTICAL * 0.5 * (centre_visc[:-1] + centre_visc[1:])
    zero_row = jnp.zeros_like(centre_visc[:1])
    upper_link = jnp.concatenate([vertical, zero_row], 0)
    lower_link = jnp.concatenate([zero_row, vertical], 0)
    basal = jnp.concatenate([jnp.zeros_like(centre_visc[:-1]), beta_col[None]], 0)
    diagonal = along_x * (west_face + east_face) + along_y * (south_face + north_face)
    diagonal = diagonal + upper_link + lower_link + basal + (1.0 - ice_cover)
    layer_count = visc_pad.shape[0]
    ratio_list = []
    inverse_list = []
    for layer_idx in range(layer_count):
        pivot = diagonal[:, layer_idx]
        if layer_idx > 0:
            pivot = pivot + lower_link[layer_idx] * ratio_list[-1]
        inverse = 1.0 / pivot
        inverse_list.append(inverse)
        ratio_list.append(-upper_link[layer_idx] * inverse)
    return (faces, lower_link, jnp.stack(ratio_list, 1), jnp.stack(inverse_list, 1))


def relax(vel_pad, rhs_field, faces, lower_link, ratios, inverses, ice_cover):
    west_face, east_face, south_face, north_face = faces
    along_x, along_y = weights_xy()
    lateral = along_x * (west_face * vel_pad[:, :, :-2, 1:-1] + east_face * vel_pad[:, :, 2:, 1:-1])
    lateral = lateral + along_y * (
        south_face * vel_pad[:, :, 1:-1, :-2] + north_face * vel_pad[:, :, 1:-1, 2:]
    )
    right_side = rhs_field + lateral
    layer_count = right_side.shape[1]
    forward_list = []
    for layer_idx in range(layer_count):
        value = right_side[:, layer_idx]
        if layer_idx > 0:
            value = value + lower_link[layer_idx] * forward_list[-1]
        forward_list.append(value * inverses[:, layer_idx])
    solved = [None] * layer_count
    solved[layer_count - 1] = forward_list[layer_count - 1]
    for layer_idx in range(layer_count - 2, -1, -1):
        solved[layer_idx] = forward_list[layer_idx] - ratios[:, layer_idx] * solved[layer_idx + 1]
    line_value = jnp.stack(solved, 1)
    centre = vel_pad[:, :, 1:-1, 1:-1]
    return ice_cover * ((1.0 - OMEGA) * centre + OMEGA * line_value)


def lane_weights(comps, width):
    along_x = jnp.concatenate([jnp.full((width,), (4.0, 1.0)[c], jnp.float32) for c in range(comps)])
    along_y = jnp.concatenate([jnp.full((width,), (1.0, 4.0)[c], jnp.float32) for c in range(comps)])
    return (along_x, along_y)


def prepare_lanes(visc_pad, beta_col, ice_cover, weights):
    faces = lateral_terms(visc_pad)
    west_face, east_face, south_face, north_face = faces
    along_x, along_y = weights
    centre_visc = visc_pad[:, 1:-1, 1:-1]
    vertical = VERTICAL * 0.5 * (centre_visc[:-1] + centre_visc[1:])
    zero_row = jnp.zeros_like(centre_visc[:1])
    upper_link = jnp.concatenate([vertical, zero_row], 0)
    lower_link = jnp.concatenate([zero_row, vertical], 0)
    basal = jnp.concatenate([jnp.zeros_like(centre_visc[:-1]), beta_col[None]], 0)
    diagonal = along_x * (west_face + east_face) + along_y * (south_face + north_face)
    diagonal = diagonal + upper_link + lower_link + basal + (1.0 - ice_cover)
    layer_count = visc_pad.shape[0]
    ratio_list = []
    inverse_list = []
    for layer_idx in range(layer_count):
        pivot = diagonal[layer_idx]
        if layer_idx > 0:
            pivot = pivot + lower_link[layer_idx] * ratio_list[-1]
        inverse = 1.0 / pivot
        inverse_list.append(inverse)
        ratio_list.append(-upper_link[layer_idx] * inverse)
    return (faces, lower_link, ratio_list, inverse_list)


def relax_lanes(vel_pad, rhs_field, faces, lower_link, ratios, inverses, ice_cover, weights):
    west_face, east_face, south_face, north_face = faces
    along_x, along_y = weights
    lateral = along_x * (west_face * vel_pad[:, :-2, 1:-1] + east_face * vel_pad[:, 2:, 1:-1])
    lateral = lateral + along_y * (
        south_face * vel_pad[:, 1:-1, :-2] + north_face * vel_pad[:, 1:-1, 2:]
    )
    right_side = rhs_field + lateral
    layer_count = right_side.shape[0]
    forward_list = []
    for layer_idx in range(layer_count):
        value = right_side[layer_idx]
        if layer_idx > 0:
            value = value + lower_link[layer_idx] * forward_list[-1]
        forward_list.append(value * inverses[layer_idx])
    solved = [None] * layer_count
    solved[layer_count - 1] = forward_list[layer_count - 1]
    for layer_idx in range(layer_count - 2, -1, -1):
        solved[layer_idx] = forward_list[layer_idx] - ratios[layer_idx] * solved[layer_idx + 1]
    line_value = jnp.stack(solved, 0)
    centre = vel_pad[:, 1:-1, 1:-1]
    return ice_cover * ((1.0 - OMEGA) * centre + OMEGA * line_value)


def pad_cells(field):
    return jnp.pad(field, [(0, 0)] * (field.ndim - 2) + [(1, 1), (1, 1)])


def shifted(piece, axis, down):
    count = lax.axis_size(axis)
    if down:
        pairs = [(i, i + 1) for i in range(count - 1)]
    else:
        pairs = [(i + 1, i) for i in range(count - 1)]
    return lax.ppermute(piece, axis, pairs)


def local(forcing, viscosity, observed, beta_tiles, ice_mask, tile_owner):
    comps, layers, rows, cols = forcing.shape
    tiles_here = beta_tiles.shape[1]
    planes = [
        forcing.reshape(comps * layers, rows, cols),
        viscosity,
        observed,
        ice_mask.astype(jnp.float32)[None],
        tile_owner.astype(jnp.float32)[None],
    ]
    plane_count = sum(p.shape[0] for p in planes)

    beta_plane = jnp.pad(beta_tiles, ((0, HALO - 1), (0, cols - tiles_here)))[None]
    head = jnp.concatenate([p[:, :HALO] for p in planes] + [beta_plane], axis=0)
    tail = jnp.concatenate([p[:, rows - HALO:] for p in planes] + [beta_plane], axis=0)
    from_above = shifted(tail, "gx", True)
    from_below = shifted(head, "gx", False)

    def stack_rows(lo, hi):
        return jnp.concatenate(
            [from_above[:plane_count, :, lo:hi]]
            + [jnp.concatenate([p[:, :, lo:hi] for p in planes], axis=0)]
            + [from_below[:plane_count, :, lo:hi]],
            axis=1,
        )

    from_left = shifted(stack_rows(cols - HALO, cols), "gy", True)
    from_right = shifted(stack_rows(0, HALO), "gy", False)

    strips_near = jnp.stack(
        [from_above[plane_count, 0, :tiles_here], beta_tiles[0], from_below[plane_count, 0, :tiles_here]]
    )
    friction_rows = lax.all_gather(strips_near, "gy", axis=1, tiled=True)
    tile_count = friction_rows.shape[1]

    packed = jnp.concatenate([from_left, stack_rows(0, cols), from_right], axis=2)
    ext_rows, ext_cols = packed.shape[1], packed.shape[2]
    at = 0
    forcing_ext = packed[at:at + comps * layers].reshape(comps, layers, ext_rows, ext_cols)
    at += comps * layers
    visc_ext = packed[at:at + layers]
    at += layers
    observed_ext = packed[at:at + comps]
    at += comps
    ice_cover = packed[at]
    owner_ext = packed[at + 1].astype(jnp.int32)

    strip_table = friction_rows.T
    high = lax.reduce_precision(strip_table, exponent_bits=8, mantissa_bits=7)
    rest = strip_table - high
    middle = lax.reduce_precision(rest, exponent_bits=8, mantissa_bits=7)
    low = rest - middle
    parts = jnp.concatenate([high, middle, low], axis=1).astype(jnp.bfloat16)
    tiles = lax.broadcasted_iota(jnp.int32, (1, 1, tile_count), 2)
    one_hot = (owner_ext[:, :, None] == tiles).astype(jnp.bfloat16)
    looked_up = lax.dot_general(
        one_hot, parts, (((2,), (0,)), ((), ())), preferred_element_type=jnp.float32
    )
    band = lax.broadcasted_iota(jnp.int32, (ext_rows, 1), 0)
    strip_of_row = jnp.where(band < HALO, 0, jnp.where(band < HALO + rows, 1, 2))
    near = friction_rows.shape[0]
    beta_col = sum(
        jnp.where(strip_of_row == k, looked_up[:, :, k] + looked_up[:, :, near + k] + looked_up[:, :, 2 * near + k], 0.0)
        for k in range(near)
    )

    def side_by_side(per_comp):
        return jnp.concatenate([per_comp[c] for c in range(comps)], axis=-1)

    weights = lane_weights(comps, ext_cols)
    visc_lanes = side_by_side([visc_ext] * comps)
    ice_lanes = side_by_side([ice_cover] * comps)
    beta_lanes = side_by_side([beta_col] * comps)
    forcing_lanes = side_by_side([forcing_ext[c] for c in range(comps)])
    observed_lanes = side_by_side([observed_ext[c] for c in range(comps)])
    faces, lower_link, ratios, inverses = prepare_lanes(
        pad_cells(visc_lanes), beta_lanes, ice_lanes, weights
    )

    def advance(field, rhs_field):
        return relax_lanes(pad_cells(field), rhs_field, faces, lower_link, ratios, inverses, ice_lanes, weights)

    velocity = jnp.zeros_like(forcing_lanes)
    for sweep_idx in range(PASSES):
        velocity = advance(velocity, forcing_lanes)
    misfit = velocity[0] - observed_lanes
    adjoint_rhs = jnp.zeros_like(forcing_lanes).at[0].set(misfit)
    adjoint = jnp.zeros_like(forcing_lanes)
    for sweep_idx in range(PASSES):
        adjoint = advance(adjoint, adjoint_rhs)

    inner = (slice(HALO, HALO + rows), slice(HALO, HALO + cols))

    def split(field):
        return jnp.stack(
            [field[:, inner[0], c * ext_cols + HALO:c * ext_cols + HALO + cols] for c in range(comps)]
        )

    velocity = split(velocity)
    adjoint = split(adjoint)
    grad_col = -ice_cover[inner] * beta_col[inner] * jnp.sum(adjoint[:, -1] * velocity[:, -1], axis=0)
    block_match = tile_owner[None] == lax.broadcasted_iota(jnp.int32, (tile_count, 1, 1), 0)
    partial_sum = jnp.sum(jnp.where(block_match, grad_col[None], 0.0), axis=(1, 2))
    owners = lax.axis_size("gy")
    chunk = tile_count // owners
    gathered = lax.all_gather(partial_sum.reshape(owners, chunk), "gy")
    mine = lax.dynamic_index_in_dim(gathered, lax.axis_index("gy"), axis=1, keepdims=False)
    grad_tiles = jnp.sum(mine, axis=0)[None]
    return (velocity, adjoint, grad_tiles)


def solution(mesh):
    in_specs = (
        P(None, None, "gx", "gy"),
        P(None, "gx", "gy"),
        P(None, "gx", "gy"),
        P("gx", "gy"),
        P("gx", "gy"),
        P("gx", "gy"),
    )
    out_specs = (P(None, None, "gx", "gy"), P(None, None, "gx", "gy"), P("gx", "gy"))
    return jax.shard_map(local, mesh=mesh, in_specs=in_specs, out_specs=out_specs, check_vma=False)
```

```python
import jax
import jax.numpy as jnp
from jax import lax
from jax.sharding import PartitionSpec as P

PASSES = 4


OMEGA = 0.8
VERTICAL = 16.0
HALO = 2 * PASSES - 1


def with_halo(cells, sides, width):
    for axis, dim in sides:
        count = lax.axis_size(axis)
        ends = count - 1
        head = lax.slice_in_dim(cells, 0, width, axis=dim)
        tail = lax.slice_in_dim(cells, cells.shape[dim] - width, cells.shape[dim], axis=dim)
        cells = jnp.concatenate(
            [
                lax.ppermute(tail, axis, [(i, (i + 1) % count) for i in range(ends)]),
                cells,
                lax.ppermute(head, axis, [((i + 1) % count, i) for i in range(ends)]),
            ],
            axis=dim,
        )
    return cells


def lateral_terms(visc_pad):
    centre_visc = visc_pad[:, 1:-1, 1:-1]
    west_face = 0.5 * (centre_visc + visc_pad[:, :-2, 1:-1])
    east_face = 0.5 * (centre_visc + visc_pad[:, 2:, 1:-1])
    south_face = 0.5 * (centre_visc + visc_pad[:, 1:-1, :-2])
    north_face = 0.5 * (centre_visc + visc_pad[:, 1:-1, 2:])
    return (west_face, east_face, south_face, north_face)


def weights_xy():
    along_x = jnp.array([4.0, 1.0], jnp.float32).reshape(2, 1, 1, 1)
    along_y = jnp.array([1.0, 4.0], jnp.float32).reshape(2, 1, 1, 1)
    return (along_x, along_y)


def prepare(visc_pad, beta_col, ice_cover):
    faces = lateral_terms(visc_pad)
    west_face, east_face, south_face, north_face = faces
    along_x, along_y = weights_xy()
    centre_visc = visc_pad[:, 1:-1, 1:-1]
    vertical = VERTICAL * 0.5 * (centre_visc[:-1] + centre_visc[1:])
    zero_row = jnp.zeros_like(centre_visc[:1])
    upper_link = jnp.concatenate([vertical, zero_row], 0)
    lower_link = jnp.concatenate([zero_row, vertical], 0)
    basal = jnp.concatenate([jnp.zeros_like(centre_visc[:-1]), beta_col[None]], 0)
    diagonal = along_x * (west_face + east_face) + along_y * (south_face + north_face)
    diagonal = diagonal + upper_link + lower_link + basal + (1.0 - ice_cover)
    layer_count = visc_pad.shape[0]
    ratio_list = []
    inverse_list = []
    for layer_idx in range(layer_count):
        pivot = diagonal[:, layer_idx]
        if layer_idx > 0:
            pivot = pivot + lower_link[layer_idx] * ratio_list[-1]
        inverse = 1.0 / pivot
        inverse_list.append(inverse)
        ratio_list.append(-upper_link[layer_idx] * inverse)
    return (faces, lower_link, jnp.stack(ratio_list, 1), jnp.stack(inverse_list, 1))


def relax(vel_pad, rhs_field, faces, lower_link, ratios, inverses, ice_cover):
    west_face, east_face, south_face, north_face = faces
    along_x, along_y = weights_xy()
    lateral = along_x * (west_face * vel_pad[:, :, :-2, 1:-1] + east_face * vel_pad[:, :, 2:, 1:-1])
    lateral = lateral + along_y * (
        south_face * vel_pad[:, :, 1:-1, :-2] + north_face * vel_pad[:, :, 1:-1, 2:]
    )
    right_side = rhs_field + lateral
    layer_count = right_side.shape[1]
    forward_list = []
    for layer_idx in range(layer_count):
        value = right_side[:, layer_idx]
        if layer_idx > 0:
            value = value + lower_link[layer_idx] * forward_list[-1]
        forward_list.append(value * inverses[:, layer_idx])
    solved = [None] * layer_count
    solved[layer_count - 1] = forward_list[layer_count - 1]
    for layer_idx in range(layer_count - 2, -1, -1):
        solved[layer_idx] = forward_list[layer_idx] - ratios[:, layer_idx] * solved[layer_idx + 1]
    line_value = jnp.stack(solved, 1)
    centre = vel_pad[:, :, 1:-1, 1:-1]
    return ice_cover * ((1.0 - OMEGA) * centre + OMEGA * line_value)


def lane_weights(comps, width):
    along_x = jnp.concatenate([jnp.full((width,), (4.0, 1.0)[c], jnp.float32) for c in range(comps)])
    along_y = jnp.concatenate([jnp.full((width,), (1.0, 4.0)[c], jnp.float32) for c in range(comps)])
    return (along_x, along_y)


def prepare_lanes(visc_pad, beta_col, ice_cover, weights):
    faces = lateral_terms(visc_pad)
    west_face, east_face, south_face, north_face = faces
    along_x, along_y = weights
    centre_visc = visc_pad[:, 1:-1, 1:-1]
    vertical = VERTICAL * 0.5 * (centre_visc[:-1] + centre_visc[1:])
    zero_row = jnp.zeros_like(centre_visc[:1])
    upper_link = jnp.concatenate([vertical, zero_row], 0)
    lower_link = jnp.concatenate([zero_row, vertical], 0)
    basal = jnp.concatenate([jnp.zeros_like(centre_visc[:-1]), beta_col[None]], 0)
    diagonal = along_x * (west_face + east_face) + along_y * (south_face + north_face)
    diagonal = diagonal + upper_link + lower_link + basal + (1.0 - ice_cover)
    layer_count = visc_pad.shape[0]
    ratio_list = []
    inverse_list = []
    for layer_idx in range(layer_count):
        pivot = diagonal[layer_idx]
        if layer_idx > 0:
            pivot = pivot + lower_link[layer_idx] * ratio_list[-1]
        inverse = 1.0 / pivot
        inverse_list.append(inverse)
        ratio_list.append(-upper_link[layer_idx] * inverse)
    return (faces, lower_link, ratio_list, inverse_list)


def relax_lanes(vel_pad, rhs_field, faces, lower_link, ratios, inverses, ice_cover, weights):
    west_face, east_face, south_face, north_face = faces
    along_x, along_y = weights
    lateral = along_x * (west_face * vel_pad[:, :-2, 1:-1] + east_face * vel_pad[:, 2:, 1:-1])
    lateral = lateral + along_y * (
        south_face * vel_pad[:, 1:-1, :-2] + north_face * vel_pad[:, 1:-1, 2:]
    )
    right_side = rhs_field + lateral
    layer_count = right_side.shape[0]
    forward_list = []
    for layer_idx in range(layer_count):
        value = right_side[layer_idx]
        if layer_idx > 0:
            value = value + lower_link[layer_idx] * forward_list[-1]
        forward_list.append(value * inverses[layer_idx])
    solved = [None] * layer_count
    solved[layer_count - 1] = forward_list[layer_count - 1]
    for layer_idx in range(layer_count - 2, -1, -1):
        solved[layer_idx] = forward_list[layer_idx] - ratios[layer_idx] * solved[layer_idx + 1]
    line_value = jnp.stack(solved, 0)
    centre = vel_pad[:, 1:-1, 1:-1]
    return ice_cover * ((1.0 - OMEGA) * centre + OMEGA * line_value)


def pad_cells(field):
    return jnp.pad(field, [(0, 0)] * (field.ndim - 2) + [(1, 1), (1, 1)])


def shifted(piece, axis, down):
    count = lax.axis_size(axis)
    if down:
        pairs = [(i, i + 1) for i in range(count - 1)]
    else:
        pairs = [(i + 1, i) for i in range(count - 1)]
    return lax.ppermute(piece, axis, pairs)


def gather_by_doubling(piece, axis):
    count = lax.axis_size(axis)
    if count & (count - 1):
        return lax.all_gather(piece, axis).reshape(-1)
    slots = lax.broadcasted_iota(jnp.int32, (count, 1), 0)
    gathered = jnp.where(slots == lax.axis_index(axis), piece[None, :], 0.0)
    step = 1
    while step < count:
        gathered = gathered + lax.ppermute(gathered, axis, [(i, i ^ step) for i in range(count)])
        step *= 2
    return gathered.reshape(-1)


def local(forcing, viscosity, observed, beta_tiles, ice_mask, tile_owner):
    comps, layers, rows, cols = forcing.shape
    tiles_here = beta_tiles.shape[1]
    planes = [
        forcing.reshape(comps * layers, rows, cols),
        viscosity,
        observed,
        ice_mask.astype(jnp.float32)[None],
        tile_owner.astype(jnp.float32)[None],
    ]
    plane_count = sum(p.shape[0] for p in planes)

    head = jnp.concatenate([p[:, :HALO] for p in planes], axis=0)
    tail = jnp.concatenate([p[:, rows - HALO:] for p in planes], axis=0)
    from_above = shifted(tail, "gx", True)
    from_below = shifted(head, "gx", False)

    def stack_rows(lo, hi):
        return jnp.concatenate(
            [from_above[:plane_count, :, lo:hi]]
            + [jnp.concatenate([p[:, :, lo:hi] for p in planes], axis=0)]
            + [from_below[:plane_count, :, lo:hi]],
            axis=1,
        )

    from_left = shifted(stack_rows(cols - HALO, cols), "gy", True)
    from_right = shifted(stack_rows(0, HALO), "gy", False)

    own_row = gather_by_doubling(beta_tiles[0], "gy")
    friction_rows = jnp.stack([shifted(own_row, "gx", True), own_row, shifted(own_row, "gx", False)])
    tile_count = friction_rows.shape[1]

    packed = jnp.concatenate([from_left, stack_rows(0, cols), from_right], axis=2)
    ext_rows, ext_cols = packed.shape[1], packed.shape[2]
    at = 0
    forcing_ext = packed[at:at + comps * layers].reshape(comps, layers, ext_rows, ext_cols)
    at += comps * layers
    visc_ext = packed[at:at + layers]
    at += layers
    observed_ext = packed[at:at + comps]
    at += comps
    ice_cover = packed[at]
    owner_ext = packed[at + 1].astype(jnp.int32)

    strip_table = friction_rows.T
    high = lax.reduce_precision(strip_table, exponent_bits=8, mantissa_bits=7)
    rest = strip_table - high
    middle = lax.reduce_precision(rest, exponent_bits=8, mantissa_bits=7)
    low = rest - middle
    parts = jnp.concatenate([high, middle, low], axis=1).astype(jnp.bfloat16)
    tiles = lax.broadcasted_iota(jnp.int32, (1, 1, tile_count), 2)
    one_hot = (owner_ext[:, :, None] == tiles).astype(jnp.bfloat16)
    looked_up = lax.dot_general(
        one_hot, parts, (((2,), (0,)), ((), ())), preferred_element_type=jnp.float32
    )
    band = lax.broadcasted_iota(jnp.int32, (ext_rows, 1), 0)
    strip_of_row = jnp.where(band < HALO, 0, jnp.where(band < HALO + rows, 1, 2))
    near = friction_rows.shape[0]
    beta_col = sum(
        jnp.where(strip_of_row == k, looked_up[:, :, k] + looked_up[:, :, near + k] + looked_up[:, :, 2 * near + k], 0.0)
        for k in range(near)
    )

    def side_by_side(per_comp):
        return jnp.concatenate([per_comp[c] for c in range(comps)], axis=-1)

    weights = lane_weights(comps, ext_cols)
    visc_lanes = side_by_side([visc_ext] * comps)
    ice_lanes = side_by_side([ice_cover] * comps)
    beta_lanes = side_by_side([beta_col] * comps)
    forcing_lanes = side_by_side([forcing_ext[c] for c in range(comps)])
    observed_lanes = side_by_side([observed_ext[c] for c in range(comps)])
    faces, lower_link, ratios, inverses = prepare_lanes(
        pad_cells(visc_lanes), beta_lanes, ice_lanes, weights
    )

    def advance(field, rhs_field):
        return relax_lanes(pad_cells(field), rhs_field, faces, lower_link, ratios, inverses, ice_lanes, weights)

    velocity = jnp.zeros_like(forcing_lanes)
    for sweep_idx in range(PASSES):
        velocity = advance(velocity, forcing_lanes)
    misfit = velocity[0] - observed_lanes
    adjoint_rhs = jnp.zeros_like(forcing_lanes).at[0].set(misfit)
    adjoint = jnp.zeros_like(forcing_lanes)
    for sweep_idx in range(PASSES):
        adjoint = advance(adjoint, adjoint_rhs)

    inner = (slice(HALO, HALO + rows), slice(HALO, HALO + cols))

    def split(field):
        return jnp.stack(
            [field[:, inner[0], c * ext_cols + HALO:c * ext_cols + HALO + cols] for c in range(comps)]
        )

    velocity = split(velocity)
    adjoint = split(adjoint)
    grad_col = -ice_cover[inner] * beta_col[inner] * jnp.sum(adjoint[:, -1] * velocity[:, -1], axis=0)
    block_match = tile_owner[None] == lax.broadcasted_iota(jnp.int32, (tile_count, 1, 1), 0)
    partial_sum = jnp.sum(jnp.where(block_match, grad_col[None], 0.0), axis=(1, 2))
    owners = lax.axis_size("gy")
    chunk = tile_count // owners
    gathered = lax.all_gather(partial_sum.reshape(owners, chunk), "gy")
    mine = lax.dynamic_index_in_dim(gathered, lax.axis_index("gy"), axis=1, keepdims=False)
    grad_tiles = jnp.sum(mine, axis=0)[None]
    return (velocity, adjoint, grad_tiles)


def solution(mesh):
    in_specs = (
        P(None, None, "gx", "gy"),
        P(None, "gx", "gy"),
        P(None, "gx", "gy"),
        P("gx", "gy"),
        P("gx", "gy"),
        P("gx", "gy"),
    )
    out_specs = (P(None, None, "gx", "gy"), P(None, None, "gx", "gy"), P("gx", "gy"))
    return jax.shard_map(local, mesh=mesh, in_specs=in_specs, out_specs=out_specs, check_vma=False)
```

```python
import jax
import jax.numpy as jnp
from jax import lax
from jax.sharding import PartitionSpec as P

PASSES = 4


OMEGA = 0.8
VERTICAL = 16.0
HALO = 2 * PASSES - 1


def with_halo(cells, sides, width):
    for axis, dim in sides:
        count = lax.axis_size(axis)
        ends = count - 1
        head = lax.slice_in_dim(cells, 0, width, axis=dim)
        tail = lax.slice_in_dim(cells, cells.shape[dim] - width, cells.shape[dim], axis=dim)
        cells = jnp.concatenate(
            [
                lax.ppermute(tail, axis, [(i, (i + 1) % count) for i in range(ends)]),
                cells,
                lax.ppermute(head, axis, [((i + 1) % count, i) for i in range(ends)]),
            ],
            axis=dim,
        )
    return cells


def lateral_terms(visc_pad):
    centre_visc = visc_pad[:, 1:-1, 1:-1]
    west_face = 0.5 * (centre_visc + visc_pad[:, :-2, 1:-1])
    east_face = 0.5 * (centre_visc + visc_pad[:, 2:, 1:-1])
    south_face = 0.5 * (centre_visc + visc_pad[:, 1:-1, :-2])
    north_face = 0.5 * (centre_visc + visc_pad[:, 1:-1, 2:])
    return (west_face, east_face, south_face, north_face)


def weights_xy():
    along_x = jnp.array([4.0, 1.0], jnp.float32).reshape(2, 1, 1, 1)
    along_y = jnp.array([1.0, 4.0], jnp.float32).reshape(2, 1, 1, 1)
    return (along_x, along_y)


def prepare(visc_pad, beta_col, ice_cover):
    faces = lateral_terms(visc_pad)
    west_face, east_face, south_face, north_face = faces
    along_x, along_y = weights_xy()
    centre_visc = visc_pad[:, 1:-1, 1:-1]
    vertical = VERTICAL * 0.5 * (centre_visc[:-1] + centre_visc[1:])
    zero_row = jnp.zeros_like(centre_visc[:1])
    upper_link = jnp.concatenate([vertical, zero_row], 0)
    lower_link = jnp.concatenate([zero_row, vertical], 0)
    basal = jnp.concatenate([jnp.zeros_like(centre_visc[:-1]), beta_col[None]], 0)
    diagonal = along_x * (west_face + east_face) + along_y * (south_face + north_face)
    diagonal = diagonal + upper_link + lower_link + basal + (1.0 - ice_cover)
    layer_count = visc_pad.shape[0]
    ratio_list = []
    inverse_list = []
    for layer_idx in range(layer_count):
        pivot = diagonal[:, layer_idx]
        if layer_idx > 0:
            pivot = pivot + lower_link[layer_idx] * ratio_list[-1]
        inverse = 1.0 / pivot
        inverse_list.append(inverse)
        ratio_list.append(-upper_link[layer_idx] * inverse)
    return (faces, lower_link, jnp.stack(ratio_list, 1), jnp.stack(inverse_list, 1))


def relax(vel_pad, rhs_field, faces, lower_link, ratios, inverses, ice_cover):
    west_face, east_face, south_face, north_face = faces
    along_x, along_y = weights_xy()
    lateral = along_x * (west_face * vel_pad[:, :, :-2, 1:-1] + east_face * vel_pad[:, :, 2:, 1:-1])
    lateral = lateral + along_y * (
        south_face * vel_pad[:, :, 1:-1, :-2] + north_face * vel_pad[:, :, 1:-1, 2:]
    )
    right_side = rhs_field + lateral
    layer_count = right_side.shape[1]
    forward_list = []
    for layer_idx in range(layer_count):
        value = right_side[:, layer_idx]
        if layer_idx > 0:
            value = value + lower_link[layer_idx] * forward_list[-1]
        forward_list.append(value * inverses[:, layer_idx])
    solved = [None] * layer_count
    solved[layer_count - 1] = forward_list[layer_count - 1]
    for layer_idx in range(layer_count - 2, -1, -1):
        solved[layer_idx] = forward_list[layer_idx] - ratios[:, layer_idx] * solved[layer_idx + 1]
    line_value = jnp.stack(solved, 1)
    centre = vel_pad[:, :, 1:-1, 1:-1]
    return ice_cover * ((1.0 - OMEGA) * centre + OMEGA * line_value)


def lane_weights(comps, width):
    along_x = jnp.concatenate([jnp.full((width,), (4.0, 1.0)[c], jnp.float32) for c in range(comps)])
    along_y = jnp.concatenate([jnp.full((width,), (1.0, 4.0)[c], jnp.float32) for c in range(comps)])
    return (along_x, along_y)


def prepare_lanes(visc_pad, beta_col, ice_cover, weights):
    faces = lateral_terms(visc_pad)
    west_face, east_face, south_face, north_face = faces
    along_x, along_y = weights
    centre_visc = visc_pad[:, 1:-1, 1:-1]
    vertical = VERTICAL * 0.5 * (centre_visc[:-1] + centre_visc[1:])
    zero_row = jnp.zeros_like(centre_visc[:1])
    upper_link = jnp.concatenate([vertical, zero_row], 0)
    lower_link = jnp.concatenate([zero_row, vertical], 0)
    basal = jnp.concatenate([jnp.zeros_like(centre_visc[:-1]), beta_col[None]], 0)
    diagonal = along_x * (west_face + east_face) + along_y * (south_face + north_face)
    diagonal = diagonal + upper_link + lower_link + basal + (1.0 - ice_cover)
    layer_count = visc_pad.shape[0]
    ratio_list = []
    inverse_list = []
    for layer_idx in range(layer_count):
        pivot = diagonal[layer_idx]
        if layer_idx > 0:
            pivot = pivot + lower_link[layer_idx] * ratio_list[-1]
        inverse = 1.0 / pivot
        inverse_list.append(inverse)
        ratio_list.append(-upper_link[layer_idx] * inverse)
    return (faces, lower_link, ratio_list, inverse_list)


def relax_lanes(vel_pad, rhs_field, faces, lower_link, ratios, inverses, ice_cover, weights):
    west_face, east_face, south_face, north_face = faces
    along_x, along_y = weights
    lateral = along_x * (west_face * vel_pad[:, :-2, 1:-1] + east_face * vel_pad[:, 2:, 1:-1])
    lateral = lateral + along_y * (
        south_face * vel_pad[:, 1:-1, :-2] + north_face * vel_pad[:, 1:-1, 2:]
    )
    right_side = rhs_field + lateral
    layer_count = right_side.shape[0]
    forward_list = []
    for layer_idx in range(layer_count):
        value = right_side[layer_idx]
        if layer_idx > 0:
            value = value + lower_link[layer_idx] * forward_list[-1]
        forward_list.append(value * inverses[layer_idx])
    solved = [None] * layer_count
    solved[layer_count - 1] = forward_list[layer_count - 1]
    for layer_idx in range(layer_count - 2, -1, -1):
        solved[layer_idx] = forward_list[layer_idx] - ratios[layer_idx] * solved[layer_idx + 1]
    line_value = jnp.stack(solved, 0)
    centre = vel_pad[:, 1:-1, 1:-1]
    return ice_cover * ((1.0 - OMEGA) * centre + OMEGA * line_value)


def pad_cells(field):
    return jnp.pad(field, [(0, 0)] * (field.ndim - 2) + [(1, 1), (1, 1)])


def shifted(piece, axis, down):
    count = lax.axis_size(axis)
    if down:
        pairs = [(i, i + 1) for i in range(count - 1)]
    else:
        pairs = [(i + 1, i) for i in range(count - 1)]
    return lax.ppermute(piece, axis, pairs)


def local(forcing, viscosity, observed, beta_tiles, ice_mask, tile_owner):
    comps, layers, rows, cols = forcing.shape
    tiles_here = beta_tiles.shape[1]
    planes = [
        forcing.reshape(comps * layers, rows, cols),
        viscosity,
        observed,
        ice_mask.astype(jnp.float32)[None],
        tile_owner.astype(jnp.float32)[None],
    ]
    plane_count = sum(p.shape[0] for p in planes)

    beta_plane = jnp.pad(beta_tiles, ((0, HALO - 1), (0, cols - tiles_here)))[None]
    head = jnp.concatenate([p[:, :HALO] for p in planes] + [beta_plane], axis=0)
    tail = jnp.concatenate([p[:, rows - HALO:] for p in planes] + [beta_plane], axis=0)
    from_above = shifted(tail, "gx", True)
    from_below = shifted(head, "gx", False)

    def stack_rows(lo, hi):
        return jnp.concatenate(
            [from_above[:plane_count, :, lo:hi]]
            + [jnp.concatenate([p[:, :, lo:hi] for p in planes], axis=0)]
            + [from_below[:plane_count, :, lo:hi]],
            axis=1,
        )

    from_left = shifted(stack_rows(cols - HALO, cols), "gy", True)
    from_right = shifted(stack_rows(0, HALO), "gy", False)

    strips_near = jnp.stack(
        [from_above[plane_count, 0, :tiles_here], beta_tiles[0], from_below[plane_count, 0, :tiles_here]]
    )
    friction_rows = lax.all_gather(strips_near, "gy", axis=1, tiled=True)
    tile_count = friction_rows.shape[1]

    own_planes = jnp.concatenate(planes, axis=0)
    ext_rows, ext_cols = rows + 2 * HALO, cols + 2 * HALO

    def extended(lo, hi):
        middle = jnp.concatenate([from_above[lo:hi], own_planes[lo:hi], from_below[lo:hi]], axis=1)
        return jnp.concatenate([from_left[lo:hi], middle, from_right[lo:hi]], axis=2)

    at = 0
    forcing_ext = extended(at, at + comps * layers).reshape(comps, layers, ext_rows, ext_cols)
    at += comps * layers
    visc_ext = extended(at, at + layers)
    at += layers
    observed_ext = extended(at, at + comps)
    at += comps
    ice_cover = extended(at, at + 1)[0]
    owner_ext = extended(at + 1, at + 2)[0].astype(jnp.int32)

    strip_table = friction_rows.T
    high = lax.reduce_precision(strip_table, exponent_bits=8, mantissa_bits=7)
    rest = strip_table - high
    middle = lax.reduce_precision(rest, exponent_bits=8, mantissa_bits=7)
    low = rest - middle
    parts = jnp.concatenate([high, middle, low], axis=1).astype(jnp.bfloat16)
    tiles = lax.broadcasted_iota(jnp.int32, (1, 1, tile_count), 2)
    one_hot = (owner_ext[:, :, None] == tiles).astype(jnp.bfloat16)
    looked_up = lax.dot_general(
        one_hot, parts, (((2,), (0,)), ((), ())), preferred_element_type=jnp.float32
    )
    band = lax.broadcasted_iota(jnp.int32, (ext_rows, 1), 0)
    strip_of_row = jnp.where(band < HALO, 0, jnp.where(band < HALO + rows, 1, 2))
    near = friction_rows.shape[0]
    beta_col = sum(
        jnp.where(strip_of_row == k, looked_up[:, :, k] + looked_up[:, :, near + k] + looked_up[:, :, 2 * near + k], 0.0)
        for k in range(near)
    )

    def side_by_side(per_comp):
        return jnp.concatenate([per_comp[c] for c in range(comps)], axis=-1)

    weights = lane_weights(comps, ext_cols)
    visc_lanes = side_by_side([visc_ext] * comps)
    ice_lanes = side_by_side([ice_cover] * comps)
    beta_lanes = side_by_side([beta_col] * comps)
    forcing_lanes = side_by_side([forcing_ext[c] for c in range(comps)])
    observed_lanes = side_by_side([observed_ext[c] for c in range(comps)])
    faces, lower_link, ratios, inverses = prepare_lanes(
        pad_cells(visc_lanes), beta_lanes, ice_lanes, weights
    )

    def advance(field, rhs_field):
        return relax_lanes(pad_cells(field), rhs_field, faces, lower_link, ratios, inverses, ice_lanes, weights)

    velocity = jnp.zeros_like(forcing_lanes)
    for sweep_idx in range(PASSES):
        velocity = advance(velocity, forcing_lanes)
    misfit = velocity[0] - observed_lanes
    adjoint_rhs = jnp.zeros_like(forcing_lanes).at[0].set(misfit)
    adjoint = jnp.zeros_like(forcing_lanes)
    for sweep_idx in range(PASSES):
        adjoint = advance(adjoint, adjoint_rhs)

    inner = (slice(HALO, HALO + rows), slice(HALO, HALO + cols))

    def split(field):
        return jnp.stack(
            [field[:, inner[0], c * ext_cols + HALO:c * ext_cols + HALO + cols] for c in range(comps)]
        )

    velocity = split(velocity)
    adjoint = split(adjoint)
    grad_col = -ice_cover[inner] * beta_col[inner] * jnp.sum(adjoint[:, -1] * velocity[:, -1], axis=0)
    block_match = tile_owner[None] == lax.broadcasted_iota(jnp.int32, (tile_count, 1, 1), 0)
    partial_sum = jnp.sum(jnp.where(block_match, grad_col[None], 0.0), axis=(1, 2))
    owners = lax.axis_size("gy")
    chunk = tile_count // owners
    gathered = lax.all_gather(partial_sum.reshape(owners, chunk), "gy")
    mine = lax.dynamic_index_in_dim(gathered, lax.axis_index("gy"), axis=1, keepdims=False)
    grad_tiles = jnp.sum(mine, axis=0)[None]
    return (velocity, adjoint, grad_tiles)


def solution(mesh):
    in_specs = (
        P(None, None, "gx", "gy"),
        P(None, "gx", "gy"),
        P(None, "gx", "gy"),
        P("gx", "gy"),
        P("gx", "gy"),
        P("gx", "gy"),
    )
    out_specs = (P(None, None, "gx", "gy"), P(None, None, "gx", "gy"), P("gx", "gy"))
    return jax.shard_map(local, mesh=mesh, in_specs=in_specs, out_specs=out_specs, check_vma=False)
```

```python
import jax
import jax.numpy as jnp
from jax import lax
from jax.sharding import PartitionSpec as P

PASSES = 4


OMEGA = 0.8
VERTICAL = 16.0
HALO = 2 * PASSES - 1


def with_halo(cells, sides, width):
    for axis, dim in sides:
        count = lax.axis_size(axis)
        ends = count - 1
        head = lax.slice_in_dim(cells, 0, width, axis=dim)
        tail = lax.slice_in_dim(cells, cells.shape[dim] - width, cells.shape[dim], axis=dim)
        cells = jnp.concatenate(
            [
                lax.ppermute(tail, axis, [(i, (i + 1) % count) for i in range(ends)]),
                cells,
                lax.ppermute(head, axis, [((i + 1) % count, i) for i in range(ends)]),
            ],
            axis=dim,
        )
    return cells


def lateral_terms(visc_pad):
    centre_visc = visc_pad[:, 1:-1, 1:-1]
    west_face = 0.5 * (centre_visc + visc_pad[:, :-2, 1:-1])
    east_face = 0.5 * (centre_visc + visc_pad[:, 2:, 1:-1])
    south_face = 0.5 * (centre_visc + visc_pad[:, 1:-1, :-2])
    north_face = 0.5 * (centre_visc + visc_pad[:, 1:-1, 2:])
    return (west_face, east_face, south_face, north_face)


def weights_xy():
    along_x = jnp.array([4.0, 1.0], jnp.float32).reshape(2, 1, 1, 1)
    along_y = jnp.array([1.0, 4.0], jnp.float32).reshape(2, 1, 1, 1)
    return (along_x, along_y)


def prepare(visc_pad, beta_col, ice_cover):
    faces = lateral_terms(visc_pad)
    west_face, east_face, south_face, north_face = faces
    along_x, along_y = weights_xy()
    centre_visc = visc_pad[:, 1:-1, 1:-1]
    vertical = VERTICAL * 0.5 * (centre_visc[:-1] + centre_visc[1:])
    zero_row = jnp.zeros_like(centre_visc[:1])
    upper_link = jnp.concatenate([vertical, zero_row], 0)
    lower_link = jnp.concatenate([zero_row, vertical], 0)
    basal = jnp.concatenate([jnp.zeros_like(centre_visc[:-1]), beta_col[None]], 0)
    diagonal = along_x * (west_face + east_face) + along_y * (south_face + north_face)
    diagonal = diagonal + upper_link + lower_link + basal + (1.0 - ice_cover)
    layer_count = visc_pad.shape[0]
    ratio_list = []
    inverse_list = []
    for layer_idx in range(layer_count):
        pivot = diagonal[:, layer_idx]
        if layer_idx > 0:
            pivot = pivot + lower_link[layer_idx] * ratio_list[-1]
        inverse = 1.0 / pivot
        inverse_list.append(inverse)
        ratio_list.append(-upper_link[layer_idx] * inverse)
    return (faces, lower_link, jnp.stack(ratio_list, 1), jnp.stack(inverse_list, 1))


def relax(vel_pad, rhs_field, faces, lower_link, ratios, inverses, ice_cover):
    west_face, east_face, south_face, north_face = faces
    along_x, along_y = weights_xy()
    lateral = along_x * (west_face * vel_pad[:, :, :-2, 1:-1] + east_face * vel_pad[:, :, 2:, 1:-1])
    lateral = lateral + along_y * (
        south_face * vel_pad[:, :, 1:-1, :-2] + north_face * vel_pad[:, :, 1:-1, 2:]
    )
    right_side = rhs_field + lateral
    layer_count = right_side.shape[1]
    forward_list = []
    for layer_idx in range(layer_count):
        value = right_side[:, layer_idx]
        if layer_idx > 0:
            value = value + lower_link[layer_idx] * forward_list[-1]
        forward_list.append(value * inverses[:, layer_idx])
    solved = [None] * layer_count
    solved[layer_count - 1] = forward_list[layer_count - 1]
    for layer_idx in range(layer_count - 2, -1, -1):
        solved[layer_idx] = forward_list[layer_idx] - ratios[:, layer_idx] * solved[layer_idx + 1]
    line_value = jnp.stack(solved, 1)
    centre = vel_pad[:, :, 1:-1, 1:-1]
    return ice_cover * ((1.0 - OMEGA) * centre + OMEGA * line_value)


def lane_weights(comps, width):
    along_x = jnp.concatenate([jnp.full((width,), (4.0, 1.0)[c], jnp.float32) for c in range(comps)])
    along_y = jnp.concatenate([jnp.full((width,), (1.0, 4.0)[c], jnp.float32) for c in range(comps)])
    return (along_x, along_y)


def prepare_lanes(visc_pad, beta_col, ice_cover, weights):
    faces = lateral_terms(visc_pad)
    west_face, east_face, south_face, north_face = faces
    along_x, along_y = weights
    centre_visc = visc_pad[:, 1:-1, 1:-1]
    vertical = VERTICAL * 0.5 * (centre_visc[:-1] + centre_visc[1:])
    zero_row = jnp.zeros_like(centre_visc[:1])
    upper_link = jnp.concatenate([vertical, zero_row], 0)
    lower_link = jnp.concatenate([zero_row, vertical], 0)
    basal = jnp.concatenate([jnp.zeros_like(centre_visc[:-1]), beta_col[None]], 0)
    diagonal = along_x * (west_face + east_face) + along_y * (south_face + north_face)
    diagonal = diagonal + upper_link + lower_link + basal + (1.0 - ice_cover)
    layer_count = visc_pad.shape[0]
    ratio_list = []
    inverse_list = []
    for layer_idx in range(layer_count):
        pivot = diagonal[layer_idx]
        if layer_idx > 0:
            pivot = pivot + lower_link[layer_idx] * ratio_list[-1]
        inverse = 1.0 / pivot
        inverse_list.append(inverse)
        ratio_list.append(-upper_link[layer_idx] * inverse)
    return (faces, lower_link, ratio_list, inverse_list)


def relax_lanes(vel_pad, rhs_field, faces, lower_link, ratios, inverses, ice_cover, weights):
    west_face, east_face, south_face, north_face = faces
    along_x, along_y = weights
    lateral = along_x * (west_face * vel_pad[:, :-2, 1:-1] + east_face * vel_pad[:, 2:, 1:-1])
    lateral = lateral + along_y * (
        south_face * vel_pad[:, 1:-1, :-2] + north_face * vel_pad[:, 1:-1, 2:]
    )
    right_side = rhs_field + lateral
    layer_count = right_side.shape[0]
    forward_list = []
    for layer_idx in range(layer_count):
        value = right_side[layer_idx]
        if layer_idx > 0:
            value = value + lower_link[layer_idx] * forward_list[-1]
        forward_list.append(value * inverses[layer_idx])
    solved = [None] * layer_count
    solved[layer_count - 1] = forward_list[layer_count - 1]
    for layer_idx in range(layer_count - 2, -1, -1):
        solved[layer_idx] = forward_list[layer_idx] - ratios[layer_idx] * solved[layer_idx + 1]
    line_value = jnp.stack(solved, 0)
    centre = vel_pad[:, 1:-1, 1:-1]
    return ice_cover * ((1.0 - OMEGA) * centre + OMEGA * line_value)


def pad_cells(field):
    return jnp.pad(field, [(0, 0)] * (field.ndim - 2) + [(1, 1), (1, 1)])


def shifted(piece, axis, down):
    count = lax.axis_size(axis)
    if down:
        pairs = [(i, i + 1) for i in range(count - 1)]
    else:
        pairs = [(i + 1, i) for i in range(count - 1)]
    return lax.ppermute(piece, axis, pairs)


def local(forcing, viscosity, observed, beta_tiles, ice_mask, tile_owner):
    comps, layers, rows, cols = forcing.shape
    tiles_here = beta_tiles.shape[1]
    planes = [
        forcing.reshape(comps * layers, rows, cols),
        viscosity,
        observed,
        ice_mask.astype(jnp.float32)[None],
        tile_owner.astype(jnp.float32)[None],
    ]
    plane_count = sum(p.shape[0] for p in planes)

    beta_plane = jnp.pad(beta_tiles, ((0, HALO - 1), (0, cols - tiles_here)))[None]
    head = jnp.concatenate([p[:, :HALO] for p in planes] + [beta_plane], axis=0)
    tail = jnp.concatenate([p[:, rows - HALO:] for p in planes] + [beta_plane], axis=0)
    from_above = shifted(tail, "gx", True)
    from_below = shifted(head, "gx", False)

    def stack_rows(lo, hi):
        return jnp.concatenate(
            [from_above[:plane_count, :, lo:hi]]
            + [jnp.concatenate([p[:, :, lo:hi] for p in planes], axis=0)]
            + [from_below[:plane_count, :, lo:hi]],
            axis=1,
        )

    from_left = shifted(stack_rows(cols - HALO, cols), "gy", True)
    from_right = shifted(stack_rows(0, HALO), "gy", False)

    strips_near = jnp.stack(
        [from_above[plane_count, 0, :tiles_here], beta_tiles[0], from_below[plane_count, 0, :tiles_here]]
    )
    friction_rows = lax.all_gather(strips_near, "gy", axis=1, tiled=True)
    tile_count = friction_rows.shape[1]

    packed = jnp.concatenate([from_left, stack_rows(0, cols), from_right], axis=2)
    ext_rows, ext_cols = packed.shape[1], packed.shape[2]
    at = 0
    forcing_ext = packed[at:at + comps * layers].reshape(comps, layers, ext_rows, ext_cols)
    at += comps * layers
    visc_ext = packed[at:at + layers]
    at += layers
    observed_ext = packed[at:at + comps]
    at += comps
    ice_cover = packed[at]
    owner_ext = packed[at + 1].astype(jnp.int32)

    tiles = lax.broadcasted_iota(jnp.int32, (tile_count, 1, 1), 0)
    owner_match = owner_ext[None] == tiles
    row_strip = jnp.concatenate(
        [
            jnp.broadcast_to(friction_rows[0][:, None], (tile_count, HALO)),
            jnp.broadcast_to(friction_rows[1][:, None], (tile_count, rows)),
            jnp.broadcast_to(friction_rows[2][:, None], (tile_count, HALO)),
        ],
        axis=1,
    )
    beta_col = jnp.sum(jnp.where(owner_match, row_strip[:, :, None], 0.0), axis=0)

    def side_by_side(per_comp):
        return jnp.concatenate([per_comp[c] for c in range(comps)], axis=-1)

    weights = lane_weights(comps, ext_cols)
    visc_lanes = side_by_side([visc_ext] * comps)
    ice_lanes = side_by_side([ice_cover] * comps)
    beta_lanes = side_by_side([beta_col] * comps)
    forcing_lanes = side_by_side([forcing_ext[c] for c in range(comps)])
    observed_lanes = side_by_side([observed_ext[c] for c in range(comps)])
    faces, lower_link, ratios, inverses = prepare_lanes(
        pad_cells(visc_lanes), beta_lanes, ice_lanes, weights
    )

    def advance(field, rhs_field):
        return relax_lanes(pad_cells(field), rhs_field, faces, lower_link, ratios, inverses, ice_lanes, weights)

    velocity = jnp.zeros_like(forcing_lanes)
    for sweep_idx in range(PASSES):
        velocity = advance(velocity, forcing_lanes)
    misfit = velocity[0] - observed_lanes
    adjoint_rhs = jnp.zeros_like(forcing_lanes).at[0].set(misfit)
    adjoint = jnp.zeros_like(forcing_lanes)
    for sweep_idx in range(PASSES):
        adjoint = advance(adjoint, adjoint_rhs)

    inner = (slice(HALO, HALO + rows), slice(HALO, HALO + cols))

    def split(field):
        return jnp.stack(
            [field[:, inner[0], c * ext_cols + HALO:c * ext_cols + HALO + cols] for c in range(comps)]
        )

    velocity = split(velocity)
    adjoint = split(adjoint)
    grad_col = -ice_cover[inner] * beta_col[inner] * jnp.sum(adjoint[:, -1] * velocity[:, -1], axis=0)
    block_match = tile_owner[None] == lax.broadcasted_iota(jnp.int32, (tile_count, 1, 1), 0)
    partial_sum = jnp.sum(jnp.where(block_match, grad_col[None], 0.0), axis=(1, 2))
    owners = lax.axis_size("gy")
    chunk = tile_count // owners
    gathered = lax.all_gather(partial_sum.reshape(owners, chunk), "gy")
    mine = lax.dynamic_index_in_dim(gathered, lax.axis_index("gy"), axis=1, keepdims=False)
    grad_tiles = jnp.sum(mine, axis=0)[None]
    return (velocity, adjoint, grad_tiles)


def solution(mesh):
    in_specs = (
        P(None, None, "gx", "gy"),
        P(None, "gx", "gy"),
        P(None, "gx", "gy"),
        P("gx", "gy"),
        P("gx", "gy"),
        P("gx", "gy"),
    )
    out_specs = (P(None, None, "gx", "gy"), P(None, None, "gx", "gy"), P("gx", "gy"))
    return jax.shard_map(local, mesh=mesh, in_specs=in_specs, out_specs=out_specs, check_vma=False)
```

```python
import jax
import jax.numpy as jnp
from jax import lax
from jax.sharding import PartitionSpec as P

PASSES = 4


OMEGA = 0.8
VERTICAL = 16.0
HALO = 2 * PASSES - 1


def with_halo(cells, sides, width):
    for axis, dim in sides:
        count = lax.axis_size(axis)
        ends = count - 1
        head = lax.slice_in_dim(cells, 0, width, axis=dim)
        tail = lax.slice_in_dim(cells, cells.shape[dim] - width, cells.shape[dim], axis=dim)
        cells = jnp.concatenate(
            [
                lax.ppermute(tail, axis, [(i, (i + 1) % count) for i in range(ends)]),
                cells,
                lax.ppermute(head, axis, [((i + 1) % count, i) for i in range(ends)]),
            ],
            axis=dim,
        )
    return cells


def lateral_terms(visc_pad):
    centre_visc = visc_pad[:, 1:-1, 1:-1]
    west_face = 0.5 * (centre_visc + visc_pad[:, :-2, 1:-1])
    east_face = 0.5 * (centre_visc + visc_pad[:, 2:, 1:-1])
    south_face = 0.5 * (centre_visc + visc_pad[:, 1:-1, :-2])
    north_face = 0.5 * (centre_visc + visc_pad[:, 1:-1, 2:])
    return (west_face, east_face, south_face, north_face)


def weights_xy():
    along_x = jnp.array([4.0, 1.0], jnp.float32).reshape(2, 1, 1, 1)
    along_y = jnp.array([1.0, 4.0], jnp.float32).reshape(2, 1, 1, 1)
    return (along_x, along_y)


def prepare(visc_pad, beta_col, ice_cover):
    faces = lateral_terms(visc_pad)
    west_face, east_face, south_face, north_face = faces
    along_x, along_y = weights_xy()
    centre_visc = visc_pad[:, 1:-1, 1:-1]
    vertical = VERTICAL * 0.5 * (centre_visc[:-1] + centre_visc[1:])
    zero_row = jnp.zeros_like(centre_visc[:1])
    upper_link = jnp.concatenate([vertical, zero_row], 0)
    lower_link = jnp.concatenate([zero_row, vertical], 0)
    basal = jnp.concatenate([jnp.zeros_like(centre_visc[:-1]), beta_col[None]], 0)
    diagonal = along_x * (west_face + east_face) + along_y * (south_face + north_face)
    diagonal = diagonal + upper_link + lower_link + basal + (1.0 - ice_cover)
    layer_count = visc_pad.shape[0]
    ratio_list = []
    inverse_list = []
    for layer_idx in range(layer_count):
        pivot = diagonal[:, layer_idx]
        if layer_idx > 0:
            pivot = pivot + lower_link[layer_idx] * ratio_list[-1]
        inverse = 1.0 / pivot
        inverse_list.append(inverse)
        ratio_list.append(-upper_link[layer_idx] * inverse)
    return (faces, lower_link, jnp.stack(ratio_list, 1), jnp.stack(inverse_list, 1))


def relax(vel_pad, rhs_field, faces, lower_link, ratios, inverses, ice_cover):
    west_face, east_face, south_face, north_face = faces
    along_x, along_y = weights_xy()
    lateral = along_x * (west_face * vel_pad[:, :, :-2, 1:-1] + east_face * vel_pad[:, :, 2:, 1:-1])
    lateral = lateral + along_y * (
        south_face * vel_pad[:, :, 1:-1, :-2] + north_face * vel_pad[:, :, 1:-1, 2:]
    )
    right_side = rhs_field + lateral
    layer_count = right_side.shape[1]
    forward_list = []
    for layer_idx in range(layer_count):
        value = right_side[:, layer_idx]
        if layer_idx > 0:
            value = value + lower_link[layer_idx] * forward_list[-1]
        forward_list.append(value * inverses[:, layer_idx])
    solved = [None] * layer_count
    solved[layer_count - 1] = forward_list[layer_count - 1]
    for layer_idx in range(layer_count - 2, -1, -1):
        solved[layer_idx] = forward_list[layer_idx] - ratios[:, layer_idx] * solved[layer_idx + 1]
    line_value = jnp.stack(solved, 1)
    centre = vel_pad[:, :, 1:-1, 1:-1]
    return ice_cover * ((1.0 - OMEGA) * centre + OMEGA * line_value)


def lane_weights(comps, width):
    along_x = jnp.concatenate([jnp.full((width,), (4.0, 1.0)[c], jnp.float32) for c in range(comps)])
    along_y = jnp.concatenate([jnp.full((width,), (1.0, 4.0)[c], jnp.float32) for c in range(comps)])
    return (along_x, along_y)


def prepare_lanes(visc_pad, beta_col, ice_cover, weights):
    faces = lateral_terms(visc_pad)
    west_face, east_face, south_face, north_face = faces
    along_x, along_y = weights
    centre_visc = visc_pad[:, 1:-1, 1:-1]
    vertical = VERTICAL * 0.5 * (centre_visc[:-1] + centre_visc[1:])
    zero_row = jnp.zeros_like(centre_visc[:1])
    upper_link = jnp.concatenate([vertical, zero_row], 0)
    lower_link = jnp.concatenate([zero_row, vertical], 0)
    basal = jnp.concatenate([jnp.zeros_like(centre_visc[:-1]), beta_col[None]], 0)
    diagonal = along_x * (west_face + east_face) + along_y * (south_face + north_face)
    diagonal = diagonal + upper_link + lower_link + basal + (1.0 - ice_cover)
    layer_count = visc_pad.shape[0]
    ratio_list = []
    inverse_list = []
    for layer_idx in range(layer_count):
        pivot = diagonal[layer_idx]
        if layer_idx > 0:
            pivot = pivot + lower_link[layer_idx] * ratio_list[-1]
        inverse = 1.0 / pivot
        inverse_list.append(inverse)
        ratio_list.append(-upper_link[layer_idx] * inverse)
    return (faces, lower_link, ratio_list, inverse_list)


def relax_lanes(vel_pad, rhs_field, faces, lower_link, ratios, inverses, ice_cover, weights):
    west_face, east_face, south_face, north_face = faces
    along_x, along_y = weights
    lateral = along_x * (west_face * vel_pad[:, :-2, 1:-1] + east_face * vel_pad[:, 2:, 1:-1])
    lateral = lateral + along_y * (
        south_face * vel_pad[:, 1:-1, :-2] + north_face * vel_pad[:, 1:-1, 2:]
    )
    right_side = rhs_field + lateral
    layer_count = right_side.shape[0]
    forward_list = []
    for layer_idx in range(layer_count):
        value = right_side[layer_idx]
        if layer_idx > 0:
            value = value + lower_link[layer_idx] * forward_list[-1]
        forward_list.append(value * inverses[layer_idx])
    solved = [None] * layer_count
    solved[layer_count - 1] = forward_list[layer_count - 1]
    for layer_idx in range(layer_count - 2, -1, -1):
        solved[layer_idx] = forward_list[layer_idx] - ratios[layer_idx] * solved[layer_idx + 1]
    line_value = jnp.stack(solved, 0)
    centre = vel_pad[:, 1:-1, 1:-1]
    return ice_cover * ((1.0 - OMEGA) * centre + OMEGA * line_value)


def pad_cells(field):
    return jnp.pad(field, [(0, 0)] * (field.ndim - 2) + [(1, 1), (1, 1)])


def shifted(piece, axis, down):
    count = lax.axis_size(axis)
    if down:
        pairs = [(i, i + 1) for i in range(count - 1)]
    else:
        pairs = [(i + 1, i) for i in range(count - 1)]
    return lax.ppermute(piece, axis, pairs)


def local(forcing, viscosity, observed, beta_tiles, ice_mask, tile_owner):
    comps, layers, rows, cols = forcing.shape
    tiles_here = beta_tiles.shape[1]
    planes = [
        forcing.reshape(comps * layers, rows, cols),
        viscosity,
        observed,
        ice_mask.astype(jnp.float32)[None],
        tile_owner.astype(jnp.float32)[None],
    ]
    plane_count = sum(p.shape[0] for p in planes)

    beta_plane = jnp.pad(beta_tiles, ((0, HALO - 1), (0, cols - tiles_here)))[None]
    head = jnp.concatenate([p[:, :HALO] for p in planes] + [beta_plane], axis=0)
    tail = jnp.concatenate([p[:, rows - HALO:] for p in planes] + [beta_plane], axis=0)
    from_above = shifted(tail, "gx", True)
    from_below = shifted(head, "gx", False)

    def stack_rows(lo, hi):
        return jnp.concatenate(
            [from_above[:plane_count, :, lo:hi]]
            + [jnp.concatenate([p[:, :, lo:hi] for p in planes], axis=0)]
            + [from_below[:plane_count, :, lo:hi]],
            axis=1,
        )

    from_left = shifted(stack_rows(cols - HALO, cols), "gy", True)
    from_right = shifted(stack_rows(0, HALO), "gy", False)

    strips_near = jnp.stack(
        [from_above[plane_count, 0, :tiles_here], beta_tiles[0], from_below[plane_count, 0, :tiles_here]]
    )
    friction_rows = lax.all_gather(strips_near, "gy", axis=1, tiled=True)
    tile_count = friction_rows.shape[1]

    packed = jnp.concatenate([from_left, stack_rows(0, cols), from_right], axis=2)
    ext_rows, ext_cols = packed.shape[1], packed.shape[2]
    at = 0
    forcing_ext = packed[at:at + comps * layers].reshape(comps, layers, ext_rows, ext_cols)
    at += comps * layers
    visc_ext = packed[at:at + layers]
    at += layers
    observed_ext = packed[at:at + comps]
    at += comps
    ice_cover = packed[at]
    owner_ext = packed[at + 1].astype(jnp.int32)

    tiles = lax.broadcasted_iota(jnp.int32, (tile_count, 1, 1), 0)
    owner_match = owner_ext[None] == tiles
    row_strip = jnp.concatenate(
        [
            jnp.broadcast_to(friction_rows[0][:, None], (tile_count, HALO)),
            jnp.broadcast_to(friction_rows[1][:, None], (tile_count, rows)),
            jnp.broadcast_to(friction_rows[2][:, None], (tile_count, HALO)),
        ],
        axis=1,
    )
    beta_col = jnp.sum(jnp.where(owner_match, row_strip[:, :, None], 0.0), axis=0)

    def side_by_side(per_comp):
        return jnp.concatenate([per_comp[c] for c in range(comps)], axis=-1)

    weights = lane_weights(comps, ext_cols)
    visc_lanes = side_by_side([visc_ext] * comps)
    ice_lanes = side_by_side([ice_cover] * comps)
    beta_lanes = side_by_side([beta_col] * comps)
    forcing_lanes = side_by_side([forcing_ext[c] for c in range(comps)])
    observed_lanes = side_by_side([observed_ext[c] for c in range(comps)])
    faces, lower_link, ratios, inverses = prepare_lanes(
        pad_cells(visc_lanes), beta_lanes, ice_lanes, weights
    )

    def advance(field, rhs_field):
        return relax_lanes(pad_cells(field), rhs_field, faces, lower_link, ratios, inverses, ice_lanes, weights)

    velocity = jnp.zeros_like(forcing_lanes)
    for sweep_idx in range(PASSES):
        velocity = advance(velocity, forcing_lanes)
    misfit = velocity[0] - observed_lanes
    adjoint_rhs = jnp.zeros_like(forcing_lanes).at[0].set(misfit)
    adjoint = jnp.zeros_like(forcing_lanes)
    for sweep_idx in range(PASSES):
        adjoint = advance(adjoint, adjoint_rhs)

    inner = (slice(HALO, HALO + rows), slice(HALO, HALO + cols))

    def split(field):
        return jnp.stack(
            [field[:, inner[0], c * ext_cols + HALO:c * ext_cols + HALO + cols] for c in range(comps)]
        )

    velocity = split(velocity)
    adjoint = split(adjoint)
    grad_col = -ice_cover[inner] * beta_col[inner] * jnp.sum(adjoint[:, -1] * velocity[:, -1], axis=0)
    high = lax.reduce_precision(grad_col, exponent_bits=8, mantissa_bits=7)
    rest = grad_col - high
    middle = lax.reduce_precision(rest, exponent_bits=8, mantissa_bits=7)
    low = rest - middle
    parts = jnp.stack([high, middle, low], axis=-1).reshape(rows * cols, 3).astype(jnp.bfloat16)
    block_match = tile_owner.reshape(rows * cols, 1) == lax.broadcasted_iota(jnp.int32, (1, tile_count), 1)
    per_part = lax.dot_general(
        block_match.astype(jnp.bfloat16), parts, (((0,), (0,)), ((), ())),
        preferred_element_type=jnp.float32,
    )
    partial_sum = per_part[:, 0] + per_part[:, 1] + per_part[:, 2]
    owners = lax.axis_size("gy")
    chunk = tile_count // owners
    gathered = lax.all_gather(partial_sum.reshape(owners, chunk), "gy")
    mine = lax.dynamic_index_in_dim(gathered, lax.axis_index("gy"), axis=1, keepdims=False)
    grad_tiles = jnp.sum(mine, axis=0)[None]
    return (velocity, adjoint, grad_tiles)


def solution(mesh):
    in_specs = (
        P(None, None, "gx", "gy"),
        P(None, "gx", "gy"),
        P(None, "gx", "gy"),
        P("gx", "gy"),
        P("gx", "gy"),
        P("gx", "gy"),
    )
    out_specs = (P(None, None, "gx", "gy"), P(None, None, "gx", "gy"), P("gx", "gy"))
    return jax.shard_map(local, mesh=mesh, in_specs=in_specs, out_specs=out_specs, check_vma=False)
```

```python
import jax
import jax.numpy as jnp
from jax import lax
from jax.sharding import PartitionSpec as P

PASSES = 4


OMEGA = 0.8
VERTICAL = 16.0
HALO = 2 * PASSES - 1


def with_halo(cells, sides, width):
    for axis, dim in sides:
        count = lax.axis_size(axis)
        ends = count - 1
        head = lax.slice_in_dim(cells, 0, width, axis=dim)
        tail = lax.slice_in_dim(cells, cells.shape[dim] - width, cells.shape[dim], axis=dim)
        cells = jnp.concatenate(
            [
                lax.ppermute(tail, axis, [(i, (i + 1) % count) for i in range(ends)]),
                cells,
                lax.ppermute(head, axis, [((i + 1) % count, i) for i in range(ends)]),
            ],
            axis=dim,
        )
    return cells


def lateral_terms(visc_pad):
    centre_visc = visc_pad[:, 1:-1, 1:-1]
    west_face = 0.5 * (centre_visc + visc_pad[:, :-2, 1:-1])
    east_face = 0.5 * (centre_visc + visc_pad[:, 2:, 1:-1])
    south_face = 0.5 * (centre_visc + visc_pad[:, 1:-1, :-2])
    north_face = 0.5 * (centre_visc + visc_pad[:, 1:-1, 2:])
    return (west_face, east_face, south_face, north_face)


def weights_xy():
    along_x = jnp.array([4.0, 1.0], jnp.float32).reshape(2, 1, 1, 1)
    along_y = jnp.array([1.0, 4.0], jnp.float32).reshape(2, 1, 1, 1)
    return (along_x, along_y)


def prepare(visc_pad, beta_col, ice_cover):
    faces = lateral_terms(visc_pad)
    west_face, east_face, south_face, north_face = faces
    along_x, along_y = weights_xy()
    centre_visc = visc_pad[:, 1:-1, 1:-1]
    vertical = VERTICAL * 0.5 * (centre_visc[:-1] + centre_visc[1:])
    zero_row = jnp.zeros_like(centre_visc[:1])
    upper_link = jnp.concatenate([vertical, zero_row], 0)
    lower_link = jnp.concatenate([zero_row, vertical], 0)
    basal = jnp.concatenate([jnp.zeros_like(centre_visc[:-1]), beta_col[None]], 0)
    diagonal = along_x * (west_face + east_face) + along_y * (south_face + north_face)
    diagonal = diagonal + upper_link + lower_link + basal + (1.0 - ice_cover)
    layer_count = visc_pad.shape[0]
    ratio_list = []
    inverse_list = []
    for layer_idx in range(layer_count):
        pivot = diagonal[:, layer_idx]
        if layer_idx > 0:
            pivot = pivot + lower_link[layer_idx] * ratio_list[-1]
        inverse = 1.0 / pivot
        inverse_list.append(inverse)
        ratio_list.append(-upper_link[layer_idx] * inverse)
    return (faces, lower_link, jnp.stack(ratio_list, 1), jnp.stack(inverse_list, 1))


def relax(vel_pad, rhs_field, faces, lower_link, ratios, inverses, ice_cover):
    west_face, east_face, south_face, north_face = faces
    along_x, along_y = weights_xy()
    lateral = along_x * (west_face * vel_pad[:, :, :-2, 1:-1] + east_face * vel_pad[:, :, 2:, 1:-1])
    lateral = lateral + along_y * (
        south_face * vel_pad[:, :, 1:-1, :-2] + north_face * vel_pad[:, :, 1:-1, 2:]
    )
    right_side = rhs_field + lateral
    layer_count = right_side.shape[1]
    forward_list = []
    for layer_idx in range(layer_count):
        value = right_side[:, layer_idx]
        if layer_idx > 0:
            value = value + lower_link[layer_idx] * forward_list[-1]
        forward_list.append(value * inverses[:, layer_idx])
    solved = [None] * layer_count
    solved[layer_count - 1] = forward_list[layer_count - 1]
    for layer_idx in range(layer_count - 2, -1, -1):
        solved[layer_idx] = forward_list[layer_idx] - ratios[:, layer_idx] * solved[layer_idx + 1]
    line_value = jnp.stack(solved, 1)
    centre = vel_pad[:, :, 1:-1, 1:-1]
    return ice_cover * ((1.0 - OMEGA) * centre + OMEGA * line_value)


def lane_weights(comps, width):
    along_x = jnp.concatenate([jnp.full((width,), (4.0, 1.0)[c], jnp.float32) for c in range(comps)])
    along_y = jnp.concatenate([jnp.full((width,), (1.0, 4.0)[c], jnp.float32) for c in range(comps)])
    return (along_x, along_y)


def prepare_lanes(visc_pad, beta_col, ice_cover, weights):
    faces = lateral_terms(visc_pad)
    west_face, east_face, south_face, north_face = faces
    along_x, along_y = weights
    centre_visc = visc_pad[:, 1:-1, 1:-1]
    vertical = VERTICAL * 0.5 * (centre_visc[:-1] + centre_visc[1:])
    zero_row = jnp.zeros_like(centre_visc[:1])
    upper_link = jnp.concatenate([vertical, zero_row], 0)
    lower_link = jnp.concatenate([zero_row, vertical], 0)
    basal = jnp.concatenate([jnp.zeros_like(centre_visc[:-1]), beta_col[None]], 0)
    diagonal = along_x * (west_face + east_face) + along_y * (south_face + north_face)
    diagonal = diagonal + upper_link + lower_link + basal + (1.0 - ice_cover)
    layer_count = visc_pad.shape[0]
    ratio_list = []
    inverse_list = []
    for layer_idx in range(layer_count):
        pivot = diagonal[layer_idx]
        if layer_idx > 0:
            pivot = pivot + lower_link[layer_idx] * ratio_list[-1]
        inverse = 1.0 / pivot
        inverse_list.append(inverse)
        ratio_list.append(-upper_link[layer_idx] * inverse)
    return (faces, lower_link, ratio_list, inverse_list)


def relax_lanes(vel_pad, rhs_field, faces, lower_link, ratios, inverses, ice_cover, weights):
    west_face, east_face, south_face, north_face = faces
    along_x, along_y = weights
    lateral = along_x * (west_face * vel_pad[:, :-2, 1:-1] + east_face * vel_pad[:, 2:, 1:-1])
    lateral = lateral + along_y * (
        south_face * vel_pad[:, 1:-1, :-2] + north_face * vel_pad[:, 1:-1, 2:]
    )
    right_side = rhs_field + lateral
    layer_count = right_side.shape[0]
    forward_list = []
    for layer_idx in range(layer_count):
        value = right_side[layer_idx]
        if layer_idx > 0:
            value = value + lower_link[layer_idx] * forward_list[-1]
        forward_list.append(value * inverses[layer_idx])
    solved = [None] * layer_count
    solved[layer_count - 1] = forward_list[layer_count - 1]
    for layer_idx in range(layer_count - 2, -1, -1):
        solved[layer_idx] = forward_list[layer_idx] - ratios[layer_idx] * solved[layer_idx + 1]
    line_value = jnp.stack(solved, 0)
    centre = vel_pad[:, 1:-1, 1:-1]
    return ice_cover * ((1.0 - OMEGA) * centre + OMEGA * line_value)


def pad_cells(field):
    return jnp.pad(field, [(0, 0)] * (field.ndim - 2) + [(1, 1), (1, 1)])


def shifted(piece, axis, down):
    count = lax.axis_size(axis)
    if down:
        pairs = [(i, i + 1) for i in range(count - 1)]
    else:
        pairs = [(i + 1, i) for i in range(count - 1)]
    return lax.ppermute(piece, axis, pairs)


def local(forcing, viscosity, observed, beta_tiles, ice_mask, tile_owner):
    comps, layers, rows, cols = forcing.shape
    tiles_here = beta_tiles.shape[1]
    planes = [
        forcing.reshape(comps * layers, rows, cols),
        viscosity,
        observed,
        ice_mask.astype(jnp.float32)[None],
        tile_owner.astype(jnp.float32)[None],
    ]
    plane_count = sum(p.shape[0] for p in planes)

    beta_plane = jnp.pad(beta_tiles, ((0, HALO - 1), (0, cols - tiles_here)))[None]
    head = jnp.concatenate([p[:, :HALO] for p in planes] + [beta_plane], axis=0)
    tail = jnp.concatenate([p[:, rows - HALO:] for p in planes] + [beta_plane], axis=0)
    from_above = shifted(tail, "gx", True)
    from_below = shifted(head, "gx", False)

    def stack_rows(lo, hi):
        return jnp.concatenate(
            [from_above[:plane_count, :, lo:hi]]
            + [jnp.concatenate([p[:, :, lo:hi] for p in planes], axis=0)]
            + [from_below[:plane_count, :, lo:hi]],
            axis=1,
        )

    from_left = shifted(stack_rows(cols - HALO, cols), "gy", True)
    from_right = shifted(stack_rows(0, HALO), "gy", False)

    strips_near = jnp.stack(
        [from_above[plane_count, 0, :tiles_here], beta_tiles[0], from_below[plane_count, 0, :tiles_here]]
    )
    friction_rows = lax.all_gather(strips_near, "gy", axis=1, tiled=True)
    tile_count = friction_rows.shape[1]

    packed = jnp.concatenate([from_left, stack_rows(0, cols), from_right], axis=2)
    ext_rows, ext_cols = packed.shape[1], packed.shape[2]
    at = 0
    forcing_ext = packed[at:at + comps * layers].reshape(comps, layers, ext_rows, ext_cols)
    at += comps * layers
    visc_ext = packed[at:at + layers]
    at += layers
    observed_ext = packed[at:at + comps]
    at += comps
    ice_cover = packed[at]
    owner_ext = packed[at + 1].astype(jnp.int32)

    strip_table = friction_rows.T
    high = lax.reduce_precision(strip_table, exponent_bits=8, mantissa_bits=7)
    rest = strip_table - high
    middle = lax.reduce_precision(rest, exponent_bits=8, mantissa_bits=7)
    low = rest - middle
    parts = jnp.concatenate([high, middle, low], axis=1).astype(jnp.bfloat16)
    tiles = lax.broadcasted_iota(jnp.int32, (1, 1, tile_count), 2)
    one_hot = (owner_ext[:, :, None] == tiles).astype(jnp.bfloat16)
    looked_up = lax.dot_general(
        one_hot, parts, (((2,), (0,)), ((), ())), preferred_element_type=jnp.float32
    )
    band = lax.broadcasted_iota(jnp.int32, (ext_rows, 1), 0)
    strip_of_row = jnp.where(band < HALO, 0, jnp.where(band < HALO + rows, 1, 2))
    near = friction_rows.shape[0]
    beta_col = sum(
        jnp.where(strip_of_row == k, looked_up[:, :, k] + looked_up[:, :, near + k] + looked_up[:, :, 2 * near + k], 0.0)
        for k in range(near)
    )

    def side_by_side(per_comp):
        return jnp.concatenate([per_comp[c] for c in range(comps)], axis=-1)

    weights = lane_weights(comps, ext_cols)
    visc_lanes = side_by_side([visc_ext] * comps)
    ice_lanes = side_by_side([ice_cover] * comps)
    beta_lanes = side_by_side([beta_col] * comps)
    forcing_lanes = side_by_side([forcing_ext[c] for c in range(comps)])
    observed_lanes = side_by_side([observed_ext[c] for c in range(comps)])
    faces, lower_link, ratios, inverses = prepare_lanes(
        pad_cells(visc_lanes), beta_lanes, ice_lanes, weights
    )

    def advance(field, rhs_field):
        return relax_lanes(pad_cells(field), rhs_field, faces, lower_link, ratios, inverses, ice_lanes, weights)

    velocity = jnp.zeros_like(forcing_lanes)
    for sweep_idx in range(PASSES):
        velocity = advance(velocity, forcing_lanes)
    misfit = velocity[0] - observed_lanes
    adjoint_rhs = jnp.zeros_like(forcing_lanes).at[0].set(misfit)
    adjoint = jnp.zeros_like(forcing_lanes)
    for sweep_idx in range(PASSES):
        adjoint = advance(adjoint, adjoint_rhs)

    inner = (slice(HALO, HALO + rows), slice(HALO, HALO + cols))

    def split(field):
        return jnp.stack(
            [field[:, inner[0], c * ext_cols + HALO:c * ext_cols + HALO + cols] for c in range(comps)]
        )

    velocity = split(velocity)
    adjoint = split(adjoint)
    grad_col = -ice_cover[inner] * beta_col[inner] * jnp.sum(adjoint[:, -1] * velocity[:, -1], axis=0)
    high = lax.reduce_precision(grad_col, exponent_bits=8, mantissa_bits=7)
    rest = grad_col - high
    middle = lax.reduce_precision(rest, exponent_bits=8, mantissa_bits=7)
    low = rest - middle
    parts = jnp.stack([high, middle, low], axis=-1).reshape(rows * cols, 3).astype(jnp.bfloat16)
    block_match = tile_owner.reshape(rows * cols, 1) == lax.broadcasted_iota(jnp.int32, (1, tile_count), 1)
    per_part = lax.dot_general(
        block_match.astype(jnp.bfloat16), parts, (((0,), (0,)), ((), ())),
        preferred_element_type=jnp.float32,
    )
    partial_sum = per_part[:, 0] + per_part[:, 1] + per_part[:, 2]
    owners = lax.axis_size("gy")
    chunk = tile_count // owners
    gathered = lax.all_gather(partial_sum.reshape(owners, chunk), "gy")
    mine = lax.dynamic_index_in_dim(gathered, lax.axis_index("gy"), axis=1, keepdims=False)
    grad_tiles = jnp.sum(mine, axis=0)[None]
    return (velocity, adjoint, grad_tiles)


def solution(mesh):
    in_specs = (
        P(None, None, "gx", "gy"),
        P(None, "gx", "gy"),
        P(None, "gx", "gy"),
        P("gx", "gy"),
        P("gx", "gy"),
        P("gx", "gy"),
    )
    out_specs = (P(None, None, "gx", "gy"), P(None, None, "gx", "gy"), P("gx", "gy"))
    return jax.shard_map(local, mesh=mesh, in_specs=in_specs, out_specs=out_specs, check_vma=False)
```

```python
import jax
import jax.numpy as jnp
from jax import lax
from jax.sharding import PartitionSpec as P

PASSES = 4


OMEGA = 0.8
VERTICAL = 16.0
HALO = 2 * PASSES - 1


def with_halo(cells, sides, width):
    for axis, dim in sides:
        count = lax.axis_size(axis)
        ends = count - 1
        head = lax.slice_in_dim(cells, 0, width, axis=dim)
        tail = lax.slice_in_dim(cells, cells.shape[dim] - width, cells.shape[dim], axis=dim)
        cells = jnp.concatenate(
            [
                lax.ppermute(tail, axis, [(i, (i + 1) % count) for i in range(ends)]),
                cells,
                lax.ppermute(head, axis, [((i + 1) % count, i) for i in range(ends)]),
            ],
            axis=dim,
        )
    return cells


def lateral_terms(visc_pad):
    centre_visc = visc_pad[:, 1:-1, 1:-1]
    west_face = 0.5 * (centre_visc + visc_pad[:, :-2, 1:-1])
    east_face = 0.5 * (centre_visc + visc_pad[:, 2:, 1:-1])
    south_face = 0.5 * (centre_visc + visc_pad[:, 1:-1, :-2])
    north_face = 0.5 * (centre_visc + visc_pad[:, 1:-1, 2:])
    return (west_face, east_face, south_face, north_face)


def weights_xy():
    along_x = jnp.array([4.0, 1.0], jnp.float32).reshape(2, 1, 1, 1)
    along_y = jnp.array([1.0, 4.0], jnp.float32).reshape(2, 1, 1, 1)
    return (along_x, along_y)


def prepare(visc_pad, beta_col, ice_cover):
    faces = lateral_terms(visc_pad)
    west_face, east_face, south_face, north_face = faces
    along_x, along_y = weights_xy()
    centre_visc = visc_pad[:, 1:-1, 1:-1]
    vertical = VERTICAL * 0.5 * (centre_visc[:-1] + centre_visc[1:])
    zero_row = jnp.zeros_like(centre_visc[:1])
    upper_link = jnp.concatenate([vertical, zero_row], 0)
    lower_link = jnp.concatenate([zero_row, vertical], 0)
    basal = jnp.concatenate([jnp.zeros_like(centre_visc[:-1]), beta_col[None]], 0)
    diagonal = along_x * (west_face + east_face) + along_y * (south_face + north_face)
    diagonal = diagonal + upper_link + lower_link + basal + (1.0 - ice_cover)
    layer_count = visc_pad.shape[0]
    ratio_list = []
    inverse_list = []
    for layer_idx in range(layer_count):
        pivot = diagonal[:, layer_idx]
        if layer_idx > 0:
            pivot = pivot + lower_link[layer_idx] * ratio_list[-1]
        inverse = 1.0 / pivot
        inverse_list.append(inverse)
        ratio_list.append(-upper_link[layer_idx] * inverse)
    return (faces, lower_link, jnp.stack(ratio_list, 1), jnp.stack(inverse_list, 1))


def relax(vel_pad, rhs_field, faces, lower_link, ratios, inverses, ice_cover):
    west_face, east_face, south_face, north_face = faces
    along_x, along_y = weights_xy()
    lateral = along_x * (west_face * vel_pad[:, :, :-2, 1:-1] + east_face * vel_pad[:, :, 2:, 1:-1])
    lateral = lateral + along_y * (
        south_face * vel_pad[:, :, 1:-1, :-2] + north_face * vel_pad[:, :, 1:-1, 2:]
    )
    right_side = rhs_field + lateral
    layer_count = right_side.shape[1]
    forward_list = []
    for layer_idx in range(layer_count):
        value = right_side[:, layer_idx]
        if layer_idx > 0:
            value = value + lower_link[layer_idx] * forward_list[-1]
        forward_list.append(value * inverses[:, layer_idx])
    solved = [None] * layer_count
    solved[layer_count - 1] = forward_list[layer_count - 1]
    for layer_idx in range(layer_count - 2, -1, -1):
        solved[layer_idx] = forward_list[layer_idx] - ratios[:, layer_idx] * solved[layer_idx + 1]
    line_value = jnp.stack(solved, 1)
    centre = vel_pad[:, :, 1:-1, 1:-1]
    return ice_cover * ((1.0 - OMEGA) * centre + OMEGA * line_value)


def lane_weights(comps, width):
    along_x = jnp.concatenate([jnp.full((width,), (4.0, 1.0)[c], jnp.float32) for c in range(comps)])
    along_y = jnp.concatenate([jnp.full((width,), (1.0, 4.0)[c], jnp.float32) for c in range(comps)])
    return (along_x, along_y)


def prepare_lanes(visc_pad, beta_col, ice_cover, weights):
    faces = lateral_terms(visc_pad)
    west_face, east_face, south_face, north_face = faces
    along_x, along_y = weights
    centre_visc = visc_pad[:, 1:-1, 1:-1]
    vertical = VERTICAL * 0.5 * (centre_visc[:-1] + centre_visc[1:])
    zero_row = jnp.zeros_like(centre_visc[:1])
    upper_link = jnp.concatenate([vertical, zero_row], 0)
    lower_link = jnp.concatenate([zero_row, vertical], 0)
    basal = jnp.concatenate([jnp.zeros_like(centre_visc[:-1]), beta_col[None]], 0)
    diagonal = along_x * (west_face + east_face) + along_y * (south_face + north_face)
    diagonal = diagonal + upper_link + lower_link + basal + (1.0 - ice_cover)
    layer_count = visc_pad.shape[0]
    ratio_list = []
    inverse_list = []
    for layer_idx in range(layer_count):
        pivot = diagonal[layer_idx]
        if layer_idx > 0:
            pivot = pivot + lower_link[layer_idx] * ratio_list[-1]
        inverse = 1.0 / pivot
        inverse_list.append(inverse)
        ratio_list.append(-upper_link[layer_idx] * inverse)
    return (faces, lower_link, ratio_list, inverse_list)


def relax_lanes(vel_pad, rhs_field, faces, lower_link, ratios, inverses, ice_cover, weights):
    west_face, east_face, south_face, north_face = faces
    along_x, along_y = weights
    lateral = along_x * (west_face * vel_pad[:, :-2, 1:-1] + east_face * vel_pad[:, 2:, 1:-1])
    lateral = lateral + along_y * (
        south_face * vel_pad[:, 1:-1, :-2] + north_face * vel_pad[:, 1:-1, 2:]
    )
    right_side = rhs_field + lateral
    layer_count = right_side.shape[0]
    forward_list = []
    for layer_idx in range(layer_count):
        value = right_side[layer_idx]
        if layer_idx > 0:
            value = value + lower_link[layer_idx] * forward_list[-1]
        forward_list.append(value * inverses[layer_idx])
    solved = [None] * layer_count
    solved[layer_count - 1] = forward_list[layer_count - 1]
    for layer_idx in range(layer_count - 2, -1, -1):
        solved[layer_idx] = forward_list[layer_idx] - ratios[layer_idx] * solved[layer_idx + 1]
    line_value = jnp.stack(solved, 0)
    centre = vel_pad[:, 1:-1, 1:-1]
    return ice_cover * ((1.0 - OMEGA) * centre + OMEGA * line_value)


def pad_cells(field):
    return jnp.pad(field, [(0, 0)] * (field.ndim - 2) + [(1, 1), (1, 1)])


def shifted(piece, axis, down):
    count = lax.axis_size(axis)
    if down:
        pairs = [(i, i + 1) for i in range(count - 1)]
    else:
        pairs = [(i + 1, i) for i in range(count - 1)]
    return lax.ppermute(piece, axis, pairs)


def local(forcing, viscosity, observed, beta_tiles, ice_mask, tile_owner):
    comps, layers, rows, cols = forcing.shape
    tiles_here = beta_tiles.shape[1]
    planes = [
        forcing.reshape(comps * layers, rows, cols),
        viscosity,
        observed,
        ice_mask.astype(jnp.float32)[None],
        tile_owner.astype(jnp.float32)[None],
    ]
    plane_count = sum(p.shape[0] for p in planes)

    beta_plane = jnp.pad(beta_tiles, ((0, HALO - 1), (0, cols - tiles_here)))[None]
    head = jnp.concatenate([p[:, :HALO] for p in planes] + [beta_plane], axis=0)
    tail = jnp.concatenate([p[:, rows - HALO:] for p in planes] + [beta_plane], axis=0)
    from_above = shifted(tail, "gx", True)
    from_below = shifted(head, "gx", False)

    def stack_rows(lo, hi):
        return jnp.concatenate(
            [from_above[:plane_count, :, lo:hi]]
            + [jnp.concatenate([p[:, :, lo:hi] for p in planes], axis=0)]
            + [from_below[:plane_count, :, lo:hi]],
            axis=1,
        )

    from_left = shifted(stack_rows(cols - HALO, cols), "gy", True)
    from_right = shifted(stack_rows(0, HALO), "gy", False)

    strips_near = jnp.stack(
        [from_above[plane_count, 0, :tiles_here], beta_tiles[0], from_below[plane_count, 0, :tiles_here]]
    )
    friction_rows = lax.all_gather(strips_near, "gy", axis=1, tiled=True)
    tile_count = friction_rows.shape[1]

    packed = jnp.concatenate([from_left, stack_rows(0, cols), from_right], axis=2)
    ext_rows, ext_cols = packed.shape[1], packed.shape[2]
    at = 0
    forcing_ext = packed[at:at + comps * layers].reshape(comps, layers, ext_rows, ext_cols)
    at += comps * layers
    visc_ext = packed[at:at + layers]
    at += layers
    observed_ext = packed[at:at + comps]
    at += comps
    ice_cover = packed[at]
    owner_ext = packed[at + 1].astype(jnp.int32)

    tiles = lax.broadcasted_iota(jnp.int32, (tile_count, 1, 1), 0)
    owner_match = owner_ext[None] == tiles
    row_strip = jnp.concatenate(
        [
            jnp.broadcast_to(friction_rows[0][:, None], (tile_count, HALO)),
            jnp.broadcast_to(friction_rows[1][:, None], (tile_count, rows)),
            jnp.broadcast_to(friction_rows[2][:, None], (tile_count, HALO)),
        ],
        axis=1,
    )
    beta_col = jnp.sum(jnp.where(owner_match, row_strip[:, :, None], 0.0), axis=0)

    def side_by_side(per_comp):
        return jnp.concatenate([per_comp[c] for c in range(comps)], axis=-1)

    weights = lane_weights(comps, ext_cols)
    visc_lanes = side_by_side([visc_ext] * comps)
    ice_lanes = side_by_side([ice_cover] * comps)
    beta_lanes = side_by_side([beta_col] * comps)
    forcing_lanes = side_by_side([forcing_ext[c] for c in range(comps)])
    observed_lanes = side_by_side([observed_ext[c] for c in range(comps)])
    faces, lower_link, ratios, inverses = prepare_lanes(
        pad_cells(visc_lanes), beta_lanes, ice_lanes, weights
    )

    def advance(field, rhs_field):
        return relax_lanes(pad_cells(field), rhs_field, faces, lower_link, ratios, inverses, ice_lanes, weights)

    velocity = jnp.zeros_like(forcing_lanes)
    for sweep_idx in range(PASSES):
        velocity = advance(velocity, forcing_lanes)
    misfit = velocity[0] - observed_lanes
    adjoint_rhs = jnp.zeros_like(forcing_lanes).at[0].set(misfit)
    adjoint = jnp.zeros_like(forcing_lanes)
    for sweep_idx in range(PASSES):
        adjoint = advance(adjoint, adjoint_rhs)

    inner = (slice(HALO, HALO + rows), slice(HALO, HALO + cols))

    def split(field):
        return jnp.stack(
            [field[:, inner[0], c * ext_cols + HALO:c * ext_cols + HALO + cols] for c in range(comps)]
        )

    velocity = split(velocity)
    adjoint = split(adjoint)
    grad_col = -ice_cover[inner] * beta_col[inner] * jnp.sum(adjoint[:, -1] * velocity[:, -1], axis=0)
    high = lax.reduce_precision(grad_col, exponent_bits=8, mantissa_bits=7)
    rest = grad_col - high
    middle = lax.reduce_precision(rest, exponent_bits=8, mantissa_bits=7)
    low = rest - middle
    parts = jnp.stack([high, middle, low], axis=-1).reshape(rows * cols, 3).astype(jnp.bfloat16)
    block_match = tile_owner.reshape(rows * cols, 1) == lax.broadcasted_iota(jnp.int32, (1, tile_count), 1)
    per_part = lax.dot_general(
        block_match.astype(jnp.bfloat16), parts, (((0,), (0,)), ((), ())),
        preferred_element_type=jnp.float32,
    )
    partial_sum = per_part[:, 0] + per_part[:, 1] + per_part[:, 2]
    owners = lax.axis_size("gy")
    received = lax.all_to_all(partial_sum.reshape(owners, -1), "gy", 0, 0, tiled=True)
    grad_tiles = jnp.sum(received, axis=0)[None]
    return (velocity, adjoint, grad_tiles)


def solution(mesh):
    in_specs = (
        P(None, None, "gx", "gy"),
        P(None, "gx", "gy"),
        P(None, "gx", "gy"),
        P("gx", "gy"),
        P("gx", "gy"),
        P("gx", "gy"),
    )
    out_specs = (P(None, None, "gx", "gy"), P(None, None, "gx", "gy"), P("gx", "gy"))
    return jax.shard_map(local, mesh=mesh, in_specs=in_specs, out_specs=out_specs, check_vma=False)
```

```python
import jax
import jax.numpy as jnp
from jax import lax
from jax.sharding import PartitionSpec as P

PASSES = 4


OMEGA = 0.8
VERTICAL = 16.0
HALO = 2 * PASSES - 1


def with_halo(cells, sides, width):
    for axis, dim in sides:
        count = lax.axis_size(axis)
        ends = count - 1
        head = lax.slice_in_dim(cells, 0, width, axis=dim)
        tail = lax.slice_in_dim(cells, cells.shape[dim] - width, cells.shape[dim], axis=dim)
        cells = jnp.concatenate(
            [
                lax.ppermute(tail, axis, [(i, (i + 1) % count) for i in range(ends)]),
                cells,
                lax.ppermute(head, axis, [((i + 1) % count, i) for i in range(ends)]),
            ],
            axis=dim,
        )
    return cells


def lateral_terms(visc_pad):
    centre_visc = visc_pad[:, 1:-1, 1:-1]
    west_face = 0.5 * (centre_visc + visc_pad[:, :-2, 1:-1])
    east_face = 0.5 * (centre_visc + visc_pad[:, 2:, 1:-1])
    south_face = 0.5 * (centre_visc + visc_pad[:, 1:-1, :-2])
    north_face = 0.5 * (centre_visc + visc_pad[:, 1:-1, 2:])
    return (west_face, east_face, south_face, north_face)


def weights_xy():
    along_x = jnp.array([4.0, 1.0], jnp.float32).reshape(2, 1, 1, 1)
    along_y = jnp.array([1.0, 4.0], jnp.float32).reshape(2, 1, 1, 1)
    return (along_x, along_y)


def prepare(visc_pad, beta_col, ice_cover):
    faces = lateral_terms(visc_pad)
    west_face, east_face, south_face, north_face = faces
    along_x, along_y = weights_xy()
    centre_visc = visc_pad[:, 1:-1, 1:-1]
    vertical = VERTICAL * 0.5 * (centre_visc[:-1] + centre_visc[1:])
    zero_row = jnp.zeros_like(centre_visc[:1])
    upper_link = jnp.concatenate([vertical, zero_row], 0)
    lower_link = jnp.concatenate([zero_row, vertical], 0)
    basal = jnp.concatenate([jnp.zeros_like(centre_visc[:-1]), beta_col[None]], 0)
    diagonal = along_x * (west_face + east_face) + along_y * (south_face + north_face)
    diagonal = diagonal + upper_link + lower_link + basal + (1.0 - ice_cover)
    layer_count = visc_pad.shape[0]
    ratio_list = []
    inverse_list = []
    for layer_idx in range(layer_count):
        pivot = diagonal[:, layer_idx]
        if layer_idx > 0:
            pivot = pivot + lower_link[layer_idx] * ratio_list[-1]
        inverse = 1.0 / pivot
        inverse_list.append(inverse)
        ratio_list.append(-upper_link[layer_idx] * inverse)
    return (faces, lower_link, jnp.stack(ratio_list, 1), jnp.stack(inverse_list, 1))


def relax(vel_pad, rhs_field, faces, lower_link, ratios, inverses, ice_cover):
    west_face, east_face, south_face, north_face = faces
    along_x, along_y = weights_xy()
    lateral = along_x * (west_face * vel_pad[:, :, :-2, 1:-1] + east_face * vel_pad[:, :, 2:, 1:-1])
    lateral = lateral + along_y * (
        south_face * vel_pad[:, :, 1:-1, :-2] + north_face * vel_pad[:, :, 1:-1, 2:]
    )
    right_side = rhs_field + lateral
    layer_count = right_side.shape[1]
    forward_list = []
    for layer_idx in range(layer_count):
        value = right_side[:, layer_idx]
        if layer_idx > 0:
            value = value + lower_link[layer_idx] * forward_list[-1]
        forward_list.append(value * inverses[:, layer_idx])
    solved = [None] * layer_count
    solved[layer_count - 1] = forward_list[layer_count - 1]
    for layer_idx in range(layer_count - 2, -1, -1):
        solved[layer_idx] = forward_list[layer_idx] - ratios[:, layer_idx] * solved[layer_idx + 1]
    line_value = jnp.stack(solved, 1)
    centre = vel_pad[:, :, 1:-1, 1:-1]
    return ice_cover * ((1.0 - OMEGA) * centre + OMEGA * line_value)


def lane_weights(comps, width):
    along_x = jnp.concatenate([jnp.full((width,), (4.0, 1.0)[c], jnp.float32) for c in range(comps)])
    along_y = jnp.concatenate([jnp.full((width,), (1.0, 4.0)[c], jnp.float32) for c in range(comps)])
    return (along_x, along_y)


def prepare_lanes(visc_pad, beta_col, ice_cover, weights):
    faces = lateral_terms(visc_pad)
    west_face, east_face, south_face, north_face = faces
    along_x, along_y = weights
    centre_visc = visc_pad[:, 1:-1, 1:-1]
    vertical = VERTICAL * 0.5 * (centre_visc[:-1] + centre_visc[1:])
    zero_row = jnp.zeros_like(centre_visc[:1])
    upper_link = jnp.concatenate([vertical, zero_row], 0)
    lower_link = jnp.concatenate([zero_row, vertical], 0)
    basal = jnp.concatenate([jnp.zeros_like(centre_visc[:-1]), beta_col[None]], 0)
    diagonal = along_x * (west_face + east_face) + along_y * (south_face + north_face)
    diagonal = diagonal + upper_link + lower_link + basal + (1.0 - ice_cover)
    layer_count = visc_pad.shape[0]
    ratio_list = []
    inverse_list = []
    for layer_idx in range(layer_count):
        pivot = diagonal[layer_idx]
        if layer_idx > 0:
            pivot = pivot + lower_link[layer_idx] * ratio_list[-1]
        inverse = 1.0 / pivot
        inverse_list.append(inverse)
        ratio_list.append(-upper_link[layer_idx] * inverse)
    return (faces, lower_link, ratio_list, inverse_list)


def relax_lanes(vel_pad, rhs_field, faces, lower_link, ratios, inverses, ice_cover, weights):
    west_face, east_face, south_face, north_face = faces
    along_x, along_y = weights
    lateral = along_x * (west_face * vel_pad[:, :-2, 1:-1] + east_face * vel_pad[:, 2:, 1:-1])
    lateral = lateral + along_y * (
        south_face * vel_pad[:, 1:-1, :-2] + north_face * vel_pad[:, 1:-1, 2:]
    )
    right_side = rhs_field + lateral
    layer_count = right_side.shape[0]
    forward_list = []
    for layer_idx in range(layer_count):
        value = right_side[layer_idx]
        if layer_idx > 0:
            value = value + lower_link[layer_idx] * forward_list[-1]
        forward_list.append(value * inverses[layer_idx])
    solved = [None] * layer_count
    solved[layer_count - 1] = forward_list[layer_count - 1]
    for layer_idx in range(layer_count - 2, -1, -1):
        solved[layer_idx] = forward_list[layer_idx] - ratios[layer_idx] * solved[layer_idx + 1]
    line_value = jnp.stack(solved, 0)
    centre = vel_pad[:, 1:-1, 1:-1]
    return ice_cover * ((1.0 - OMEGA) * centre + OMEGA * line_value)


def pad_cells(field):
    return jnp.pad(field, [(0, 0)] * (field.ndim - 2) + [(1, 1), (1, 1)])


def shifted(piece, axis, down):
    count = lax.axis_size(axis)
    if down:
        pairs = [(i, i + 1) for i in range(count - 1)]
    else:
        pairs = [(i + 1, i) for i in range(count - 1)]
    return lax.ppermute(piece, axis, pairs)


def local(forcing, viscosity, observed, beta_tiles, ice_mask, tile_owner):
    comps, layers, rows, cols = forcing.shape
    tiles_here = beta_tiles.shape[1]
    float_planes = [forcing.reshape(comps * layers, rows, cols), viscosity, observed]
    int_planes = [ice_mask[None], tile_owner[None]]

    def pieces(rows_at, cols_at):
        return [p[:, rows_at, cols_at] for p in float_planes] + [
            p[:, rows_at, cols_at].astype(jnp.float32) for p in int_planes
        ]

    plane_count = sum(p.shape[0] for p in float_planes + int_planes)
    every = slice(None)

    beta_plane = jnp.pad(beta_tiles, ((0, HALO - 1), (0, cols - tiles_here)))[None]
    head = jnp.concatenate(pieces(slice(0, HALO), every) + [beta_plane], axis=0)
    tail = jnp.concatenate(pieces(slice(rows - HALO, rows), every) + [beta_plane], axis=0)
    from_above = shifted(tail, "gx", True)
    from_below = shifted(head, "gx", False)

    def stack_rows(lo, hi):
        return jnp.concatenate(
            [from_above[:plane_count, :, lo:hi]]
            + [jnp.concatenate(pieces(every, slice(lo, hi)), axis=0)]
            + [from_below[:plane_count, :, lo:hi]],
            axis=1,
        )

    from_left = shifted(stack_rows(cols - HALO, cols), "gy", True)
    from_right = shifted(stack_rows(0, HALO), "gy", False)

    strips_near = jnp.stack(
        [from_above[plane_count, 0, :tiles_here], beta_tiles[0], from_below[plane_count, 0, :tiles_here]]
    )
    friction_rows = lax.all_gather(strips_near, "gy", axis=1, tiled=True)
    tile_count = friction_rows.shape[1]

    packed = jnp.concatenate([from_left, stack_rows(0, cols), from_right], axis=2)
    ext_rows, ext_cols = packed.shape[1], packed.shape[2]
    at = 0
    forcing_ext = packed[at:at + comps * layers].reshape(comps, layers, ext_rows, ext_cols)
    at += comps * layers
    visc_ext = packed[at:at + layers]
    at += layers
    observed_ext = packed[at:at + comps]
    at += comps
    ice_cover = packed[at]
    owner_ext = packed[at + 1].astype(jnp.int32)

    tiles = lax.broadcasted_iota(jnp.int32, (tile_count, 1, 1), 0)
    owner_match = owner_ext[None] == tiles
    row_strip = jnp.concatenate(
        [
            jnp.broadcast_to(friction_rows[0][:, None], (tile_count, HALO)),
            jnp.broadcast_to(friction_rows[1][:, None], (tile_count, rows)),
            jnp.broadcast_to(friction_rows[2][:, None], (tile_count, HALO)),
        ],
        axis=1,
    )
    beta_col = jnp.sum(jnp.where(owner_match, row_strip[:, :, None], 0.0), axis=0)

    def side_by_side(per_comp):
        return jnp.concatenate([per_comp[c] for c in range(comps)], axis=-1)

    weights = lane_weights(comps, ext_cols)
    visc_lanes = side_by_side([visc_ext] * comps)
    ice_lanes = side_by_side([ice_cover] * comps)
    beta_lanes = side_by_side([beta_col] * comps)
    forcing_lanes = side_by_side([forcing_ext[c] for c in range(comps)])
    observed_lanes = side_by_side([observed_ext[c] for c in range(comps)])
    faces, lower_link, ratios, inverses = prepare_lanes(
        pad_cells(visc_lanes), beta_lanes, ice_lanes, weights
    )

    def advance(field, rhs_field):
        return relax_lanes(pad_cells(field), rhs_field, faces, lower_link, ratios, inverses, ice_lanes, weights)

    velocity = jnp.zeros_like(forcing_lanes)
    for sweep_idx in range(PASSES):
        velocity = advance(velocity, forcing_lanes)
    misfit = velocity[0] - observed_lanes
    adjoint_rhs = jnp.zeros_like(forcing_lanes).at[0].set(misfit)
    adjoint = jnp.zeros_like(forcing_lanes)
    for sweep_idx in range(PASSES):
        adjoint = advance(adjoint, adjoint_rhs)

    inner = (slice(HALO, HALO + rows), slice(HALO, HALO + cols))

    def split(field):
        return jnp.stack(
            [field[:, inner[0], c * ext_cols + HALO:c * ext_cols + HALO + cols] for c in range(comps)]
        )

    velocity = split(velocity)
    adjoint = split(adjoint)
    grad_col = -ice_cover[inner] * beta_col[inner] * jnp.sum(adjoint[:, -1] * velocity[:, -1], axis=0)
    high = lax.reduce_precision(grad_col, exponent_bits=8, mantissa_bits=7)
    rest = grad_col - high
    middle = lax.reduce_precision(rest, exponent_bits=8, mantissa_bits=7)
    low = rest - middle
    parts = jnp.stack([high, middle, low], axis=-1).reshape(rows * cols, 3).astype(jnp.bfloat16)
    block_match = tile_owner.reshape(rows * cols, 1) == lax.broadcasted_iota(jnp.int32, (1, tile_count), 1)
    per_part = lax.dot_general(
        block_match.astype(jnp.bfloat16), parts, (((0,), (0,)), ((), ())),
        preferred_element_type=jnp.float32,
    )
    partial_sum = per_part[:, 0] + per_part[:, 1] + per_part[:, 2]
    owners = lax.axis_size("gy")
    chunk = tile_count // owners
    gathered = lax.all_gather(partial_sum.reshape(owners, chunk), "gy")
    mine = lax.dynamic_index_in_dim(gathered, lax.axis_index("gy"), axis=1, keepdims=False)
    grad_tiles = jnp.sum(mine, axis=0)[None]
    return (velocity, adjoint, grad_tiles)


def solution(mesh):
    in_specs = (
        P(None, None, "gx", "gy"),
        P(None, "gx", "gy"),
        P(None, "gx", "gy"),
        P("gx", "gy"),
        P("gx", "gy"),
        P("gx", "gy"),
    )
    out_specs = (P(None, None, "gx", "gy"), P(None, None, "gx", "gy"), P("gx", "gy"))
    return jax.shard_map(local, mesh=mesh, in_specs=in_specs, out_specs=out_specs, check_vma=False)
```

```python
import jax
import jax.numpy as jnp
from jax import lax
from jax.sharding import PartitionSpec as P

PASSES = 4


OMEGA = 0.8
VERTICAL = 16.0
HALO = 2 * PASSES - 1


def with_halo(cells, sides, width):
    for axis, dim in sides:
        count = lax.axis_size(axis)
        ends = count - 1
        head = lax.slice_in_dim(cells, 0, width, axis=dim)
        tail = lax.slice_in_dim(cells, cells.shape[dim] - width, cells.shape[dim], axis=dim)
        cells = jnp.concatenate(
            [
                lax.ppermute(tail, axis, [(i, (i + 1) % count) for i in range(ends)]),
                cells,
                lax.ppermute(head, axis, [((i + 1) % count, i) for i in range(ends)]),
            ],
            axis=dim,
        )
    return cells


def lateral_terms(visc_pad):
    centre_visc = visc_pad[:, 1:-1, 1:-1]
    west_face = 0.5 * (centre_visc + visc_pad[:, :-2, 1:-1])
    east_face = 0.5 * (centre_visc + visc_pad[:, 2:, 1:-1])
    south_face = 0.5 * (centre_visc + visc_pad[:, 1:-1, :-2])
    north_face = 0.5 * (centre_visc + visc_pad[:, 1:-1, 2:])
    return (west_face, east_face, south_face, north_face)


def weights_xy():
    along_x = jnp.array([4.0, 1.0], jnp.float32).reshape(2, 1, 1, 1)
    along_y = jnp.array([1.0, 4.0], jnp.float32).reshape(2, 1, 1, 1)
    return (along_x, along_y)


def prepare(visc_pad, beta_col, ice_cover):
    faces = lateral_terms(visc_pad)
    west_face, east_face, south_face, north_face = faces
    along_x, along_y = weights_xy()
    centre_visc = visc_pad[:, 1:-1, 1:-1]
    vertical = VERTICAL * 0.5 * (centre_visc[:-1] + centre_visc[1:])
    zero_row = jnp.zeros_like(centre_visc[:1])
    upper_link = jnp.concatenate([vertical, zero_row], 0)
    lower_link = jnp.concatenate([zero_row, vertical], 0)
    basal = jnp.concatenate([jnp.zeros_like(centre_visc[:-1]), beta_col[None]], 0)
    diagonal = along_x * (west_face + east_face) + along_y * (south_face + north_face)
    diagonal = diagonal + upper_link + lower_link + basal + (1.0 - ice_cover)
    layer_count = visc_pad.shape[0]
    ratio_list = []
    inverse_list = []
    for layer_idx in range(layer_count):
        pivot = diagonal[:, layer_idx]
        if layer_idx > 0:
            pivot = pivot + lower_link[layer_idx] * ratio_list[-1]
        inverse = 1.0 / pivot
        inverse_list.append(inverse)
        ratio_list.append(-upper_link[layer_idx] * inverse)
    return (faces, lower_link, jnp.stack(ratio_list, 1), jnp.stack(inverse_list, 1))


def relax(vel_pad, rhs_field, faces, lower_link, ratios, inverses, ice_cover):
    west_face, east_face, south_face, north_face = faces
    along_x, along_y = weights_xy()
    lateral = along_x * (west_face * vel_pad[:, :, :-2, 1:-1] + east_face * vel_pad[:, :, 2:, 1:-1])
    lateral = lateral + along_y * (
        south_face * vel_pad[:, :, 1:-1, :-2] + north_face * vel_pad[:, :, 1:-1, 2:]
    )
    right_side = rhs_field + lateral
    layer_count = right_side.shape[1]
    forward_list = []
    for layer_idx in range(layer_count):
        value = right_side[:, layer_idx]
        if layer_idx > 0:
            value = value + lower_link[layer_idx] * forward_list[-1]
        forward_list.append(value * inverses[:, layer_idx])
    solved = [None] * layer_count
    solved[layer_count - 1] = forward_list[layer_count - 1]
    for layer_idx in range(layer_count - 2, -1, -1):
        solved[layer_idx] = forward_list[layer_idx] - ratios[:, layer_idx] * solved[layer_idx + 1]
    line_value = jnp.stack(solved, 1)
    centre = vel_pad[:, :, 1:-1, 1:-1]
    return ice_cover * ((1.0 - OMEGA) * centre + OMEGA * line_value)


def lane_weights(comps, width):
    along_x = jnp.concatenate([jnp.full((width,), (4.0, 1.0)[c], jnp.float32) for c in range(comps)])
    along_y = jnp.concatenate([jnp.full((width,), (1.0, 4.0)[c], jnp.float32) for c in range(comps)])
    return (along_x, along_y)


def prepare_lanes(visc_pad, beta_col, ice_cover, weights):
    faces = lateral_terms(visc_pad)
    west_face, east_face, south_face, north_face = faces
    along_x, along_y = weights
    centre_visc = visc_pad[:, 1:-1, 1:-1]
    vertical = VERTICAL * 0.5 * (centre_visc[:-1] + centre_visc[1:])
    zero_row = jnp.zeros_like(centre_visc[:1])
    upper_link = jnp.concatenate([vertical, zero_row], 0)
    lower_link = jnp.concatenate([zero_row, vertical], 0)
    basal = jnp.concatenate([jnp.zeros_like(centre_visc[:-1]), beta_col[None]], 0)
    diagonal = along_x * (west_face + east_face) + along_y * (south_face + north_face)
    diagonal = diagonal + upper_link + lower_link + basal + (1.0 - ice_cover)
    layer_count = visc_pad.shape[0]
    ratio_list = []
    inverse_list = []
    for layer_idx in range(layer_count):
        pivot = diagonal[layer_idx]
        if layer_idx > 0:
            pivot = pivot + lower_link[layer_idx] * ratio_list[-1]
        inverse = 1.0 / pivot
        inverse_list.append(inverse)
        ratio_list.append(-upper_link[layer_idx] * inverse)
    return (faces, lower_link, ratio_list, inverse_list)


def relax_lanes(vel_pad, rhs_field, faces, lower_link, ratios, inverses, ice_cover, weights):
    west_face, east_face, south_face, north_face = faces
    along_x, along_y = weights
    lateral = along_x * (west_face * vel_pad[:, :-2, 1:-1] + east_face * vel_pad[:, 2:, 1:-1])
    lateral = lateral + along_y * (
        south_face * vel_pad[:, 1:-1, :-2] + north_face * vel_pad[:, 1:-1, 2:]
    )
    right_side = rhs_field + lateral
    layer_count = right_side.shape[0]
    forward_list = []
    for layer_idx in range(layer_count):
        value = right_side[layer_idx]
        if layer_idx > 0:
            value = value + lower_link[layer_idx] * forward_list[-1]
        forward_list.append(value * inverses[layer_idx])
    solved = [None] * layer_count
    solved[layer_count - 1] = forward_list[layer_count - 1]
    for layer_idx in range(layer_count - 2, -1, -1):
        solved[layer_idx] = forward_list[layer_idx] - ratios[layer_idx] * solved[layer_idx + 1]
    line_value = jnp.stack(solved, 0)
    centre = vel_pad[:, 1:-1, 1:-1]
    return ice_cover * ((1.0 - OMEGA) * centre + OMEGA * line_value)


def pad_cells(field):
    return jnp.pad(field, [(0, 0)] * (field.ndim - 2) + [(1, 1), (1, 1)])


def shifted(piece, axis, down):
    count = lax.axis_size(axis)
    if down:
        pairs = [(i, i + 1) for i in range(count - 1)]
    else:
        pairs = [(i + 1, i) for i in range(count - 1)]
    return lax.ppermute(piece, axis, pairs)


def stack_planes(parts):
    total = sum(p.shape[0] for p in parts)
    index = lax.broadcasted_iota(jnp.int32, (total,) + parts[0].shape[1:], 0)
    stacked = None
    start = 0
    for part in parts:
        count = part.shape[0]
        placed = jnp.pad(part, [(start, total - start - count)] + [(0, 0)] * (part.ndim - 1))
        if stacked is None:
            stacked = placed
        else:
            stacked = jnp.where(index >= start, placed, stacked)
        start += count
    return stacked


def local(forcing, viscosity, observed, beta_tiles, ice_mask, tile_owner):
    comps, layers, rows, cols = forcing.shape
    tiles_here = beta_tiles.shape[1]
    float_planes = [forcing.reshape(comps * layers, rows, cols), viscosity, observed]
    int_planes = [ice_mask[None], tile_owner[None]]

    def pieces(rows_at, cols_at):
        return [p[:, rows_at, cols_at] for p in float_planes] + [
            p[:, rows_at, cols_at].astype(jnp.float32) for p in int_planes
        ]

    plane_count = sum(p.shape[0] for p in float_planes + int_planes)
    every = slice(None)

    beta_plane = jnp.pad(beta_tiles, ((0, HALO - 1), (0, cols - tiles_here)))[None]
    head = stack_planes(pieces(slice(0, HALO), every) + [beta_plane])
    tail = stack_planes(pieces(slice(rows - HALO, rows), every) + [beta_plane])
    from_above = shifted(tail, "gx", True)
    from_below = shifted(head, "gx", False)

    def stack_rows(lo, hi):
        return jnp.concatenate(
            [from_above[:plane_count, :, lo:hi]]
            + [jnp.concatenate(pieces(every, slice(lo, hi)), axis=0)]
            + [from_below[:plane_count, :, lo:hi]],
            axis=1,
        )

    from_left = shifted(stack_rows(cols - HALO, cols), "gy", True)
    from_right = shifted(stack_rows(0, HALO), "gy", False)

    strips_near = jnp.stack(
        [from_above[plane_count, 0, :tiles_here], beta_tiles[0], from_below[plane_count, 0, :tiles_here]]
    )
    friction_rows = lax.all_gather(strips_near, "gy", axis=1, tiled=True)
    tile_count = friction_rows.shape[1]

    packed = jnp.concatenate([from_left, stack_rows(0, cols), from_right], axis=2)
    ext_rows, ext_cols = packed.shape[1], packed.shape[2]
    at = 0
    forcing_ext = packed[at:at + comps * layers].reshape(comps, layers, ext_rows, ext_cols)
    at += comps * layers
    visc_ext = packed[at:at + layers]
    at += layers
    observed_ext = packed[at:at + comps]
    at += comps
    ice_cover = packed[at]
    owner_ext = packed[at + 1].astype(jnp.int32)

    tiles = lax.broadcasted_iota(jnp.int32, (tile_count, 1, 1), 0)
    owner_match = owner_ext[None] == tiles
    row_strip = jnp.concatenate(
        [
            jnp.broadcast_to(friction_rows[0][:, None], (tile_count, HALO)),
            jnp.broadcast_to(friction_rows[1][:, None], (tile_count, rows)),
            jnp.broadcast_to(friction_rows[2][:, None], (tile_count, HALO)),
        ],
        axis=1,
    )
    beta_col = jnp.sum(jnp.where(owner_match, row_strip[:, :, None], 0.0), axis=0)

    def side_by_side(per_comp):
        return jnp.concatenate([per_comp[c] for c in range(comps)], axis=-1)

    weights = lane_weights(comps, ext_cols)
    visc_lanes = side_by_side([visc_ext] * comps)
    ice_lanes = side_by_side([ice_cover] * comps)
    beta_lanes = side_by_side([beta_col] * comps)
    forcing_lanes = side_by_side([forcing_ext[c] for c in range(comps)])
    observed_lanes = side_by_side([observed_ext[c] for c in range(comps)])
    faces, lower_link, ratios, inverses = prepare_lanes(
        pad_cells(visc_lanes), beta_lanes, ice_lanes, weights
    )

    def advance(field, rhs_field):
        return relax_lanes(pad_cells(field), rhs_field, faces, lower_link, ratios, inverses, ice_lanes, weights)

    velocity = jnp.zeros_like(forcing_lanes)
    for sweep_idx in range(PASSES):
        velocity = advance(velocity, forcing_lanes)
    misfit = velocity[0] - observed_lanes
    adjoint_rhs = jnp.zeros_like(forcing_lanes).at[0].set(misfit)
    adjoint = jnp.zeros_like(forcing_lanes)
    for sweep_idx in range(PASSES):
        adjoint = advance(adjoint, adjoint_rhs)

    inner = (slice(HALO, HALO + rows), slice(HALO, HALO + cols))

    def split(field):
        return jnp.stack(
            [field[:, inner[0], c * ext_cols + HALO:c * ext_cols + HALO + cols] for c in range(comps)]
        )

    velocity = split(velocity)
    adjoint = split(adjoint)
    grad_col = -ice_cover[inner] * beta_col[inner] * jnp.sum(adjoint[:, -1] * velocity[:, -1], axis=0)
    high = lax.reduce_precision(grad_col, exponent_bits=8, mantissa_bits=7)
    rest = grad_col - high
    middle = lax.reduce_precision(rest, exponent_bits=8, mantissa_bits=7)
    low = rest - middle
    parts = jnp.stack([high, middle, low], axis=-1).reshape(rows * cols, 3).astype(jnp.bfloat16)
    block_match = tile_owner.reshape(rows * cols, 1) == lax.broadcasted_iota(jnp.int32, (1, tile_count), 1)
    per_part = lax.dot_general(
        block_match.astype(jnp.bfloat16), parts, (((0,), (0,)), ((), ())),
        preferred_element_type=jnp.float32,
    )
    partial_sum = per_part[:, 0] + per_part[:, 1] + per_part[:, 2]
    owners = lax.axis_size("gy")
    chunk = tile_count // owners
    gathered = lax.all_gather(partial_sum.reshape(owners, chunk), "gy")
    mine = lax.dynamic_index_in_dim(gathered, lax.axis_index("gy"), axis=1, keepdims=False)
    grad_tiles = jnp.sum(mine, axis=0)[None]
    return (velocity, adjoint, grad_tiles)


def solution(mesh):
    in_specs = (
        P(None, None, "gx", "gy"),
        P(None, "gx", "gy"),
        P(None, "gx", "gy"),
        P("gx", "gy"),
        P("gx", "gy"),
        P("gx", "gy"),
    )
    out_specs = (P(None, None, "gx", "gy"), P(None, None, "gx", "gy"), P("gx", "gy"))
    return jax.shard_map(local, mesh=mesh, in_specs=in_specs, out_specs=out_specs, check_vma=False)
```

```python
import jax
import jax.numpy as jnp
from jax import lax
from jax.sharding import PartitionSpec as P

PASSES = 4


OMEGA = 0.8
VERTICAL = 16.0
HALO = 2 * PASSES - 1


def with_halo(cells, sides, width):
    for axis, dim in sides:
        count = lax.axis_size(axis)
        ends = count - 1
        head = lax.slice_in_dim(cells, 0, width, axis=dim)
        tail = lax.slice_in_dim(cells, cells.shape[dim] - width, cells.shape[dim], axis=dim)
        cells = jnp.concatenate(
            [
                lax.ppermute(tail, axis, [(i, (i + 1) % count) for i in range(ends)]),
                cells,
                lax.ppermute(head, axis, [((i + 1) % count, i) for i in range(ends)]),
            ],
            axis=dim,
        )
    return cells


def lateral_terms(visc_pad):
    centre_visc = visc_pad[:, 1:-1, 1:-1]
    west_face = 0.5 * (centre_visc + visc_pad[:, :-2, 1:-1])
    east_face = 0.5 * (centre_visc + visc_pad[:, 2:, 1:-1])
    south_face = 0.5 * (centre_visc + visc_pad[:, 1:-1, :-2])
    north_face = 0.5 * (centre_visc + visc_pad[:, 1:-1, 2:])
    return (west_face, east_face, south_face, north_face)


def weights_xy():
    along_x = jnp.array([4.0, 1.0], jnp.float32).reshape(2, 1, 1, 1)
    along_y = jnp.array([1.0, 4.0], jnp.float32).reshape(2, 1, 1, 1)
    return (along_x, along_y)


def prepare(visc_pad, beta_col, ice_cover):
    faces = lateral_terms(visc_pad)
    west_face, east_face, south_face, north_face = faces
    along_x, along_y = weights_xy()
    centre_visc = visc_pad[:, 1:-1, 1:-1]
    vertical = VERTICAL * 0.5 * (centre_visc[:-1] + centre_visc[1:])
    zero_row = jnp.zeros_like(centre_visc[:1])
    upper_link = jnp.concatenate([vertical, zero_row], 0)
    lower_link = jnp.concatenate([zero_row, vertical], 0)
    basal = jnp.concatenate([jnp.zeros_like(centre_visc[:-1]), beta_col[None]], 0)
    diagonal = along_x * (west_face + east_face) + along_y * (south_face + north_face)
    diagonal = diagonal + upper_link + lower_link + basal + (1.0 - ice_cover)
    layer_count = visc_pad.shape[0]
    ratio_list = []
    inverse_list = []
    for layer_idx in range(layer_count):
        pivot = diagonal[:, layer_idx]
        if layer_idx > 0:
            pivot = pivot + lower_link[layer_idx] * ratio_list[-1]
        inverse = 1.0 / pivot
        inverse_list.append(inverse)
        ratio_list.append(-upper_link[layer_idx] * inverse)
    return (faces, lower_link, jnp.stack(ratio_list, 1), jnp.stack(inverse_list, 1))


def relax(vel_pad, rhs_field, faces, lower_link, ratios, inverses, ice_cover):
    west_face, east_face, south_face, north_face = faces
    along_x, along_y = weights_xy()
    lateral = along_x * (west_face * vel_pad[:, :, :-2, 1:-1] + east_face * vel_pad[:, :, 2:, 1:-1])
    lateral = lateral + along_y * (
        south_face * vel_pad[:, :, 1:-1, :-2] + north_face * vel_pad[:, :, 1:-1, 2:]
    )
    right_side = rhs_field + lateral
    layer_count = right_side.shape[1]
    forward_list = []
    for layer_idx in range(layer_count):
        value = right_side[:, layer_idx]
        if layer_idx > 0:
            value = value + lower_link[layer_idx] * forward_list[-1]
        forward_list.append(value * inverses[:, layer_idx])
    solved = [None] * layer_count
    solved[layer_count - 1] = forward_list[layer_count - 1]
    for layer_idx in range(layer_count - 2, -1, -1):
        solved[layer_idx] = forward_list[layer_idx] - ratios[:, layer_idx] * solved[layer_idx + 1]
    line_value = jnp.stack(solved, 1)
    centre = vel_pad[:, :, 1:-1, 1:-1]
    return ice_cover * ((1.0 - OMEGA) * centre + OMEGA * line_value)


def lane_weights(comps, width):
    along_x = jnp.concatenate([jnp.full((width,), (4.0, 1.0)[c], jnp.float32) for c in range(comps)])
    along_y = jnp.concatenate([jnp.full((width,), (1.0, 4.0)[c], jnp.float32) for c in range(comps)])
    return (along_x, along_y)


def prepare_lanes(visc_pad, beta_col, ice_cover, weights):
    faces = lateral_terms(visc_pad)
    west_face, east_face, south_face, north_face = faces
    along_x, along_y = weights
    centre_visc = visc_pad[:, 1:-1, 1:-1]
    vertical = VERTICAL * 0.5 * (centre_visc[:-1] + centre_visc[1:])
    zero_row = jnp.zeros_like(centre_visc[:1])
    upper_link = jnp.concatenate([vertical, zero_row], 0)
    lower_link = jnp.concatenate([zero_row, vertical], 0)
    basal = jnp.concatenate([jnp.zeros_like(centre_visc[:-1]), beta_col[None]], 0)
    diagonal = along_x * (west_face + east_face) + along_y * (south_face + north_face)
    diagonal = diagonal + upper_link + lower_link + basal + (1.0 - ice_cover)
    layer_count = visc_pad.shape[0]
    ratio_list = []
    inverse_list = []
    for layer_idx in range(layer_count):
        pivot = diagonal[layer_idx]
        if layer_idx > 0:
            pivot = pivot + lower_link[layer_idx] * ratio_list[-1]
        inverse = 1.0 / pivot
        inverse_list.append(inverse)
        ratio_list.append(-upper_link[layer_idx] * inverse)
    return (faces, lower_link, ratio_list, inverse_list)


def relax_lanes(vel_pad, rhs_field, faces, lower_link, ratios, inverses, ice_cover, weights):
    west_face, east_face, south_face, north_face = faces
    along_x, along_y = weights
    lateral = along_x * (west_face * vel_pad[:, :-2, 1:-1] + east_face * vel_pad[:, 2:, 1:-1])
    lateral = lateral + along_y * (
        south_face * vel_pad[:, 1:-1, :-2] + north_face * vel_pad[:, 1:-1, 2:]
    )
    right_side = rhs_field + lateral
    layer_count = right_side.shape[0]
    forward_list = []
    for layer_idx in range(layer_count):
        value = right_side[layer_idx]
        if layer_idx > 0:
            value = value + lower_link[layer_idx] * forward_list[-1]
        forward_list.append(value * inverses[layer_idx])
    solved = [None] * layer_count
    solved[layer_count - 1] = forward_list[layer_count - 1]
    for layer_idx in range(layer_count - 2, -1, -1):
        solved[layer_idx] = forward_list[layer_idx] - ratios[layer_idx] * solved[layer_idx + 1]
    line_value = jnp.stack(solved, 0)
    centre = vel_pad[:, 1:-1, 1:-1]
    return ice_cover * ((1.0 - OMEGA) * centre + OMEGA * line_value)


def pad_cells(field):
    return jnp.pad(field, [(0, 0)] * (field.ndim - 2) + [(1, 1), (1, 1)])


def shifted(piece, axis, down):
    count = lax.axis_size(axis)
    if down:
        pairs = [(i, i + 1) for i in range(count - 1)]
    else:
        pairs = [(i + 1, i) for i in range(count - 1)]
    return lax.ppermute(piece, axis, pairs)


def local(forcing, viscosity, observed, beta_tiles, ice_mask, tile_owner):
    comps, layers, rows, cols = forcing.shape
    tiles_here = beta_tiles.shape[1]
    float_planes = [forcing.reshape(comps * layers, rows, cols), viscosity, observed]
    int_planes = [ice_mask[None], tile_owner[None]]

    def pieces(rows_at, cols_at):
        return [p[:, rows_at, cols_at] for p in float_planes] + [
            p[:, rows_at, cols_at].astype(jnp.float32) for p in int_planes
        ]

    plane_count = sum(p.shape[0] for p in float_planes + int_planes)
    every = slice(None)

    from_left = shifted(jnp.concatenate(pieces(every, slice(cols - HALO, cols)), axis=0), "gy", True)
    from_right = shifted(jnp.concatenate(pieces(every, slice(0, HALO)), axis=0), "gy", False)
    widened = jnp.concatenate(
        [from_left, jnp.concatenate(pieces(every, every), axis=0), from_right], axis=2
    )
    wide_cols = widened.shape[2]
    beta_plane = jnp.pad(beta_tiles, ((0, HALO - 1), (0, wide_cols - tiles_here)))[None]
    head = jnp.concatenate([widened[:, :HALO], beta_plane], axis=0)
    tail = jnp.concatenate([widened[:, rows - HALO:], beta_plane], axis=0)
    from_above = shifted(tail, "gx", True)
    from_below = shifted(head, "gx", False)

    strips_near = jnp.stack(
        [from_above[plane_count, 0, :tiles_here], beta_tiles[0], from_below[plane_count, 0, :tiles_here]]
    )
    friction_rows = lax.all_gather(strips_near, "gy", axis=1, tiled=True)
    tile_count = friction_rows.shape[1]

    packed = jnp.concatenate([from_above[:plane_count], widened, from_below[:plane_count]], axis=1)
    ext_rows, ext_cols = packed.shape[1], packed.shape[2]
    at = 0
    forcing_ext = packed[at:at + comps * layers].reshape(comps, layers, ext_rows, ext_cols)
    at += comps * layers
    visc_ext = packed[at:at + layers]
    at += layers
    observed_ext = packed[at:at + comps]
    at += comps
    ice_cover = packed[at]
    owner_ext = packed[at + 1].astype(jnp.int32)

    tiles = lax.broadcasted_iota(jnp.int32, (tile_count, 1, 1), 0)
    owner_match = owner_ext[None] == tiles
    row_strip = jnp.concatenate(
        [
            jnp.broadcast_to(friction_rows[0][:, None], (tile_count, HALO)),
            jnp.broadcast_to(friction_rows[1][:, None], (tile_count, rows)),
            jnp.broadcast_to(friction_rows[2][:, None], (tile_count, HALO)),
        ],
        axis=1,
    )
    beta_col = jnp.sum(jnp.where(owner_match, row_strip[:, :, None], 0.0), axis=0)

    def side_by_side(per_comp):
        return jnp.concatenate([per_comp[c] for c in range(comps)], axis=-1)

    weights = lane_weights(comps, ext_cols)
    visc_lanes = side_by_side([visc_ext] * comps)
    ice_lanes = side_by_side([ice_cover] * comps)
    beta_lanes = side_by_side([beta_col] * comps)
    forcing_lanes = side_by_side([forcing_ext[c] for c in range(comps)])
    observed_lanes = side_by_side([observed_ext[c] for c in range(comps)])
    faces, lower_link, ratios, inverses = prepare_lanes(
        pad_cells(visc_lanes), beta_lanes, ice_lanes, weights
    )

    def advance(field, rhs_field):
        return relax_lanes(pad_cells(field), rhs_field, faces, lower_link, ratios, inverses, ice_lanes, weights)

    velocity = jnp.zeros_like(forcing_lanes)
    for sweep_idx in range(PASSES):
        velocity = advance(velocity, forcing_lanes)
    misfit = velocity[0] - observed_lanes
    adjoint_rhs = jnp.zeros_like(forcing_lanes).at[0].set(misfit)
    adjoint = jnp.zeros_like(forcing_lanes)
    for sweep_idx in range(PASSES):
        adjoint = advance(adjoint, adjoint_rhs)

    inner = (slice(HALO, HALO + rows), slice(HALO, HALO + cols))

    def split(field):
        return jnp.stack(
            [field[:, inner[0], c * ext_cols + HALO:c * ext_cols + HALO + cols] for c in range(comps)]
        )

    velocity = split(velocity)
    adjoint = split(adjoint)
    grad_col = -ice_cover[inner] * beta_col[inner] * jnp.sum(adjoint[:, -1] * velocity[:, -1], axis=0)
    high = lax.reduce_precision(grad_col, exponent_bits=8, mantissa_bits=7)
    rest = grad_col - high
    middle = lax.reduce_precision(rest, exponent_bits=8, mantissa_bits=7)
    low = rest - middle
    parts = jnp.stack([high, middle, low], axis=-1).reshape(rows * cols, 3).astype(jnp.bfloat16)
    block_match = tile_owner.reshape(rows * cols, 1) == lax.broadcasted_iota(jnp.int32, (1, tile_count), 1)
    per_part = lax.dot_general(
        block_match.astype(jnp.bfloat16), parts, (((0,), (0,)), ((), ())),
        preferred_element_type=jnp.float32,
    )
    partial_sum = per_part[:, 0] + per_part[:, 1] + per_part[:, 2]
    owners = lax.axis_size("gy")
    chunk = tile_count // owners
    gathered = lax.all_gather(partial_sum.reshape(owners, chunk), "gy")
    mine = lax.dynamic_index_in_dim(gathered, lax.axis_index("gy"), axis=1, keepdims=False)
    grad_tiles = jnp.sum(mine, axis=0)[None]
    return (velocity, adjoint, grad_tiles)


def solution(mesh):
    in_specs = (
        P(None, None, "gx", "gy"),
        P(None, "gx", "gy"),
        P(None, "gx", "gy"),
        P("gx", "gy"),
        P("gx", "gy"),
        P("gx", "gy"),
    )
    out_specs = (P(None, None, "gx", "gy"), P(None, None, "gx", "gy"), P("gx", "gy"))
    return jax.shard_map(local, mesh=mesh, in_specs=in_specs, out_specs=out_specs, check_vma=False)
```

```python
import jax
import jax.numpy as jnp
from jax import lax
from jax.sharding import PartitionSpec as P

PASSES = 4


OMEGA = 0.8
VERTICAL = 16.0
HALO = 2 * PASSES - 1


def with_halo(cells, sides, width):
    for axis, dim in sides:
        count = lax.axis_size(axis)
        ends = count - 1
        head = lax.slice_in_dim(cells, 0, width, axis=dim)
        tail = lax.slice_in_dim(cells, cells.shape[dim] - width, cells.shape[dim], axis=dim)
        cells = jnp.concatenate(
            [
                lax.ppermute(tail, axis, [(i, (i + 1) % count) for i in range(ends)]),
                cells,
                lax.ppermute(head, axis, [((i + 1) % count, i) for i in range(ends)]),
            ],
            axis=dim,
        )
    return cells


def lateral_terms(visc_pad):
    centre_visc = visc_pad[:, 1:-1, 1:-1]
    west_face = 0.5 * (centre_visc + visc_pad[:, :-2, 1:-1])
    east_face = 0.5 * (centre_visc + visc_pad[:, 2:, 1:-1])
    south_face = 0.5 * (centre_visc + visc_pad[:, 1:-1, :-2])
    north_face = 0.5 * (centre_visc + visc_pad[:, 1:-1, 2:])
    return (west_face, east_face, south_face, north_face)


def weights_xy():
    along_x = jnp.array([4.0, 1.0], jnp.float32).reshape(2, 1, 1, 1)
    along_y = jnp.array([1.0, 4.0], jnp.float32).reshape(2, 1, 1, 1)
    return (along_x, along_y)


def prepare(visc_pad, beta_col, ice_cover):
    faces = lateral_terms(visc_pad)
    west_face, east_face, south_face, north_face = faces
    along_x, along_y = weights_xy()
    centre_visc = visc_pad[:, 1:-1, 1:-1]
    vertical = VERTICAL * 0.5 * (centre_visc[:-1] + centre_visc[1:])
    zero_row = jnp.zeros_like(centre_visc[:1])
    upper_link = jnp.concatenate([vertical, zero_row], 0)
    lower_link = jnp.concatenate([zero_row, vertical], 0)
    basal = jnp.concatenate([jnp.zeros_like(centre_visc[:-1]), beta_col[None]], 0)
    diagonal = along_x * (west_face + east_face) + along_y * (south_face + north_face)
    diagonal = diagonal + upper_link + lower_link + basal + (1.0 - ice_cover)
    layer_count = visc_pad.shape[0]
    ratio_list = []
    inverse_list = []
    for layer_idx in range(layer_count):
        pivot = diagonal[:, layer_idx]
        if layer_idx > 0:
            pivot = pivot + lower_link[layer_idx] * ratio_list[-1]
        inverse = 1.0 / pivot
        inverse_list.append(inverse)
        ratio_list.append(-upper_link[layer_idx] * inverse)
    return (faces, lower_link, jnp.stack(ratio_list, 1), jnp.stack(inverse_list, 1))


def relax(vel_pad, rhs_field, faces, lower_link, ratios, inverses, ice_cover):
    west_face, east_face, south_face, north_face = faces
    along_x, along_y = weights_xy()
    lateral = along_x * (west_face * vel_pad[:, :, :-2, 1:-1] + east_face * vel_pad[:, :, 2:, 1:-1])
    lateral = lateral + along_y * (
        south_face * vel_pad[:, :, 1:-1, :-2] + north_face * vel_pad[:, :, 1:-1, 2:]
    )
    right_side = rhs_field + lateral
    layer_count = right_side.shape[1]
    forward_list = []
    for layer_idx in range(layer_count):
        value = right_side[:, layer_idx]
        if layer_idx > 0:
            value = value + lower_link[layer_idx] * forward_list[-1]
        forward_list.append(value * inverses[:, layer_idx])
    solved = [None] * layer_count
    solved[layer_count - 1] = forward_list[layer_count - 1]
    for layer_idx in range(layer_count - 2, -1, -1):
        solved[layer_idx] = forward_list[layer_idx] - ratios[:, layer_idx] * solved[layer_idx + 1]
    line_value = jnp.stack(solved, 1)
    centre = vel_pad[:, :, 1:-1, 1:-1]
    return ice_cover * ((1.0 - OMEGA) * centre + OMEGA * line_value)


def lane_weights(comps, width):
    along_x = jnp.concatenate([jnp.full((width,), (4.0, 1.0)[c], jnp.float32) for c in range(comps)])
    along_y = jnp.concatenate([jnp.full((width,), (1.0, 4.0)[c], jnp.float32) for c in range(comps)])
    return (along_x, along_y)


def prepare_lanes(visc_pad, beta_col, ice_cover, weights):
    faces = lateral_terms(visc_pad)
    west_face, east_face, south_face, north_face = faces
    along_x, along_y = weights
    centre_visc = visc_pad[:, 1:-1, 1:-1]
    vertical = VERTICAL * 0.5 * (centre_visc[:-1] + centre_visc[1:])
    zero_row = jnp.zeros_like(centre_visc[:1])
    upper_link = jnp.concatenate([vertical, zero_row], 0)
    lower_link = jnp.concatenate([zero_row, vertical], 0)
    basal = jnp.concatenate([jnp.zeros_like(centre_visc[:-1]), beta_col[None]], 0)
    diagonal = along_x * (west_face + east_face) + along_y * (south_face + north_face)
    diagonal = diagonal + upper_link + lower_link + basal + (1.0 - ice_cover)
    layer_count = visc_pad.shape[0]
    ratio_list = []
    inverse_list = []
    for layer_idx in range(layer_count):
        pivot = diagonal[layer_idx]
        if layer_idx > 0:
            pivot = pivot + lower_link[layer_idx] * ratio_list[-1]
        inverse = 1.0 / pivot
        inverse_list.append(inverse)
        ratio_list.append(-upper_link[layer_idx] * inverse)
    return (faces, lower_link, ratio_list, inverse_list)


def relax_lanes(vel_pad, rhs_field, faces, lower_link, ratios, inverses, ice_cover, weights):
    west_face, east_face, south_face, north_face = faces
    along_x, along_y = weights
    lateral = along_x * (west_face * vel_pad[:, :-2, 1:-1] + east_face * vel_pad[:, 2:, 1:-1])
    lateral = lateral + along_y * (
        south_face * vel_pad[:, 1:-1, :-2] + north_face * vel_pad[:, 1:-1, 2:]
    )
    right_side = rhs_field + lateral
    layer_count = right_side.shape[0]
    forward_list = []
    for layer_idx in range(layer_count):
        value = right_side[layer_idx]
        if layer_idx > 0:
            value = value + lower_link[layer_idx] * forward_list[-1]
        forward_list.append(value * inverses[layer_idx])
    solved = [None] * layer_count
    solved[layer_count - 1] = forward_list[layer_count - 1]
    for layer_idx in range(layer_count - 2, -1, -1):
        solved[layer_idx] = forward_list[layer_idx] - ratios[layer_idx] * solved[layer_idx + 1]
    line_value = jnp.stack(solved, 0)
    centre = vel_pad[:, 1:-1, 1:-1]
    return ice_cover * ((1.0 - OMEGA) * centre + OMEGA * line_value)


def pad_cells(field):
    return jnp.pad(field, [(0, 0)] * (field.ndim - 2) + [(1, 1), (1, 1)])


def shifted(piece, axis, down):
    count = lax.axis_size(axis)
    if down:
        pairs = [(i, i + 1) for i in range(count - 1)]
    else:
        pairs = [(i + 1, i) for i in range(count - 1)]
    return lax.ppermute(piece, axis, pairs)


def local(forcing, viscosity, observed, beta_tiles, ice_mask, tile_owner):
    comps, layers, rows, cols = forcing.shape
    tiles_here = beta_tiles.shape[1]
    float_planes = [forcing.reshape(comps * layers, rows, cols), viscosity, observed]
    int_planes = [ice_mask[None], tile_owner[None]]

    def pieces(rows_at, cols_at):
        return [p[:, rows_at, cols_at] for p in float_planes] + [
            p[:, rows_at, cols_at].astype(jnp.float32) for p in int_planes
        ]

    plane_count = sum(p.shape[0] for p in float_planes + int_planes)
    every = slice(None)

    beta_plane = jnp.pad(beta_tiles, ((0, HALO - 1), (0, cols - tiles_here)))[None]
    head = jnp.concatenate(pieces(slice(0, HALO), every) + [beta_plane], axis=0)
    tail = jnp.concatenate(pieces(slice(rows - HALO, rows), every) + [beta_plane], axis=0)
    from_above = shifted(tail, "gx", True)
    from_below = shifted(head, "gx", False)

    def stack_rows(lo, hi):
        return jnp.concatenate(
            [from_above[:plane_count, :, lo:hi]]
            + [jnp.concatenate(pieces(every, slice(lo, hi)), axis=0)]
            + [from_below[:plane_count, :, lo:hi]],
            axis=1,
        )

    from_left = shifted(stack_rows(cols - HALO, cols), "gy", True)
    from_right = shifted(stack_rows(0, HALO), "gy", False)

    strips_near = jnp.stack(
        [from_above[plane_count, 0, :tiles_here], beta_tiles[0], from_below[plane_count, 0, :tiles_here]]
    )
    friction_rows = lax.all_gather(strips_near, "gy").transpose(1, 0, 2).reshape(strips_near.shape[0], -1)
    tile_count = friction_rows.shape[1]

    packed = jnp.concatenate([from_left, stack_rows(0, cols), from_right], axis=2)
    ext_rows, ext_cols = packed.shape[1], packed.shape[2]
    at = 0
    forcing_ext = packed[at:at + comps * layers].reshape(comps, layers, ext_rows, ext_cols)
    at += comps * layers
    visc_ext = packed[at:at + layers]
    at += layers
    observed_ext = packed[at:at + comps]
    at += comps
    ice_cover = packed[at]
    owner_ext = packed[at + 1].astype(jnp.int32)

    tiles = lax.broadcasted_iota(jnp.int32, (tile_count, 1, 1), 0)
    owner_match = owner_ext[None] == tiles
    row_strip = jnp.concatenate(
        [
            jnp.broadcast_to(friction_rows[0][:, None], (tile_count, HALO)),
            jnp.broadcast_to(friction_rows[1][:, None], (tile_count, rows)),
            jnp.broadcast_to(friction_rows[2][:, None], (tile_count, HALO)),
        ],
        axis=1,
    )
    beta_col = jnp.sum(jnp.where(owner_match, row_strip[:, :, None], 0.0), axis=0)

    def side_by_side(per_comp):
        return jnp.concatenate([per_comp[c] for c in range(comps)], axis=-1)

    weights = lane_weights(comps, ext_cols)
    visc_lanes = side_by_side([visc_ext] * comps)
    ice_lanes = side_by_side([ice_cover] * comps)
    beta_lanes = side_by_side([beta_col] * comps)
    forcing_lanes = side_by_side([forcing_ext[c] for c in range(comps)])
    observed_lanes = side_by_side([observed_ext[c] for c in range(comps)])
    faces, lower_link, ratios, inverses = prepare_lanes(
        pad_cells(visc_lanes), beta_lanes, ice_lanes, weights
    )

    def advance(field, rhs_field):
        return relax_lanes(pad_cells(field), rhs_field, faces, lower_link, ratios, inverses, ice_lanes, weights)

    velocity = jnp.zeros_like(forcing_lanes)
    for sweep_idx in range(PASSES):
        velocity = advance(velocity, forcing_lanes)
    misfit = velocity[0] - observed_lanes
    adjoint_rhs = jnp.zeros_like(forcing_lanes).at[0].set(misfit)
    adjoint = jnp.zeros_like(forcing_lanes)
    for sweep_idx in range(PASSES):
        adjoint = advance(adjoint, adjoint_rhs)

    inner = (slice(HALO, HALO + rows), slice(HALO, HALO + cols))

    def split(field):
        return jnp.stack(
            [field[:, inner[0], c * ext_cols + HALO:c * ext_cols + HALO + cols] for c in range(comps)]
        )

    velocity = split(velocity)
    adjoint = split(adjoint)
    grad_col = -ice_cover[inner] * beta_col[inner] * jnp.sum(adjoint[:, -1] * velocity[:, -1], axis=0)
    high = lax.reduce_precision(grad_col, exponent_bits=8, mantissa_bits=7)
    rest = grad_col - high
    middle = lax.reduce_precision(rest, exponent_bits=8, mantissa_bits=7)
    low = rest - middle
    parts = jnp.stack([high, middle, low], axis=-1).reshape(rows * cols, 3).astype(jnp.bfloat16)
    block_match = tile_owner.reshape(rows * cols, 1) == lax.broadcasted_iota(jnp.int32, (1, tile_count), 1)
    per_part = lax.dot_general(
        block_match.astype(jnp.bfloat16), parts, (((0,), (0,)), ((), ())),
        preferred_element_type=jnp.float32,
    )
    partial_sum = per_part[:, 0] + per_part[:, 1] + per_part[:, 2]
    owners = lax.axis_size("gy")
    chunk = tile_count // owners
    gathered = lax.all_gather(partial_sum.reshape(owners, chunk), "gy")
    mine = lax.dynamic_index_in_dim(gathered, lax.axis_index("gy"), axis=1, keepdims=False)
    grad_tiles = jnp.sum(mine, axis=0)[None]
    return (velocity, adjoint, grad_tiles)


def solution(mesh):
    in_specs = (
        P(None, None, "gx", "gy"),
        P(None, "gx", "gy"),
        P(None, "gx", "gy"),
        P("gx", "gy"),
        P("gx", "gy"),
        P("gx", "gy"),
    )
    out_specs = (P(None, None, "gx", "gy"), P(None, None, "gx", "gy"), P("gx", "gy"))
    return jax.shard_map(local, mesh=mesh, in_specs=in_specs, out_specs=out_specs, check_vma=False)
```
